256 devices in a mesh: ctx: 8 (over x, z_lo), tp: 32 (over z_hi, y, core).
Axes of the slice: x: 4, y: 4, z: 8 (z_hi: 4, z_lo: 2; z = z_hi * 2 + z_lo), core: 2. Of those that a mesh axis runs over, the one named last changes fastest.
Arguments:
- states: bfloat16 [8192, 2048], P(('ctx', 'tp')), may hold values from -6 to 6
- short_lengths: int32 [64], P('ctx'), may hold values from 1 to 64, 3072 in all
- attn_gain: float32 [2048], replicated, may hold values from 0.5 to 16
- wq: bfloat16 [2048, 2048], P(None, 'tp'), may hold values from -0.125 to 0.125
- wkv: bfloat16 [2048, 512], replicated, may hold values from -0.125 to 0.125
- wo: bfloat16 [2048, 2048], P('tp'), may hold values from -0.125 to 0.125
- mlp_gain: float32 [2048], replicated, may hold values from 0.5 to 1.5
- w_gate: bfloat16 [2048, 5632], P(None, 'tp'), may hold values from -0.125 to 0.125
- w_up: bfloat16 [2048, 5632], P(None, 'tp'), may hold values from -0.125 to 0.125
- w_down: bfloat16 [5632, 2048], P('tp'), may hold values from -0.078125 to 0.078125
Outputs:
- updated: bfloat16 [8192, 2048], P(('ctx', 'tp'))
- long_cache: bfloat16 [2, 2048, 512], P(None, 'ctx', 'tp')
- short_cache: bfloat16 [64, 64, 512], P('ctx', None, 'tp')
The draws below stay inside these ranges and needn't reach their ends.
Inputs may be any that keep to these rules, and one draw needn't show every extreme that they name: `short_lengths`: rows of a short prompt at or beyond its length are padding; the largest length is 64.
All inputs are finite; a program needn't handle non-finite values. No bound on the sum of `short_lengths` on one device may be relied on, other than what follows from the above.
Results may differ from the reference program's by a relative error of at most 0.022.
The reference program's roundings to bfloat16 on the way count: a program that leaves them out, or rounds other values in their place, can miss the bound.
Values may be sent and summed in bfloat16 or wider, within the bound.
No kernel may reach another device: no remote copies, remote signals or barrier semaphores. Data moves between devices by JAX's collectives and lax.ppermute only.
A program may use at most 64 MiB of HBM per device.

```python
import math
import jax
import jax.numpy as jnp
import numpy as np
from jax import lax

D = 2048
HEADS = 32
KVH = 4
HEAD_SIZE = 64
FF = 5632
LONG = 2
LLEN = 2048
SLEN = 64
SHORT_PER = 8
TOKENS = 8192
NSHORT = 64
CACHE_W = 512
N_CTX = 8
N_TP = 32


def draw_attn_gain(key, part):
    return 1.0 + 0.1 * jnp.clip(jax.random.normal(key, (D,), jnp.float32), -5.0, 5.0)


def level_of(own_key, dims, pieces, least, high):
    def one(axis_at, parts):
        draws = jax.random.uniform(jax.random.fold_in(jax.random.fold_in(own_key, 6), axis_at), (parts,), jnp.float32, least / len(pieces), high / len(pieces))
        return jnp.repeat(jnp.exp(draws), dims[axis_at] // parts).reshape((-1,) + (1,) * (len(dims) - axis_at - 1))

    factor_of = one(*pieces[0])
    for cut in pieces[1:]:
        factor_of = factor_of * one(*cut)
    return factor_of


def length_profile(number_of, total, most, skew):
    loads = [(1 << 20) // math.isqrt(standing ** skew) + 1 for standing in range(2, number_of + 1)]
    rest, given = total - most - (number_of - 1), [1] * (number_of - 1)
    while rest > 0:
        movable = [i for i in range(number_of - 1) if given[i] < most]
        pool, remaining = sum([loads[i] for i in movable]), rest
        for i in movable:
            more = min(most - given[i], max(1, remaining * loads[i] // pool), rest)
            given[i] = given[i] + more
            rest = rest - more
    return np.array([most] + given)


def uneven_parts(rng, amount, total, bound, slope):
    if amount == 2:
        one = jax.random.randint(rng, (), max(1, total - bound), min(bound, total - 1) + 1)
        return jnp.stack([one, total - one])
    tallies = jnp.asarray(length_profile(amount, total, bound, slope), jnp.int32)
    pairs = (amount - 1) // 2
    source_of, sink = tallies[1:1 + 2 * pairs:2], tallies[2:2 + 2 * pairs:2]
    margin = jnp.minimum(source_of - 1, bound - sink)
    shifted = jax.random.randint(jax.random.fold_in(rng, 1), (pairs,), 0, 1 << 20) % (margin + 1)
    tallies = tallies.at[1:1 + 2 * pairs:2].set(source_of - shifted).at[2:2 + 2 * pairs:2].set(sink + shifted)
    return tallies[jax.random.permutation(jax.random.fold_in(rng, 2), amount)]


def normal_values(key, extent, deviation, reach, cuts=(), kind=jnp.bfloat16):
    values = deviation * jax.random.normal(key, extent, jnp.float32)
    if cuts:
        values = values * level_of(key, extent, cuts, -0.22, 0.18)
    return jnp.clip(values, -reach, reach).astype(kind)


def setup_inputs(seed: int = 0) -> dict:
    key_list = jax.random.split(jax.random.key(seed), 11)
    return {
        "states": normal_values(key_list[0], (TOKENS, D), 1.0, 6.0, ((0, 256),)),
        "short_lengths": uneven_parts(key_list[1], NSHORT, NSHORT * SLEN * 3 // 4, SLEN, 2).astype(jnp.int32),
        "attn_gain": draw_attn_gain(jax.random.fold_in(key_list[10], 71), 0),
        "wq": normal_values(key_list[3], (D, HEADS * HEAD_SIZE), D ** -0.5, 0.125, ((1, 32),)),
        "wkv": normal_values(key_list[4], (D, CACHE_W), D ** -0.5, 0.125),
        "wo": normal_values(key_list[5], (HEADS * HEAD_SIZE, D), (HEADS * HEAD_SIZE) ** -0.5, 0.125, ((0, 32),)),
        "mlp_gain": jnp.clip(1.0 + 0.1 * jax.random.normal(key_list[6], (D,), jnp.float32), 0.5, 1.5),
        "w_gate": normal_values(key_list[7], (D, FF), D ** -0.5, 0.125, ((1, 32),)),
        "w_up": normal_values(key_list[8], (D, FF), D ** -0.5, 0.125, ((1, 32),)),
        "w_down": normal_values(key_list[9], (FF, D), FF ** -0.5, 0.078125, ((0, 32),)),
    }


EPS = 1e-05
THETA = 10000.0
NEG = -1e+30

def rms_scale(matrix, gain):
    entries = matrix.astype(jnp.float32)
    power = lax.optimization_barrier(jnp.mean(entries * entries, axis=-1, keepdims=True))
    return (entries * lax.rsqrt(power + EPS) * gain.astype(jnp.float32)).astype(jnp.bfloat16)

def rotate(entries, positions):
    half_width = entries.shape[-1] // 2
    frequency = THETA ** (-jnp.arange(half_width, dtype=jnp.float32) * 2.0 / entries.shape[-1])
    angles = positions.astype(jnp.float32)[:, None] * frequency[None, :]
    cosine = jnp.cos(angles)[:, None, :]
    sine_wave = jnp.sin(angles)[:, None, :]
    first_half = entries[..., :half_width]
    second_half = entries[..., half_width:]
    return jnp.concatenate([first_half * cosine - second_half * sine_wave, second_half * cosine + first_half * sine_wave], axis=-1)

def rank_positions(ctx_rank, rank_rows, block_len, long_rows, n_blocks):
    index_row = jnp.arange(rank_rows, dtype=jnp.int32)
    half_index = index_row // block_len % 2
    offset_row = index_row % block_len
    which_block = jnp.where(half_index == 0, ctx_rank, n_blocks - 1 - ctx_rank)
    long_pos = which_block * block_len + offset_row
    short_pos = (index_row - long_rows) % SLEN
    return jnp.where(index_row < long_rows, long_pos, short_pos).astype(jnp.int32)

def to_natural(flat, ranks, rank_rows, long_rows, block_len):
    tail = flat.shape[1:]
    grouped = flat.reshape((ranks, rank_rows) + tail)[:, :long_rows]
    grouped = grouped.reshape((ranks, LONG, 2, block_len) + tail)
    ordered = jnp.concatenate([grouped[:, :, 0], grouped[::-1, :, 1]], axis=0)
    ordered = jnp.moveaxis(ordered, 1, 0)
    return ordered.reshape((LONG, 2 * ranks * block_len) + tail)

def from_natural(natural, ranks, block_len):
    tail = natural.shape[2:]
    split_up = jnp.moveaxis(natural.reshape((LONG, 2 * ranks, block_len) + tail), 1, 0)
    paired = jnp.stack([split_up[:ranks], split_up[ranks:][::-1]], axis=2)
    return paired.reshape((ranks, LONG * 2 * block_len) + tail)

def soft_attend(query_matrix, key_matrix, value_matrix, allowed):
    logit_scores = jnp.einsum('ugt,uat->uga', query_matrix.astype(jnp.float32), key_matrix.astype(jnp.float32)) * HEAD_SIZE ** (-0.5)
    logit_scores = jnp.where(allowed, logit_scores, NEG)
    peak = lax.optimization_barrier(jnp.max(logit_scores, axis=-1, keepdims=True))
    weights = jnp.where(allowed, jnp.exp(logit_scores - peak), 0.0)
    attention_probability = lax.optimization_barrier(weights.astype(jnp.bfloat16)).astype(jnp.float32)
    context_sum = jnp.einsum('tse,ten->tsn', attention_probability, value_matrix.astype(jnp.float32))
    return (context_sum / lax.optimization_barrier(jnp.sum(weights, axis=-1, keepdims=True))).astype(jnp.bfloat16)

def grouped_sum(left, right, groups):
    span = left.shape[1] // groups
    left_parts = jnp.moveaxis(left.reshape(left.shape[0], groups, span), 1, 0)
    right_parts = right.reshape(groups, span, right.shape[1])

    def add_part(running, operands):
        partial_sum = jnp.dot(operands[0], operands[1], preferred_element_type=jnp.float32)
        partial_sum = lax.optimization_barrier(partial_sum.astype(jnp.bfloat16)).astype(jnp.float32)
        return (running + partial_sum, None)
    start_sum = jnp.zeros((left.shape[0], right.shape[1]), jnp.float32)
    return lax.scan(add_part, start_sum, (left_parts, right_parts))[0]

def reference(states, short_lengths, attn_gain, wq, wkv, wo, mlp_gain, w_gate, w_up, w_down):
    ranks = N_CTX
    n_blocks = 2 * ranks
    block_len = LLEN // n_blocks
    long_rows = LONG * 2 * block_len
    rank_rows = long_rows + SHORT_PER * SLEN
    tokens = rank_rows * ranks
    n_short = SHORT_PER * ranks
    group_size = HEADS // KVH
    positions = jax.vmap(lambda ctx_rank: rank_positions(ctx_rank, rank_rows, block_len, long_rows, n_blocks))(jnp.arange(ranks, dtype=jnp.int32)).reshape(-1)
    normed = rms_scale(states, attn_gain)
    query_matrix = rotate(jnp.dot(normed, wq, preferred_element_type=jnp.float32).reshape(tokens, HEADS, HEAD_SIZE), positions).astype(jnp.bfloat16)
    pairs = jnp.dot(normed, wkv, preferred_element_type=jnp.float32).reshape(tokens, KVH, 2, HEAD_SIZE)
    key_matrix = rotate(pairs[:, :, 0], positions).astype(jnp.bfloat16)
    value_matrix = pairs[:, :, 1].astype(jnp.bfloat16)
    long_q = to_natural(query_matrix, ranks, rank_rows, long_rows, block_len)
    long_k = to_natural(key_matrix, ranks, rank_rows, long_rows, block_len)
    long_v = to_natural(value_matrix, ranks, rank_rows, long_rows, block_len)
    long_cache = jnp.stack([long_k, long_v], axis=3).reshape(LONG, LLEN, 2 * KVH * HEAD_SIZE)
    natural_pos = jnp.arange(LLEN, dtype=jnp.int32)
    causal = (natural_pos[None, :] <= natural_pos[:, None])[None]
    rep_k = jnp.repeat(long_k, group_size, axis=2)
    rep_v = jnp.repeat(long_v, group_size, axis=2)

    def long_head(operands):
        return soft_attend(operands[0], operands[1], operands[2], causal)
    per_head = lax.map(long_head, (jnp.moveaxis(long_q, 2, 0), jnp.moveaxis(rep_k, 2, 0), jnp.moveaxis(rep_v, 2, 0)))
    long_out = from_natural(jnp.moveaxis(per_head, 0, 2), ranks, block_len)

    def short_part(flat):
        tail = flat.shape[1:]
        return flat.reshape((ranks, rank_rows) + tail)[:, long_rows:].reshape((n_short, SLEN) + tail)
    short_q = short_part(query_matrix)
    short_k = short_part(key_matrix)
    short_v = short_part(value_matrix)
    short_cache = jnp.stack([short_k, short_v], axis=3).reshape(n_short, SLEN, 2 * KVH * HEAD_SIZE)
    offsets = jnp.arange(SLEN, dtype=jnp.int32)
    short_mask = (offsets[None, :] <= offsets[:, None])[None] & (offsets[None, None, :] < short_lengths[:, None, None])
    short_mask = jnp.repeat(short_mask, HEADS, axis=0)
    batch_q = jnp.moveaxis(short_q, 2, 1).reshape(n_short * HEADS, SLEN, HEAD_SIZE)
    batch_k = jnp.moveaxis(jnp.repeat(short_k, group_size, axis=2), 2, 1).reshape(n_short * HEADS, SLEN, HEAD_SIZE)
    batch_v = jnp.moveaxis(jnp.repeat(short_v, group_size, axis=2), 2, 1).reshape(n_short * HEADS, SLEN, HEAD_SIZE)
    short_out = soft_attend(batch_q, batch_k, batch_v, short_mask).reshape(n_short, HEADS, SLEN, HEAD_SIZE)
    short_out = jnp.moveaxis(short_out, 1, 2).reshape(ranks, SHORT_PER * SLEN, HEADS, HEAD_SIZE)
    attn = jnp.concatenate([long_out, short_out], axis=1).reshape(tokens, HEADS * HEAD_SIZE)
    mixed = grouped_sum(attn, wo, N_TP)
    residual = (states.astype(jnp.float32) + mixed).astype(jnp.bfloat16)
    normed2 = rms_scale(residual, mlp_gain)
    gate = jnp.dot(normed2, w_gate, preferred_element_type=jnp.float32)
    up_part = jnp.dot(normed2, w_up, preferred_element_type=jnp.float32)
    hidden = (jax.nn.silu(gate) * up_part).astype(jnp.bfloat16)
    down = grouped_sum(hidden, w_down, N_TP)
    updated = (residual.astype(jnp.float32) + down).astype(jnp.bfloat16)
    return (updated, long_cache, short_cache)
```

```python
import jax
import jax.numpy as jnp
from jax import lax
from jax.sharding import PartitionSpec as P

KVH = 4
HEAD_SIZE = 64
LONG = 2
LLEN = 2048
SLEN = 64


EPS = 1e-05
THETA = 10000.0
NEG = -1e30


def rms_scale(matrix, gain):
    entries = matrix.astype(jnp.float32)
    power = jnp.mean(entries * entries, axis=-1, keepdims=True)
    return (entries * lax.rsqrt(power + EPS) * gain).astype(jnp.bfloat16)


def rotate(entries, positions):
    half_width = entries.shape[-1] // 2
    frequency = THETA ** (-jnp.arange(half_width, dtype=jnp.float32) * 2.0 / entries.shape[-1])
    angles = positions.astype(jnp.float32)[:, None] * frequency[None, :]
    cosine = jnp.cos(angles)[:, None, :]
    sine_wave = jnp.sin(angles)[:, None, :]
    first_half = entries[..., :half_width]
    second_half = entries[..., half_width:]
    return jnp.concatenate(
        [
            first_half * cosine - second_half * sine_wave,
            second_half * cosine + first_half * sine_wave,
        ],
        axis=-1,
    )


def rank_positions(ctx_rank, rank_rows, block_len, long_rows, n_blocks):
    index_row = jnp.arange(rank_rows, dtype=jnp.int32)
    half_index = index_row // block_len % 2
    offset_row = index_row % block_len
    which_block = jnp.where(half_index == 0, ctx_rank, n_blocks - 1 - ctx_rank)
    long_pos = which_block * block_len + offset_row
    short_pos = (index_row - long_rows) % SLEN
    return jnp.where(index_row < long_rows, long_pos, short_pos)


def project(matrix, positions, wq, wkv_head, heads_dev):
    row_count = matrix.shape[0]
    query_matrix = jnp.dot(matrix, wq, preferred_element_type=jnp.float32).reshape(
        row_count, heads_dev, HEAD_SIZE
    )
    query_matrix = rotate(query_matrix, positions).astype(jnp.bfloat16)
    pairs = jnp.dot(matrix, wkv_head, preferred_element_type=jnp.float32)
    key_matrix = rotate(pairs[:, None, :HEAD_SIZE], positions).astype(jnp.bfloat16)[:, 0]
    value_matrix = pairs[:, HEAD_SIZE:].astype(jnp.bfloat16)
    return jnp.concatenate(
        [query_matrix.reshape(row_count, heads_dev * HEAD_SIZE), key_matrix, value_matrix], axis=1
    )


def attend(soft_state, query_matrix, query_pos, key_matrix, value_matrix, key_pos, valid_keys):
    best_score, weight_sum, weighted = soft_state
    logit_scores = jnp.einsum(
        "rzsm,rvm->rzsv", query_matrix, key_matrix, preferred_element_type=jnp.float32
    ) * HEAD_SIZE ** (-0.5)
    allowed = (key_pos[None, :] <= query_pos[:, None])[None, None] & valid_keys[:, None, None, :]
    logit_scores = jnp.where(allowed, logit_scores, NEG)
    new_best = jnp.maximum(best_score, jnp.max(logit_scores, axis=-1))
    weights = jnp.where(allowed, jnp.exp(logit_scores - new_best[..., None]), 0.0)
    weight_sum = jnp.sum(weights, axis=-1)
    weighted = jnp.einsum(
        "awlp,ape->awle",
        weights.astype(jnp.bfloat16),
        value_matrix,
        preferred_element_type=jnp.float32,
    )
    return (new_best, weight_sum, weighted)


def per_device(states, short_lengths, attn_gain, wq, wkv, wo, mlp_gain, w_gate, w_up, w_down):
    n_ctx = lax.axis_size("ctx")
    n_tp = lax.axis_size("tp")
    ctx_rank = lax.axis_index("ctx")
    tp_index = lax.axis_index("tp")
    tok_rows = states.shape[0]
    rank_rows = tok_rows * n_tp
    n_blocks = 2 * n_ctx
    block_len = LLEN // n_blocks
    long_rows = LONG * 2 * block_len
    heads_dev = wq.shape[1] // HEAD_SIZE
    q_cols = heads_dev * HEAD_SIZE
    pair_width = 2 * HEAD_SIZE
    cache_cols = KVH * pair_width // n_tp
    kv_group = tp_index * KVH // n_tp
    wkv_head = lax.dynamic_slice_in_dim(wkv, kv_group * pair_width, pair_width, 1)
    first_col = tp_index * cache_cols - kv_group * pair_width
    positions = rank_positions(ctx_rank, rank_rows, block_len, long_rows, n_blocks)
    packed = project(
        lax.all_gather(rms_scale(states, attn_gain), "tp", axis=0, tiled=True),
        positions,
        wq,
        wkv_head,
        heads_dev,
    )
    query_matrix = packed[:, :q_cols].reshape(rank_rows, heads_dev, HEAD_SIZE)
    key_matrix = packed[:, q_cols : q_cols + HEAD_SIZE]
    value_matrix = packed[:, q_cols + HEAD_SIZE :]
    long_q = (
        query_matrix[:long_rows]
        .reshape(LONG, 2 * block_len, heads_dev, HEAD_SIZE)
        .transpose(0, 2, 1, 3)
    )
    long_k = key_matrix[:long_rows].reshape(LONG, 2, 1, block_len, HEAD_SIZE)
    long_v = value_matrix[:long_rows].reshape(LONG, 2, 1, block_len, HEAD_SIZE)
    long_qpos = positions[: 2 * block_len]
    half_pick = jnp.arange(2, dtype=jnp.int32)[:, None, None]
    long_init = (
        jnp.full((LONG, heads_dev, 2 * block_len), NEG, jnp.float32),
        jnp.zeros((LONG, heads_dev, 2 * block_len), jnp.float32),
        jnp.zeros((LONG, heads_dev, 2 * block_len, HEAD_SIZE), jnp.float32),
        jnp.zeros((LONG, 2, block_len, cache_cols), jnp.float32),
    )
    gathered = lax.all_gather(jnp.stack([long_k[:, :, 0], long_v[:, :, 0]]), "ctx", axis=0)
    piece_k = jnp.moveaxis(gathered[:, 0], 0, 2)
    piece_v = jnp.moveaxis(gathered[:, 1], 0, 2)
    piece_blocks = piece_k.shape[2]
    block_ids = jnp.arange(piece_blocks, dtype=jnp.int32)
    held_blocks = jnp.stack([block_ids, n_blocks - 1 - block_ids])
    key_pos = (
        held_blocks[:, :, None] * block_len + jnp.arange(block_len, dtype=jnp.int32)
    ).reshape(-1)
    key_count = 2 * piece_blocks * block_len
    flat_k = piece_k.reshape(LONG, key_count, HEAD_SIZE)
    flat_v = piece_v.reshape(LONG, key_count, HEAD_SIZE)
    all_valid = jnp.ones((LONG, key_count), dtype=bool)
    soft_state = long_init[:3]
    soft_state = attend(soft_state, long_q, long_qpos, flat_k, flat_v, key_pos, all_valid)
    joined = jnp.concatenate([piece_k, piece_v], axis=-1)
    own_cols = lax.dynamic_slice_in_dim(joined, first_col, cache_cols, 4)
    selector = ((held_blocks[None] // 2 == ctx_rank) & (held_blocks[None] % 2 == half_pick)).astype(
        jnp.bfloat16
    )
    cache_rows = jnp.einsum(
        "ehj,phjbc->pebc", selector, own_cols, preferred_element_type=jnp.float32
    )
    folded = soft_state + (cache_rows,)
    long_out = (
        (folded[2] / folded[1][..., None])
        .astype(jnp.bfloat16)
        .transpose(0, 2, 1, 3)
        .reshape(long_rows, q_cols)
    )
    long_cache = folded[3].astype(jnp.bfloat16).reshape(LONG, 2 * block_len, cache_cols)
    short_count = short_lengths.shape[0]
    short_q = (
        query_matrix[long_rows:]
        .reshape(short_count, SLEN, heads_dev, HEAD_SIZE)
        .transpose(0, 2, 1, 3)
    )
    short_k = key_matrix[long_rows:].reshape(short_count, SLEN, HEAD_SIZE)
    short_v = value_matrix[long_rows:].reshape(short_count, SLEN, HEAD_SIZE)
    offsets = jnp.arange(SLEN, dtype=jnp.int32)
    short_valid = offsets[None, :] < short_lengths[:, None]
    short_init = (
        jnp.full((short_count, heads_dev, SLEN), NEG, jnp.float32),
        jnp.zeros((short_count, heads_dev, SLEN), jnp.float32),
        jnp.zeros((short_count, heads_dev, SLEN, HEAD_SIZE), jnp.float32),
    )
    short_state = attend(short_init, short_q, offsets, short_k, short_v, offsets, short_valid)
    short_out = (
        (short_state[2] / short_state[1][..., None])
        .astype(jnp.bfloat16)
        .transpose(0, 2, 1, 3)
        .reshape(short_count * SLEN, q_cols)
    )
    short_cache = lax.dynamic_slice_in_dim(
        jnp.concatenate([short_k, short_v], axis=-1), first_col, cache_cols, 2
    )
    attn = jnp.concatenate([long_out, short_out], axis=0)
    mixed = lax.psum_scatter(
        jnp.dot(attn, wo, preferred_element_type=jnp.float32).astype(jnp.bfloat16),
        "tp",
        scatter_dimension=0,
        tiled=True,
    ).astype(jnp.float32)
    residual = (states.astype(jnp.float32) + mixed).astype(jnp.bfloat16)
    piece = lax.all_gather(rms_scale(residual, mlp_gain), "tp", axis=0, tiled=True)
    gate = jnp.dot(piece, w_gate, preferred_element_type=jnp.float32)
    up_part = jnp.dot(piece, w_up, preferred_element_type=jnp.float32)
    hidden = (jax.nn.silu(gate) * up_part).astype(jnp.bfloat16)
    down = lax.psum_scatter(
        jnp.dot(hidden, w_down, preferred_element_type=jnp.float32).astype(jnp.bfloat16),
        "tp",
        scatter_dimension=0,
        tiled=True,
    ).astype(jnp.float32)
    updated = (residual.astype(jnp.float32) + down).astype(jnp.bfloat16)
    return (updated, long_cache, short_cache)


def solution(mesh):
    in_specs = (
        P(("ctx", "tp"), None),
        P("ctx"),
        P(),
        P(None, "tp"),
        P(),
        P("tp", None),
        P(),
        P(None, "tp"),
        P(None, "tp"),
        P("tp", None),
    )
    out_specs = (P(("ctx", "tp"), None), P(None, "ctx", "tp"), P("ctx", None, "tp"))
    return jax.shard_map(
        per_device, mesh=mesh, in_specs=in_specs, out_specs=out_specs, check_vma=False
    )
```

```python
import jax
import jax.numpy as jnp
from jax import lax
from jax.sharding import PartitionSpec as P

KVH = 4
HEAD_SIZE = 64
LONG = 2
LLEN = 2048
SLEN = 64


EPS = 1e-05
THETA = 10000.0
NEG = -1e30


def rms_scale(matrix, gain):
    entries = matrix.astype(jnp.float32)
    power = jnp.mean(entries * entries, axis=-1, keepdims=True)
    return (entries * lax.rsqrt(power + EPS) * gain).astype(jnp.bfloat16)


def rotate(entries, positions):
    half_width = entries.shape[-1] // 2
    frequency = THETA ** (-jnp.arange(half_width, dtype=jnp.float32) * 2.0 / entries.shape[-1])
    angles = positions.astype(jnp.float32)[:, None] * frequency[None, :]
    cosine = jnp.cos(angles)[:, None, :]
    sine_wave = jnp.sin(angles)[:, None, :]
    first_half = entries[..., :half_width]
    second_half = entries[..., half_width:]
    return jnp.concatenate(
        [
            first_half * cosine - second_half * sine_wave,
            second_half * cosine + first_half * sine_wave,
        ],
        axis=-1,
    )


def rank_positions(ctx_rank, rank_rows, block_len, long_rows, n_blocks):
    index_row = jnp.arange(rank_rows, dtype=jnp.int32)
    half_index = index_row // block_len % 2
    offset_row = index_row % block_len
    which_block = jnp.where(half_index == 0, ctx_rank, n_blocks - 1 - ctx_rank)
    long_pos = which_block * block_len + offset_row
    short_pos = (index_row - long_rows) % SLEN
    return jnp.where(index_row < long_rows, long_pos, short_pos)


TP_DIMS = ((4, 8), (4, 2), (2, 1))


def shift_perm(n, stride, d, total):
    return [(t, t + (((t // stride) % n + d) % n - (t // stride) % n) * stride) for t in range(total)]


def scatter_stage(x, axis, n, stride, total):
    me = (lax.axis_index("tp") // stride) % n
    acc = lax.dynamic_index_in_dim(x, me, axis, keepdims=False).astype(jnp.float32)
    for d in range(1, n):
        part = lax.dynamic_index_in_dim(x, (me + d) % n, axis, keepdims=False)
        got = lax.ppermute(part.astype(jnp.bfloat16), "tp", shift_perm(n, stride, d, total))
        acc = acc + got.astype(jnp.float32)
    return acc


def tp_reduce_scatter(x):
    total = lax.axis_size("tp")
    rows, width = x.shape
    sizes = [n for n, _ in TP_DIMS]
    x = x.reshape(tuple(sizes) + (rows // total, width))
    for axis in reversed(range(len(TP_DIMS))):
        n, stride = TP_DIMS[axis]
        x = scatter_stage(x, axis, n, stride, total)
    return x


def gather_stage(x, axis, n, stride, total):
    me = (lax.axis_index("tp") // stride) % n
    parts = [x] + [
        lax.ppermute(x, "tp", shift_perm(n, stride, (n - k) % n, total)) for k in range(1, n)
    ]
    return jnp.roll(jnp.stack(parts, axis=axis), me, axis=axis)


def tp_all_gather(x):
    total = lax.axis_size("tp")
    rows, width = x.shape
    for axis, (n, stride) in enumerate(TP_DIMS):
        x = gather_stage(x, axis, n, stride, total)
    return x.reshape(rows * total, width)


def ctx_all_gather(x):
    n = lax.axis_size("ctx")
    me = lax.axis_index("ctx")
    parts = [x] + [
        lax.ppermute(x, "ctx", [(j, (j - k) % n) for j in range(n)]) for k in range(1, n)
    ]
    return jnp.roll(jnp.stack(parts), me, axis=0)


def project(matrix, positions, wq, wkv_head, heads_dev):
    row_count = matrix.shape[0]
    query_matrix = jnp.dot(matrix, wq, preferred_element_type=jnp.float32).reshape(
        row_count, heads_dev, HEAD_SIZE
    )
    query_matrix = rotate(query_matrix, positions).astype(jnp.bfloat16)
    pairs = jnp.dot(matrix, wkv_head, preferred_element_type=jnp.float32)
    key_matrix = rotate(pairs[:, None, :HEAD_SIZE], positions).astype(jnp.bfloat16)[:, 0]
    value_matrix = pairs[:, HEAD_SIZE:].astype(jnp.bfloat16)
    return jnp.concatenate(
        [query_matrix.reshape(row_count, heads_dev * HEAD_SIZE), key_matrix, value_matrix], axis=1
    )


def attend(soft_state, query_matrix, query_pos, key_matrix, value_matrix, key_pos, valid_keys):
    best_score, weight_sum, weighted = soft_state
    logit_scores = jnp.einsum(
        "rzsm,rvm->rzsv", query_matrix, key_matrix, preferred_element_type=jnp.float32
    ) * HEAD_SIZE ** (-0.5)
    allowed = (key_pos[None, :] <= query_pos[:, None])[None, None] & valid_keys[:, None, None, :]
    logit_scores = jnp.where(allowed, logit_scores, NEG)
    new_best = jnp.maximum(best_score, jnp.max(logit_scores, axis=-1))
    weights = jnp.where(allowed, jnp.exp(logit_scores - new_best[..., None]), 0.0)
    weight_sum = jnp.sum(weights, axis=-1)
    weighted = jnp.einsum(
        "awlp,ape->awle",
        weights.astype(jnp.bfloat16),
        value_matrix,
        preferred_element_type=jnp.float32,
    )
    return (new_best, weight_sum, weighted)


def per_device(states, short_lengths, attn_gain, wq, wkv, wo, mlp_gain, w_gate, w_up, w_down):
    n_ctx = lax.axis_size("ctx")
    n_tp = lax.axis_size("tp")
    ctx_rank = lax.axis_index("ctx")
    tp_index = lax.axis_index("tp")
    tok_rows = states.shape[0]
    rank_rows = tok_rows * n_tp
    n_blocks = 2 * n_ctx
    block_len = LLEN // n_blocks
    long_rows = LONG * 2 * block_len
    heads_dev = wq.shape[1] // HEAD_SIZE
    q_cols = heads_dev * HEAD_SIZE
    pair_width = 2 * HEAD_SIZE
    cache_cols = KVH * pair_width // n_tp
    kv_group = tp_index * KVH // n_tp
    wkv_head = lax.dynamic_slice_in_dim(wkv, kv_group * pair_width, pair_width, 1)
    first_col = tp_index * cache_cols - kv_group * pair_width
    positions = rank_positions(ctx_rank, rank_rows, block_len, long_rows, n_blocks)
    packed = project(
        tp_all_gather(rms_scale(states, attn_gain)),
        positions,
        wq,
        wkv_head,
        heads_dev,
    )
    query_matrix = packed[:, :q_cols].reshape(rank_rows, heads_dev, HEAD_SIZE)
    key_matrix = packed[:, q_cols : q_cols + HEAD_SIZE]
    value_matrix = packed[:, q_cols + HEAD_SIZE :]
    long_q = (
        query_matrix[:long_rows]
        .reshape(LONG, 2 * block_len, heads_dev, HEAD_SIZE)
        .transpose(0, 2, 1, 3)
    )
    long_k = key_matrix[:long_rows].reshape(LONG, 2, 1, block_len, HEAD_SIZE)
    long_v = value_matrix[:long_rows].reshape(LONG, 2, 1, block_len, HEAD_SIZE)
    long_qpos = positions[: 2 * block_len]
    half_pick = jnp.arange(2, dtype=jnp.int32)[:, None, None]
    long_init = (
        jnp.full((LONG, heads_dev, 2 * block_len), NEG, jnp.float32),
        jnp.zeros((LONG, heads_dev, 2 * block_len), jnp.float32),
        jnp.zeros((LONG, heads_dev, 2 * block_len, HEAD_SIZE), jnp.float32),
        jnp.zeros((LONG, 2, block_len, cache_cols), jnp.float32),
    )
    gathered = ctx_all_gather(jnp.stack([long_k[:, :, 0], long_v[:, :, 0]]))
    piece_k = jnp.moveaxis(gathered[:, 0], 0, 2)
    piece_v = jnp.moveaxis(gathered[:, 1], 0, 2)
    piece_blocks = piece_k.shape[2]
    block_ids = jnp.arange(piece_blocks, dtype=jnp.int32)
    held_blocks = jnp.stack([block_ids, n_blocks - 1 - block_ids])
    key_pos = (
        held_blocks[:, :, None] * block_len + jnp.arange(block_len, dtype=jnp.int32)
    ).reshape(-1)
    key_count = 2 * piece_blocks * block_len
    flat_k = piece_k.reshape(LONG, key_count, HEAD_SIZE)
    flat_v = piece_v.reshape(LONG, key_count, HEAD_SIZE)
    all_valid = jnp.ones((LONG, key_count), dtype=bool)
    soft_state = long_init[:3]
    soft_state = attend(soft_state, long_q, long_qpos, flat_k, flat_v, key_pos, all_valid)
    joined = jnp.concatenate([piece_k, piece_v], axis=-1)
    own_cols = lax.dynamic_slice_in_dim(joined, first_col, cache_cols, 4)
    selector = ((held_blocks[None] // 2 == ctx_rank) & (held_blocks[None] % 2 == half_pick)).astype(
        jnp.bfloat16
    )
    cache_rows = jnp.einsum(
        "ehj,phjbc->pebc", selector, own_cols, preferred_element_type=jnp.float32
    )
    folded = soft_state + (cache_rows,)
    long_out = (
        (folded[2] / folded[1][..., None])
        .astype(jnp.bfloat16)
        .transpose(0, 2, 1, 3)
        .reshape(long_rows, q_cols)
    )
    long_cache = folded[3].astype(jnp.bfloat16).reshape(LONG, 2 * block_len, cache_cols)
    short_count = short_lengths.shape[0]
    short_q = (
        query_matrix[long_rows:]
        .reshape(short_count, SLEN, heads_dev, HEAD_SIZE)
        .transpose(0, 2, 1, 3)
    )
    short_k = key_matrix[long_rows:].reshape(short_count, SLEN, HEAD_SIZE)
    short_v = value_matrix[long_rows:].reshape(short_count, SLEN, HEAD_SIZE)
    offsets = jnp.arange(SLEN, dtype=jnp.int32)
    short_valid = offsets[None, :] < short_lengths[:, None]
    short_init = (
        jnp.full((short_count, heads_dev, SLEN), NEG, jnp.float32),
        jnp.zeros((short_count, heads_dev, SLEN), jnp.float32),
        jnp.zeros((short_count, heads_dev, SLEN, HEAD_SIZE), jnp.float32),
    )
    short_state = attend(short_init, short_q, offsets, short_k, short_v, offsets, short_valid)
    short_out = (
        (short_state[2] / short_state[1][..., None])
        .astype(jnp.bfloat16)
        .transpose(0, 2, 1, 3)
        .reshape(short_count * SLEN, q_cols)
    )
    short_cache = lax.dynamic_slice_in_dim(
        jnp.concatenate([short_k, short_v], axis=-1), first_col, cache_cols, 2
    )
    attn = jnp.concatenate([long_out, short_out], axis=0)
    mixed = tp_reduce_scatter(
        jnp.dot(attn, wo, preferred_element_type=jnp.float32).astype(jnp.bfloat16)
    )
    residual = (states.astype(jnp.float32) + mixed).astype(jnp.bfloat16)
    piece = tp_all_gather(rms_scale(residual, mlp_gain))
    gate = jnp.dot(piece, w_gate, preferred_element_type=jnp.float32)
    up_part = jnp.dot(piece, w_up, preferred_element_type=jnp.float32)
    hidden = (jax.nn.silu(gate) * up_part).astype(jnp.bfloat16)
    down = tp_reduce_scatter(
        jnp.dot(hidden, w_down, preferred_element_type=jnp.float32).astype(jnp.bfloat16)
    )
    updated = (residual.astype(jnp.float32) + down).astype(jnp.bfloat16)
    return (updated, long_cache, short_cache)


def solution(mesh):
    in_specs = (
        P(("ctx", "tp"), None),
        P("ctx"),
        P(),
        P(None, "tp"),
        P(),
        P("tp", None),
        P(),
        P(None, "tp"),
        P(None, "tp"),
        P("tp", None),
    )
    out_specs = (P(("ctx", "tp"), None), P(None, "ctx", "tp"), P("ctx", None, "tp"))
    return jax.shard_map(
        per_device, mesh=mesh, in_specs=in_specs, out_specs=out_specs, check_vma=False
    )
```

```python
import jax
import jax.numpy as jnp
from jax import lax
from jax.sharding import PartitionSpec as P

KVH = 4
HEAD_SIZE = 64
LONG = 2
LLEN = 2048
SLEN = 64


EPS = 1e-05
THETA = 10000.0
NEG = -1e30


def rms_scale(matrix, gain):
    entries = matrix.astype(jnp.float32)
    power = jnp.mean(entries * entries, axis=-1, keepdims=True)
    return (entries * lax.rsqrt(power + EPS) * gain).astype(jnp.bfloat16)


def rotate(entries, positions):
    half_width = entries.shape[-1] // 2
    frequency = THETA ** (-jnp.arange(half_width, dtype=jnp.float32) * 2.0 / entries.shape[-1])
    angles = positions.astype(jnp.float32)[:, None] * frequency[None, :]
    cosine = jnp.cos(angles)[:, None, :]
    sine_wave = jnp.sin(angles)[:, None, :]
    first_half = entries[..., :half_width]
    second_half = entries[..., half_width:]
    return jnp.concatenate(
        [
            first_half * cosine - second_half * sine_wave,
            second_half * cosine + first_half * sine_wave,
        ],
        axis=-1,
    )


def rank_positions(ctx_rank, rank_rows, block_len, long_rows, n_blocks):
    index_row = jnp.arange(rank_rows, dtype=jnp.int32)
    half_index = index_row // block_len % 2
    offset_row = index_row % block_len
    which_block = jnp.where(half_index == 0, ctx_rank, n_blocks - 1 - ctx_rank)
    long_pos = which_block * block_len + offset_row
    short_pos = (index_row - long_rows) % SLEN
    return jnp.where(index_row < long_rows, long_pos, short_pos)


TP_DIMS = ((4, 8), (4, 2), (2, 1))


def shift_perm(n, stride, d, total):
    return [(t, t + (((t // stride) % n + d) % n - (t // stride) % n) * stride) for t in range(total)]


def scatter_stage(x, axis, n, stride, total):
    me = (lax.axis_index("tp") // stride) % n
    acc = lax.dynamic_index_in_dim(x, me, axis, keepdims=False).astype(jnp.float32)
    for d in range(1, n):
        part = lax.dynamic_index_in_dim(x, (me + d) % n, axis, keepdims=False)
        got = lax.ppermute(part.astype(jnp.bfloat16), "tp", shift_perm(n, stride, d, total))
        acc = acc + got.astype(jnp.float32)
    return acc


def tp_reduce_scatter(x):
    total = lax.axis_size("tp")
    rows, width = x.shape
    sizes = [n for n, _ in TP_DIMS]
    x = x.reshape(tuple(sizes) + (rows // total, width))
    for axis in reversed(range(len(TP_DIMS))):
        n, stride = TP_DIMS[axis]
        x = scatter_stage(x, axis, n, stride, total)
    return x


def gather_stage(x, axis, n, stride, total, placed):
    parts = [x] + [
        lax.ppermute(x, "tp", shift_perm(n, stride, (n - k) % n, total)) for k in range(1, n)
    ]
    if not placed:
        return jnp.stack(parts, axis=axis)
    me = (lax.axis_index("tp") // stride) % n
    out = jnp.zeros(x.shape[:axis] + (n,) + x.shape[axis:], x.dtype)
    for k, part in enumerate(parts):
        out = lax.dynamic_update_index_in_dim(out, part, (me + k) % n, axis)
    return out


def tp_all_gather(x, placed=True):
    total = lax.axis_size("tp")
    rows, width = x.shape
    for axis, (n, stride) in enumerate(TP_DIMS):
        x = gather_stage(x, axis, n, stride, total, placed)
    return x.reshape(rows * total, width)


def relative_scatter_stage(x, axis, n, stride, total):
    acc = lax.index_in_dim(x, 0, axis, keepdims=False).astype(jnp.float32)
    for d in range(1, n):
        part = lax.index_in_dim(x, d, axis, keepdims=False)
        got = lax.ppermute(part.astype(jnp.bfloat16), "tp", shift_perm(n, stride, d, total))
        acc = acc + got.astype(jnp.float32)
    return acc


def tp_reduce_scatter_relative(x):
    total = lax.axis_size("tp")
    rows, width = x.shape
    sizes = [n for n, _ in TP_DIMS]
    x = x.reshape(tuple(sizes) + (rows // total, width))
    for axis in reversed(range(len(TP_DIMS))):
        n, stride = TP_DIMS[axis]
        x = relative_scatter_stage(x, axis, n, stride, total)
    return x


def ctx_all_gather(x):
    n = lax.axis_size("ctx")
    parts = [x] + [
        lax.ppermute(x, "ctx", [(j, (j - k) % n) for j in range(n)]) for k in range(1, n)
    ]
    return jnp.stack(parts)


def project(matrix, positions, wq, wkv_head, heads_dev):
    row_count = matrix.shape[0]
    query_matrix = jnp.dot(matrix, wq, preferred_element_type=jnp.float32).reshape(
        row_count, heads_dev, HEAD_SIZE
    )
    query_matrix = rotate(query_matrix, positions).astype(jnp.bfloat16)
    pairs = jnp.dot(matrix, wkv_head, preferred_element_type=jnp.float32)
    key_matrix = rotate(pairs[:, None, :HEAD_SIZE], positions).astype(jnp.bfloat16)[:, 0]
    value_matrix = pairs[:, HEAD_SIZE:].astype(jnp.bfloat16)
    return jnp.concatenate(
        [query_matrix.reshape(row_count, heads_dev * HEAD_SIZE), key_matrix, value_matrix], axis=1
    )


def attend(soft_state, query_matrix, query_pos, key_matrix, value_matrix, key_pos, valid_keys):
    best_score, weight_sum, weighted = soft_state
    logit_scores = jnp.einsum(
        "rzsm,rvm->rzsv", query_matrix, key_matrix, preferred_element_type=jnp.float32
    ) * HEAD_SIZE ** (-0.5)
    allowed = (key_pos[None, :] <= query_pos[:, None])[None, None] & valid_keys[:, None, None, :]
    logit_scores = jnp.where(allowed, logit_scores, NEG)
    new_best = jnp.maximum(best_score, jnp.max(logit_scores, axis=-1))
    weights = jnp.where(allowed, jnp.exp(logit_scores - new_best[..., None]), 0.0)
    weight_sum = jnp.sum(weights, axis=-1)
    weighted = jnp.einsum(
        "awlp,ape->awle",
        weights.astype(jnp.bfloat16),
        value_matrix,
        preferred_element_type=jnp.float32,
    )
    return (new_best, weight_sum, weighted)


def per_device(states, short_lengths, attn_gain, wq, wkv, wo, mlp_gain, w_gate, w_up, w_down):
    n_ctx = lax.axis_size("ctx")
    n_tp = lax.axis_size("tp")
    ctx_rank = lax.axis_index("ctx")
    tp_index = lax.axis_index("tp")
    tok_rows = states.shape[0]
    rank_rows = tok_rows * n_tp
    n_blocks = 2 * n_ctx
    block_len = LLEN // n_blocks
    long_rows = LONG * 2 * block_len
    heads_dev = wq.shape[1] // HEAD_SIZE
    q_cols = heads_dev * HEAD_SIZE
    pair_width = 2 * HEAD_SIZE
    cache_cols = KVH * pair_width // n_tp
    kv_group = tp_index * KVH // n_tp
    wkv_head = lax.dynamic_slice_in_dim(wkv, kv_group * pair_width, pair_width, 1)
    first_col = tp_index * cache_cols - kv_group * pair_width
    positions = rank_positions(ctx_rank, rank_rows, block_len, long_rows, n_blocks)
    packed = project(
        tp_all_gather(rms_scale(states, attn_gain)),
        positions,
        wq,
        wkv_head,
        heads_dev,
    )
    query_matrix = packed[:, :q_cols].reshape(rank_rows, heads_dev, HEAD_SIZE)
    key_matrix = packed[:, q_cols : q_cols + HEAD_SIZE]
    value_matrix = packed[:, q_cols + HEAD_SIZE :]
    long_q = (
        query_matrix[:long_rows]
        .reshape(LONG, 2 * block_len, heads_dev, HEAD_SIZE)
        .transpose(0, 2, 1, 3)
    )
    long_k = key_matrix[:long_rows].reshape(LONG, 2, 1, block_len, HEAD_SIZE)
    long_v = value_matrix[:long_rows].reshape(LONG, 2, 1, block_len, HEAD_SIZE)
    long_qpos = positions[: 2 * block_len]
    half_pick = jnp.arange(2, dtype=jnp.int32)[:, None, None]
    long_init = (
        jnp.full((LONG, heads_dev, 2 * block_len), NEG, jnp.float32),
        jnp.zeros((LONG, heads_dev, 2 * block_len), jnp.float32),
        jnp.zeros((LONG, heads_dev, 2 * block_len, HEAD_SIZE), jnp.float32),
        jnp.zeros((LONG, 2, block_len, cache_cols), jnp.float32),
    )
    gathered = ctx_all_gather(jnp.stack([long_k[:, :, 0], long_v[:, :, 0]]))
    piece_k = jnp.moveaxis(gathered[:, 0], 0, 2)
    piece_v = jnp.moveaxis(gathered[:, 1], 0, 2)
    piece_blocks = piece_k.shape[2]
    block_ids = (ctx_rank + jnp.arange(piece_blocks, dtype=jnp.int32)) % n_ctx
    held_blocks = jnp.stack([block_ids, n_blocks - 1 - block_ids])
    key_pos = (
        held_blocks[:, :, None] * block_len + jnp.arange(block_len, dtype=jnp.int32)
    ).reshape(-1)
    key_count = 2 * piece_blocks * block_len
    flat_k = piece_k.reshape(LONG, key_count, HEAD_SIZE)
    flat_v = piece_v.reshape(LONG, key_count, HEAD_SIZE)
    all_valid = jnp.ones((LONG, key_count), dtype=bool)
    soft_state = long_init[:3]
    soft_state = attend(soft_state, long_q, long_qpos, flat_k, flat_v, key_pos, all_valid)
    joined = jnp.concatenate([piece_k, piece_v], axis=-1)
    own_cols = lax.dynamic_slice_in_dim(joined, first_col, cache_cols, 4)
    selector = ((held_blocks[None] // 2 == ctx_rank) & (held_blocks[None] % 2 == half_pick)).astype(
        jnp.bfloat16
    )
    cache_rows = jnp.einsum(
        "ehj,phjbc->pebc", selector, own_cols, preferred_element_type=jnp.float32
    )
    folded = soft_state + (cache_rows,)
    long_out = (
        (folded[2] / folded[1][..., None])
        .astype(jnp.bfloat16)
        .transpose(0, 2, 1, 3)
        .reshape(long_rows, q_cols)
    )
    long_cache = folded[3].astype(jnp.bfloat16).reshape(LONG, 2 * block_len, cache_cols)
    short_count = short_lengths.shape[0]
    short_q = (
        query_matrix[long_rows:]
        .reshape(short_count, SLEN, heads_dev, HEAD_SIZE)
        .transpose(0, 2, 1, 3)
    )
    short_k = key_matrix[long_rows:].reshape(short_count, SLEN, HEAD_SIZE)
    short_v = value_matrix[long_rows:].reshape(short_count, SLEN, HEAD_SIZE)
    offsets = jnp.arange(SLEN, dtype=jnp.int32)
    short_valid = offsets[None, :] < short_lengths[:, None]
    short_init = (
        jnp.full((short_count, heads_dev, SLEN), NEG, jnp.float32),
        jnp.zeros((short_count, heads_dev, SLEN), jnp.float32),
        jnp.zeros((short_count, heads_dev, SLEN, HEAD_SIZE), jnp.float32),
    )
    short_state = attend(short_init, short_q, offsets, short_k, short_v, offsets, short_valid)
    short_out = (
        (short_state[2] / short_state[1][..., None])
        .astype(jnp.bfloat16)
        .transpose(0, 2, 1, 3)
        .reshape(short_count * SLEN, q_cols)
    )
    short_cache = lax.dynamic_slice_in_dim(
        jnp.concatenate([short_k, short_v], axis=-1), first_col, cache_cols, 2
    )
    attn = jnp.concatenate([long_out, short_out], axis=0)
    mixed = tp_reduce_scatter(
        jnp.dot(attn, wo, preferred_element_type=jnp.float32).astype(jnp.bfloat16)
    )
    residual = (states.astype(jnp.float32) + mixed).astype(jnp.bfloat16)
    piece = tp_all_gather(rms_scale(residual, mlp_gain), placed=False)
    gate = jnp.dot(piece, w_gate, preferred_element_type=jnp.float32)
    up_part = jnp.dot(piece, w_up, preferred_element_type=jnp.float32)
    hidden = (jax.nn.silu(gate) * up_part).astype(jnp.bfloat16)
    down = tp_reduce_scatter_relative(
        jnp.dot(hidden, w_down, preferred_element_type=jnp.float32).astype(jnp.bfloat16)
    )
    updated = (residual.astype(jnp.float32) + down).astype(jnp.bfloat16)
    return (updated, long_cache, short_cache)


def solution(mesh):
    in_specs = (
        P(("ctx", "tp"), None),
        P("ctx"),
        P(),
        P(None, "tp"),
        P(),
        P("tp", None),
        P(),
        P(None, "tp"),
        P(None, "tp"),
        P("tp", None),
    )
    out_specs = (P(("ctx", "tp"), None), P(None, "ctx", "tp"), P("ctx", None, "tp"))
    return jax.shard_map(
        per_device, mesh=mesh, in_specs=in_specs, out_specs=out_specs, check_vma=False
    )
```

```python
import jax
import jax.numpy as jnp
from jax import lax
from jax.sharding import PartitionSpec as P

KVH = 4
HEAD_SIZE = 64
LONG = 2
LLEN = 2048
SLEN = 64


EPS = 1e-05
THETA = 10000.0
NEG = -1e30


def rms_scale(matrix, gain):
    entries = matrix.astype(jnp.float32)
    power = jnp.mean(entries * entries, axis=-1, keepdims=True)
    return (entries * lax.rsqrt(power + EPS) * gain).astype(jnp.bfloat16)


def rotate(entries, positions):
    half_width = entries.shape[-1] // 2
    frequency = THETA ** (-jnp.arange(half_width, dtype=jnp.float32) * 2.0 / entries.shape[-1])
    angles = positions.astype(jnp.float32)[:, None] * frequency[None, :]
    cosine = jnp.cos(angles)[:, None, :]
    sine_wave = jnp.sin(angles)[:, None, :]
    first_half = entries[..., :half_width]
    second_half = entries[..., half_width:]
    return jnp.concatenate(
        [
            first_half * cosine - second_half * sine_wave,
            second_half * cosine + first_half * sine_wave,
        ],
        axis=-1,
    )


def rank_positions(ctx_rank, rank_rows, block_len, long_rows, n_blocks):
    index_row = jnp.arange(rank_rows, dtype=jnp.int32)
    half_index = index_row // block_len % 2
    offset_row = index_row % block_len
    which_block = jnp.where(half_index == 0, ctx_rank, n_blocks - 1 - ctx_rank)
    long_pos = which_block * block_len + offset_row
    short_pos = (index_row - long_rows) % SLEN
    return jnp.where(index_row < long_rows, long_pos, short_pos)


TP_DIMS = ((4, 8), (4, 2), (2, 1))


def shift_perm(n, stride, d, total):
    return [(t, t + (((t // stride) % n + d) % n - (t // stride) % n) * stride) for t in range(total)]


def scatter_stage(x, axis, n, stride, total):
    me = (lax.axis_index("tp") // stride) % n
    acc = lax.dynamic_index_in_dim(x, me, axis, keepdims=False).astype(jnp.float32)
    for d in range(1, n):
        part = lax.dynamic_index_in_dim(x, (me + d) % n, axis, keepdims=False)
        got = lax.ppermute(part.astype(jnp.bfloat16), "tp", shift_perm(n, stride, d, total))
        acc = acc + got.astype(jnp.float32)
    return acc


def tp_reduce_scatter(x):
    total = lax.axis_size("tp")
    rows, width = x.shape
    sizes = [n for n, _ in TP_DIMS]
    x = x.reshape(tuple(sizes) + (rows // total, width))
    for axis in reversed(range(len(TP_DIMS))):
        n, stride = TP_DIMS[axis]
        x = scatter_stage(x, axis, n, stride, total)
    return x


def gather_stage(x, axis, n, stride, total, placed):
    parts = [x] + [
        lax.ppermute(x, "tp", shift_perm(n, stride, (n - k) % n, total)) for k in range(1, n)
    ]
    if not placed:
        return jnp.stack(parts, axis=axis)
    me = (lax.axis_index("tp") // stride) % n
    out = jnp.zeros(x.shape[:axis] + (n,) + x.shape[axis:], x.dtype)
    for k, part in enumerate(parts):
        out = lax.dynamic_update_index_in_dim(out, part, (me + k) % n, axis)
    return out


def tp_all_gather(x, placed=True):
    total = lax.axis_size("tp")
    rows, width = x.shape
    for axis, (n, stride) in enumerate(TP_DIMS):
        x = gather_stage(x, axis, n, stride, total, placed)
    return x.reshape(rows * total, width)


def relative_scatter_stage(x, axis, n, stride, total):
    acc = lax.index_in_dim(x, 0, axis, keepdims=False).astype(jnp.float32)
    for d in range(1, n):
        part = lax.index_in_dim(x, d, axis, keepdims=False)
        got = lax.ppermute(part.astype(jnp.bfloat16), "tp", shift_perm(n, stride, d, total))
        acc = acc + got.astype(jnp.float32)
    return acc


def tp_reduce_scatter_relative(x):
    total = lax.axis_size("tp")
    rows, width = x.shape
    sizes = [n for n, _ in TP_DIMS]
    x = x.reshape(tuple(sizes) + (rows // total, width))
    for axis in reversed(range(len(TP_DIMS))):
        n, stride = TP_DIMS[axis]
        x = relative_scatter_stage(x, axis, n, stride, total)
    return x


def ctx_all_gather(x):
    n = lax.axis_size("ctx")
    parts = [x] + [
        lax.ppermute(x, "ctx", [(j, (j - k) % n) for j in range(n)]) for k in range(1, n)
    ]
    return jnp.stack(parts)


CHUNKS = 2


def column_chunks(matrix, axis=1):
    width = matrix.shape[axis] // CHUNKS
    return [lax.slice_in_dim(matrix, i * width, (i + 1) * width, axis=axis) for i in range(CHUNKS)]


def split_dot(pieces, weight):
    parts = column_chunks(weight, axis=0)
    total = jnp.dot(pieces[0], parts[0], preferred_element_type=jnp.float32)
    for piece, part in zip(pieces[1:], parts[1:]):
        total = total + jnp.dot(piece, part, preferred_element_type=jnp.float32)
    return total


def project(pieces, positions, wq, wkv_head, heads_dev):
    row_count = pieces[0].shape[0]
    query_matrix = split_dot(pieces, wq).reshape(row_count, heads_dev, HEAD_SIZE)
    query_matrix = rotate(query_matrix, positions).astype(jnp.bfloat16)
    pairs = split_dot(pieces, wkv_head)
    key_matrix = rotate(pairs[:, None, :HEAD_SIZE], positions).astype(jnp.bfloat16)[:, 0]
    value_matrix = pairs[:, HEAD_SIZE:].astype(jnp.bfloat16)
    return jnp.concatenate(
        [query_matrix.reshape(row_count, heads_dev * HEAD_SIZE), key_matrix, value_matrix], axis=1
    )


def attend(soft_state, query_matrix, query_pos, key_matrix, value_matrix, key_pos, valid_keys):
    best_score, weight_sum, weighted = soft_state
    logit_scores = jnp.einsum(
        "rzsm,rvm->rzsv", query_matrix, key_matrix, preferred_element_type=jnp.float32
    ) * HEAD_SIZE ** (-0.5)
    allowed = (key_pos[None, :] <= query_pos[:, None])[None, None] & valid_keys[:, None, None, :]
    logit_scores = jnp.where(allowed, logit_scores, NEG)
    new_best = jnp.maximum(best_score, jnp.max(logit_scores, axis=-1))
    weights = jnp.where(allowed, jnp.exp(logit_scores - new_best[..., None]), 0.0)
    weight_sum = jnp.sum(weights, axis=-1)
    weighted = jnp.einsum(
        "awlp,ape->awle",
        weights.astype(jnp.bfloat16),
        value_matrix,
        preferred_element_type=jnp.float32,
    )
    return (new_best, weight_sum, weighted)


def per_device(states, short_lengths, attn_gain, wq, wkv, wo, mlp_gain, w_gate, w_up, w_down):
    n_ctx = lax.axis_size("ctx")
    n_tp = lax.axis_size("tp")
    ctx_rank = lax.axis_index("ctx")
    tp_index = lax.axis_index("tp")
    tok_rows = states.shape[0]
    rank_rows = tok_rows * n_tp
    n_blocks = 2 * n_ctx
    block_len = LLEN // n_blocks
    long_rows = LONG * 2 * block_len
    heads_dev = wq.shape[1] // HEAD_SIZE
    q_cols = heads_dev * HEAD_SIZE
    pair_width = 2 * HEAD_SIZE
    cache_cols = KVH * pair_width // n_tp
    kv_group = tp_index * KVH // n_tp
    wkv_head = lax.dynamic_slice_in_dim(wkv, kv_group * pair_width, pair_width, 1)
    first_col = tp_index * cache_cols - kv_group * pair_width
    positions = rank_positions(ctx_rank, rank_rows, block_len, long_rows, n_blocks)
    packed = project(
        [tp_all_gather(piece) for piece in column_chunks(rms_scale(states, attn_gain))],
        positions,
        wq,
        wkv_head,
        heads_dev,
    )
    query_matrix = packed[:, :q_cols].reshape(rank_rows, heads_dev, HEAD_SIZE)
    key_matrix = packed[:, q_cols : q_cols + HEAD_SIZE]
    value_matrix = packed[:, q_cols + HEAD_SIZE :]
    long_q = (
        query_matrix[:long_rows]
        .reshape(LONG, 2 * block_len, heads_dev, HEAD_SIZE)
        .transpose(0, 2, 1, 3)
    )
    long_k = key_matrix[:long_rows].reshape(LONG, 2, 1, block_len, HEAD_SIZE)
    long_v = value_matrix[:long_rows].reshape(LONG, 2, 1, block_len, HEAD_SIZE)
    long_qpos = positions[: 2 * block_len]
    half_pick = jnp.arange(2, dtype=jnp.int32)[:, None, None]
    long_init = (
        jnp.full((LONG, heads_dev, 2 * block_len), NEG, jnp.float32),
        jnp.zeros((LONG, heads_dev, 2 * block_len), jnp.float32),
        jnp.zeros((LONG, heads_dev, 2 * block_len, HEAD_SIZE), jnp.float32),
        jnp.zeros((LONG, 2, block_len, cache_cols), jnp.float32),
    )
    gathered = ctx_all_gather(jnp.stack([long_k[:, :, 0], long_v[:, :, 0]]))
    piece_k = jnp.moveaxis(gathered[:, 0], 0, 2)
    piece_v = jnp.moveaxis(gathered[:, 1], 0, 2)
    piece_blocks = piece_k.shape[2]
    block_ids = (ctx_rank + jnp.arange(piece_blocks, dtype=jnp.int32)) % n_ctx
    held_blocks = jnp.stack([block_ids, n_blocks - 1 - block_ids])
    key_pos = (
        held_blocks[:, :, None] * block_len + jnp.arange(block_len, dtype=jnp.int32)
    ).reshape(-1)
    key_count = 2 * piece_blocks * block_len
    flat_k = piece_k.reshape(LONG, key_count, HEAD_SIZE)
    flat_v = piece_v.reshape(LONG, key_count, HEAD_SIZE)
    all_valid = jnp.ones((LONG, key_count), dtype=bool)
    soft_state = long_init[:3]
    soft_state = attend(soft_state, long_q, long_qpos, flat_k, flat_v, key_pos, all_valid)
    joined = jnp.concatenate([piece_k, piece_v], axis=-1)
    own_cols = lax.dynamic_slice_in_dim(joined, first_col, cache_cols, 4)
    selector = ((held_blocks[None] // 2 == ctx_rank) & (held_blocks[None] % 2 == half_pick)).astype(
        jnp.bfloat16
    )
    cache_rows = jnp.einsum(
        "ehj,phjbc->pebc", selector, own_cols, preferred_element_type=jnp.float32
    )
    folded = soft_state + (cache_rows,)
    long_out = (
        (folded[2] / folded[1][..., None])
        .astype(jnp.bfloat16)
        .transpose(0, 2, 1, 3)
        .reshape(long_rows, q_cols)
    )
    long_cache = folded[3].astype(jnp.bfloat16).reshape(LONG, 2 * block_len, cache_cols)
    short_count = short_lengths.shape[0]
    short_q = (
        query_matrix[long_rows:]
        .reshape(short_count, SLEN, heads_dev, HEAD_SIZE)
        .transpose(0, 2, 1, 3)
    )
    short_k = key_matrix[long_rows:].reshape(short_count, SLEN, HEAD_SIZE)
    short_v = value_matrix[long_rows:].reshape(short_count, SLEN, HEAD_SIZE)
    offsets = jnp.arange(SLEN, dtype=jnp.int32)
    short_valid = offsets[None, :] < short_lengths[:, None]
    short_init = (
        jnp.full((short_count, heads_dev, SLEN), NEG, jnp.float32),
        jnp.zeros((short_count, heads_dev, SLEN), jnp.float32),
        jnp.zeros((short_count, heads_dev, SLEN, HEAD_SIZE), jnp.float32),
    )
    short_state = attend(short_init, short_q, offsets, short_k, short_v, offsets, short_valid)
    short_out = (
        (short_state[2] / short_state[1][..., None])
        .astype(jnp.bfloat16)
        .transpose(0, 2, 1, 3)
        .reshape(short_count * SLEN, q_cols)
    )
    short_cache = lax.dynamic_slice_in_dim(
        jnp.concatenate([short_k, short_v], axis=-1), first_col, cache_cols, 2
    )
    attn = jnp.concatenate([long_out, short_out], axis=0)
    mixed = jnp.concatenate(
        [
            tp_reduce_scatter(jnp.dot(attn, part, preferred_element_type=jnp.float32).astype(jnp.bfloat16))
            for part in column_chunks(wo)
        ],
        axis=1,
    )
    residual = (states.astype(jnp.float32) + mixed).astype(jnp.bfloat16)
    pieces = [tp_all_gather(piece, placed=False) for piece in column_chunks(rms_scale(residual, mlp_gain))]
    gate = split_dot(pieces, w_gate)
    up_part = split_dot(pieces, w_up)
    hidden = (jax.nn.silu(gate) * up_part).astype(jnp.bfloat16)
    down = jnp.concatenate(
        [
            tp_reduce_scatter_relative(
                jnp.dot(hidden, part, preferred_element_type=jnp.float32).astype(jnp.bfloat16)
            )
            for part in column_chunks(w_down)
        ],
        axis=1,
    )
    updated = (residual.astype(jnp.float32) + down).astype(jnp.bfloat16)
    return (updated, long_cache, short_cache)


def solution(mesh):
    in_specs = (
        P(("ctx", "tp"), None),
        P("ctx"),
        P(),
        P(None, "tp"),
        P(),
        P("tp", None),
        P(),
        P(None, "tp"),
        P(None, "tp"),
        P("tp", None),
    )
    out_specs = (P(("ctx", "tp"), None), P(None, "ctx", "tp"), P("ctx", None, "tp"))
    return jax.shard_map(
        per_device, mesh=mesh, in_specs=in_specs, out_specs=out_specs, check_vma=False
    )
```

```python
import jax
import jax.numpy as jnp
from jax import lax
from jax.sharding import PartitionSpec as P

KVH = 4
HEAD_SIZE = 64
LONG = 2
LLEN = 2048
SLEN = 64


EPS = 1e-05
THETA = 10000.0
NEG = -1e30


def rms_scale(matrix, gain):
    entries = matrix.astype(jnp.float32)
    power = jnp.mean(entries * entries, axis=-1, keepdims=True)
    return (entries * lax.rsqrt(power + EPS) * gain).astype(jnp.bfloat16)


def rotate(entries, positions):
    half_width = entries.shape[-1] // 2
    frequency = THETA ** (-jnp.arange(half_width, dtype=jnp.float32) * 2.0 / entries.shape[-1])
    angles = positions.astype(jnp.float32)[:, None] * frequency[None, :]
    cosine = jnp.cos(angles)[:, None, :]
    sine_wave = jnp.sin(angles)[:, None, :]
    first_half = entries[..., :half_width]
    second_half = entries[..., half_width:]
    return jnp.concatenate(
        [
            first_half * cosine - second_half * sine_wave,
            second_half * cosine + first_half * sine_wave,
        ],
        axis=-1,
    )


def rank_positions(ctx_rank, rank_rows, block_len, long_rows, n_blocks):
    index_row = jnp.arange(rank_rows, dtype=jnp.int32)
    half_index = index_row // block_len % 2
    offset_row = index_row % block_len
    which_block = jnp.where(half_index == 0, ctx_rank, n_blocks - 1 - ctx_rank)
    long_pos = which_block * block_len + offset_row
    short_pos = (index_row - long_rows) % SLEN
    return jnp.where(index_row < long_rows, long_pos, short_pos)


TP_DIMS = ((4, 8), (4, 2), (2, 1))


def shift_perm(n, stride, d, total):
    return [(t, t + (((t // stride) % n + d) % n - (t // stride) % n) * stride) for t in range(total)]


def scatter_stage(x, axis, n, stride, total):
    me = (lax.axis_index("tp") // stride) % n
    acc = lax.dynamic_index_in_dim(x, me, axis, keepdims=False).astype(jnp.float32)
    for d in range(1, n):
        part = lax.dynamic_index_in_dim(x, (me + d) % n, axis, keepdims=False)
        got = lax.ppermute(part.astype(jnp.bfloat16), "tp", shift_perm(n, stride, d, total))
        acc = acc + got.astype(jnp.float32)
    return acc


def tp_reduce_scatter(x):
    total = lax.axis_size("tp")
    rows, width = x.shape
    sizes = [n for n, _ in TP_DIMS]
    x = x.reshape(tuple(sizes) + (rows // total, width))
    for axis in reversed(range(len(TP_DIMS))):
        n, stride = TP_DIMS[axis]
        x = scatter_stage(x, axis, n, stride, total)
    return x


def gather_stage(x, axis, n, stride, total, placed):
    parts = [x] + [
        lax.ppermute(x, "tp", shift_perm(n, stride, (n - k) % n, total)) for k in range(1, n)
    ]
    if not placed:
        return jnp.stack(parts, axis=axis)
    me = (lax.axis_index("tp") // stride) % n
    out = jnp.zeros(x.shape[:axis] + (n,) + x.shape[axis:], x.dtype)
    for k, part in enumerate(parts):
        out = lax.dynamic_update_index_in_dim(out, part, (me + k) % n, axis)
    return out


def tp_all_gather(x, placed=True):
    total = lax.axis_size("tp")
    rows, width = x.shape
    for axis, (n, stride) in enumerate(TP_DIMS):
        x = gather_stage(x, axis, n, stride, total, placed)
    return x.reshape(rows * total, width)


def relative_scatter_stage(x, axis, n, stride, total):
    acc = lax.index_in_dim(x, 0, axis, keepdims=False).astype(jnp.float32)
    for d in range(1, n):
        part = lax.index_in_dim(x, d, axis, keepdims=False)
        got = lax.ppermute(part.astype(jnp.bfloat16), "tp", shift_perm(n, stride, d, total))
        acc = acc + got.astype(jnp.float32)
    return acc


def tp_reduce_scatter_relative(x):
    total = lax.axis_size("tp")
    rows, width = x.shape
    sizes = [n for n, _ in TP_DIMS]
    x = x.reshape(tuple(sizes) + (rows // total, width))
    for axis in reversed(range(len(TP_DIMS))):
        n, stride = TP_DIMS[axis]
        x = relative_scatter_stage(x, axis, n, stride, total)
    return x


def ctx_all_gather(x):
    n = lax.axis_size("ctx")
    parts = [x] + [
        lax.ppermute(x, "ctx", [(j, (j - k) % n) for j in range(n)]) for k in range(1, n)
    ]
    return parts


CHUNKS = 2


def column_chunks(matrix, axis=1, count=CHUNKS):
    width = matrix.shape[axis] // count
    return [lax.slice_in_dim(matrix, i * width, (i + 1) * width, axis=axis) for i in range(count)]


def split_dot(pieces, weight):
    parts = column_chunks(weight, axis=0, count=len(pieces))
    total = jnp.dot(pieces[0], parts[0], preferred_element_type=jnp.float32)
    for piece, part in zip(pieces[1:], parts[1:]):
        total = total + jnp.dot(piece, part, preferred_element_type=jnp.float32)
    return total


def project(pieces, positions, wq, wkv_head, heads_dev):
    row_count = pieces[0].shape[0]
    query_matrix = split_dot(pieces, wq).reshape(row_count, heads_dev, HEAD_SIZE)
    query_matrix = rotate(query_matrix, positions).astype(jnp.bfloat16)
    pairs = split_dot(pieces, wkv_head)
    key_matrix = rotate(pairs[:, None, :HEAD_SIZE], positions).astype(jnp.bfloat16)[:, 0]
    value_matrix = pairs[:, HEAD_SIZE:].astype(jnp.bfloat16)
    return jnp.concatenate(
        [query_matrix.reshape(row_count, heads_dev * HEAD_SIZE), key_matrix, value_matrix], axis=1
    )


def attend(soft_state, query_matrix, query_pos, key_matrix, value_matrix, key_pos, valid_keys):
    best_score, weight_sum, weighted = soft_state
    logit_scores = jnp.einsum(
        "rzsm,rvm->rzsv", query_matrix, key_matrix, preferred_element_type=jnp.float32
    ) * HEAD_SIZE ** (-0.5)
    allowed = (key_pos[None, :] <= query_pos[:, None])[None, None] & valid_keys[:, None, None, :]
    logit_scores = jnp.where(allowed, logit_scores, NEG)
    new_best = jnp.maximum(best_score, jnp.max(logit_scores, axis=-1))
    weights = jnp.where(allowed, jnp.exp(logit_scores - new_best[..., None]), 0.0)
    weight_sum = jnp.sum(weights, axis=-1)
    weighted = jnp.einsum(
        "awlp,ape->awle",
        weights.astype(jnp.bfloat16),
        value_matrix,
        preferred_element_type=jnp.float32,
    )
    return (new_best, weight_sum, weighted)


def per_device(states, short_lengths, attn_gain, wq, wkv, wo, mlp_gain, w_gate, w_up, w_down):
    n_ctx = lax.axis_size("ctx")
    n_tp = lax.axis_size("tp")
    ctx_rank = lax.axis_index("ctx")
    tp_index = lax.axis_index("tp")
    tok_rows = states.shape[0]
    rank_rows = tok_rows * n_tp
    n_blocks = 2 * n_ctx
    block_len = LLEN // n_blocks
    long_rows = LONG * 2 * block_len
    heads_dev = wq.shape[1] // HEAD_SIZE
    q_cols = heads_dev * HEAD_SIZE
    pair_width = 2 * HEAD_SIZE
    cache_cols = KVH * pair_width // n_tp
    kv_group = tp_index * KVH // n_tp
    wkv_head = lax.dynamic_slice_in_dim(wkv, kv_group * pair_width, pair_width, 1)
    first_col = tp_index * cache_cols - kv_group * pair_width
    positions = rank_positions(ctx_rank, rank_rows, block_len, long_rows, n_blocks)
    packed = project(
        [tp_all_gather(rms_scale(states, attn_gain))],
        positions,
        wq,
        wkv_head,
        heads_dev,
    )
    query_matrix = packed[:, :q_cols].reshape(rank_rows, heads_dev, HEAD_SIZE)
    key_matrix = packed[:, q_cols : q_cols + HEAD_SIZE]
    value_matrix = packed[:, q_cols + HEAD_SIZE :]
    long_q = (
        query_matrix[:long_rows]
        .reshape(LONG, 2 * block_len, heads_dev, HEAD_SIZE)
        .transpose(0, 2, 1, 3)
    )
    long_k = key_matrix[:long_rows].reshape(LONG, 2, 1, block_len, HEAD_SIZE)
    long_v = value_matrix[:long_rows].reshape(LONG, 2, 1, block_len, HEAD_SIZE)
    long_qpos = positions[: 2 * block_len]
    half_pick = jnp.arange(2, dtype=jnp.int32)[:, None, None]
    long_init = (
        jnp.full((LONG, heads_dev, 2 * block_len), NEG, jnp.float32),
        jnp.zeros((LONG, heads_dev, 2 * block_len), jnp.float32),
        jnp.zeros((LONG, heads_dev, 2 * block_len, HEAD_SIZE), jnp.float32),
        jnp.zeros((LONG, 2, block_len, cache_cols), jnp.float32),
    )
    parts = ctx_all_gather(jnp.concatenate([long_k[:, :, 0], long_v[:, :, 0]], axis=-1))
    piece_blocks = len(parts)
    block_ids = (ctx_rank + jnp.arange(piece_blocks, dtype=jnp.int32)) % n_ctx
    held_blocks = jnp.stack([block_ids, n_blocks - 1 - block_ids], axis=1)
    key_pos = (
        held_blocks[:, :, None] * block_len + jnp.arange(block_len, dtype=jnp.int32)
    ).reshape(-1)
    key_count = 2 * piece_blocks * block_len
    flat_kv = jnp.concatenate(
        [part.reshape(LONG, 2 * block_len, pair_width) for part in parts], axis=1
    )
    flat_k = flat_kv[..., :HEAD_SIZE]
    flat_v = flat_kv[..., HEAD_SIZE:]
    all_valid = jnp.ones((LONG, key_count), dtype=bool)
    soft_state = long_init[:3]
    soft_state = attend(soft_state, long_q, long_qpos, flat_k, flat_v, key_pos, all_valid)
    own_cols = lax.dynamic_slice_in_dim(flat_kv, first_col, cache_cols, 2).reshape(
        LONG, piece_blocks, 2, block_len, cache_cols
    )
    selector = ((held_blocks[None] // 2 == ctx_rank) & (held_blocks[None] % 2 == half_pick)).astype(
        jnp.bfloat16
    )
    cache_rows = jnp.einsum(
        "ejh,pjhbc->pebc", selector, own_cols, preferred_element_type=jnp.float32
    )
    folded = soft_state + (cache_rows,)
    long_out = (
        (folded[2] / folded[1][..., None])
        .astype(jnp.bfloat16)
        .transpose(0, 2, 1, 3)
        .reshape(long_rows, q_cols)
    )
    long_cache = folded[3].astype(jnp.bfloat16).reshape(LONG, 2 * block_len, cache_cols)
    short_count = short_lengths.shape[0]
    short_q = (
        query_matrix[long_rows:]
        .reshape(short_count, SLEN, heads_dev, HEAD_SIZE)
        .transpose(0, 2, 1, 3)
    )
    short_k = key_matrix[long_rows:].reshape(short_count, SLEN, HEAD_SIZE)
    short_v = value_matrix[long_rows:].reshape(short_count, SLEN, HEAD_SIZE)
    offsets = jnp.arange(SLEN, dtype=jnp.int32)
    short_valid = offsets[None, :] < short_lengths[:, None]
    short_init = (
        jnp.full((short_count, heads_dev, SLEN), NEG, jnp.float32),
        jnp.zeros((short_count, heads_dev, SLEN), jnp.float32),
        jnp.zeros((short_count, heads_dev, SLEN, HEAD_SIZE), jnp.float32),
    )
    short_state = attend(short_init, short_q, offsets, short_k, short_v, offsets, short_valid)
    short_out = (
        (short_state[2] / short_state[1][..., None])
        .astype(jnp.bfloat16)
        .transpose(0, 2, 1, 3)
        .reshape(short_count * SLEN, q_cols)
    )
    short_cache = lax.dynamic_slice_in_dim(
        jnp.concatenate([short_k, short_v], axis=-1), first_col, cache_cols, 2
    )
    attn = jnp.concatenate([long_out, short_out], axis=0)
    mixed = jnp.concatenate(
        [
            tp_reduce_scatter(jnp.dot(attn, part, preferred_element_type=jnp.float32).astype(jnp.bfloat16))
            for part in column_chunks(wo)
        ],
        axis=1,
    )
    residual = (states.astype(jnp.float32) + mixed).astype(jnp.bfloat16)
    pieces = [tp_all_gather(rms_scale(residual, mlp_gain), placed=False)]
    gate = split_dot(pieces, w_gate)
    up_part = split_dot(pieces, w_up)
    hidden = (jax.nn.silu(gate) * up_part).astype(jnp.bfloat16)
    down = jnp.concatenate(
        [
            tp_reduce_scatter_relative(
                jnp.dot(hidden, part, preferred_element_type=jnp.float32).astype(jnp.bfloat16)
            )
            for part in column_chunks(w_down)
        ],
        axis=1,
    )
    updated = (residual.astype(jnp.float32) + down).astype(jnp.bfloat16)
    return (updated, long_cache, short_cache)


def solution(mesh):
    in_specs = (
        P(("ctx", "tp"), None),
        P("ctx"),
        P(),
        P(None, "tp"),
        P(),
        P("tp", None),
        P(),
        P(None, "tp"),
        P(None, "tp"),
        P("tp", None),
    )
    out_specs = (P(("ctx", "tp"), None), P(None, "ctx", "tp"), P("ctx", None, "tp"))
    return jax.shard_map(
        per_device, mesh=mesh, in_specs=in_specs, out_specs=out_specs, check_vma=False
    )
```

```python
import jax
import jax.numpy as jnp
from jax import lax
from jax.sharding import PartitionSpec as P

KVH = 4
HEAD_SIZE = 64
LONG = 2
LLEN = 2048
SLEN = 64


EPS = 1e-05
THETA = 10000.0
NEG = -1e30


def rms_scale(matrix, gain):
    entries = matrix.astype(jnp.float32)
    power = jnp.mean(entries * entries, axis=-1, keepdims=True)
    return (entries * lax.rsqrt(power + EPS) * gain).astype(jnp.bfloat16)


def rotate(entries, positions):
    half_width = entries.shape[-1] // 2
    frequency = THETA ** (-jnp.arange(half_width, dtype=jnp.float32) * 2.0 / entries.shape[-1])
    angles = positions.astype(jnp.float32)[:, None] * frequency[None, :]
    cosine = jnp.cos(angles)[:, None, :]
    sine_wave = jnp.sin(angles)[:, None, :]
    first_half = entries[..., :half_width]
    second_half = entries[..., half_width:]
    return jnp.concatenate(
        [
            first_half * cosine - second_half * sine_wave,
            second_half * cosine + first_half * sine_wave,
        ],
        axis=-1,
    )


def rank_positions(ctx_rank, rank_rows, block_len, long_rows, n_blocks):
    index_row = jnp.arange(rank_rows, dtype=jnp.int32)
    half_index = index_row // block_len % 2
    offset_row = index_row % block_len
    which_block = jnp.where(half_index == 0, ctx_rank, n_blocks - 1 - ctx_rank)
    long_pos = which_block * block_len + offset_row
    short_pos = (index_row - long_rows) % SLEN
    return jnp.where(index_row < long_rows, long_pos, short_pos)


TP_DIMS = ((4, 8), (4, 2), (2, 1))


def shift_perm(n, stride, d, total):
    return [(t, t + (((t // stride) % n + d) % n - (t // stride) % n) * stride) for t in range(total)]


def exchange(x, n, stride, d, total):
    if n != 4 or stride != 2 or d != 2:
        return lax.ppermute(x, "tp", shift_perm(n, stride, d, total))
    half = x.shape[0] // 2
    ahead = lax.ppermute(x[:half], "tp", shift_perm(n, stride, d, total))
    back = shift_perm(n, stride, n - 1, total)
    around = lax.ppermute(lax.ppermute(x[half:], "tp", back), "tp", back)
    return jnp.concatenate([ahead, around], axis=0)


def scatter_stage(x, axis, n, stride, total):
    me = (lax.axis_index("tp") // stride) % n
    acc = lax.dynamic_index_in_dim(x, me, axis, keepdims=False).astype(jnp.float32)
    for d in range(1, n):
        part = lax.dynamic_index_in_dim(x, (me + d) % n, axis, keepdims=False)
        got = exchange(part.astype(jnp.bfloat16), n, stride, d, total)
        acc = acc + got.astype(jnp.float32)
    return acc


def tp_reduce_scatter(x):
    total = lax.axis_size("tp")
    rows, width = x.shape
    sizes = [n for n, _ in TP_DIMS]
    x = x.reshape(tuple(sizes) + (rows // total, width))
    for axis in reversed(range(len(TP_DIMS))):
        n, stride = TP_DIMS[axis]
        x = scatter_stage(x, axis, n, stride, total)
    return x


def gather_stage(x, axis, n, stride, total, placed):
    parts = [x] + [
        exchange(x, n, stride, (n - k) % n, total) for k in range(1, n)
    ]
    if not placed:
        return jnp.stack(parts, axis=axis)
    me = (lax.axis_index("tp") // stride) % n
    out = jnp.zeros(x.shape[:axis] + (n,) + x.shape[axis:], x.dtype)
    for k, part in enumerate(parts):
        out = lax.dynamic_update_index_in_dim(out, part, (me + k) % n, axis)
    return out


def tp_all_gather(x, placed=True):
    total = lax.axis_size("tp")
    rows, width = x.shape
    for axis, (n, stride) in enumerate(TP_DIMS):
        x = gather_stage(x, axis, n, stride, total, placed)
    return x.reshape(rows * total, width)


def relative_scatter_stage(x, axis, n, stride, total):
    acc = lax.index_in_dim(x, 0, axis, keepdims=False).astype(jnp.float32)
    for d in range(1, n):
        part = lax.index_in_dim(x, d, axis, keepdims=False)
        got = exchange(part.astype(jnp.bfloat16), n, stride, d, total)
        acc = acc + got.astype(jnp.float32)
    return acc


def tp_reduce_scatter_relative(x):
    total = lax.axis_size("tp")
    rows, width = x.shape
    sizes = [n for n, _ in TP_DIMS]
    x = x.reshape(tuple(sizes) + (rows // total, width))
    for axis in reversed(range(len(TP_DIMS))):
        n, stride = TP_DIMS[axis]
        x = relative_scatter_stage(x, axis, n, stride, total)
    return x


def ctx_all_gather(x):
    n = lax.axis_size("ctx")
    parts = [x] + [
        lax.ppermute(x, "ctx", [(j, (j - k) % n) for j in range(n)]) for k in range(1, n)
    ]
    return parts


CHUNKS = 2


def column_chunks(matrix, axis=1, count=CHUNKS):
    width = matrix.shape[axis] // count
    return [lax.slice_in_dim(matrix, i * width, (i + 1) * width, axis=axis) for i in range(count)]


def split_dot(pieces, weight):
    parts = column_chunks(weight, axis=0, count=len(pieces))
    total = jnp.dot(pieces[0], parts[0], preferred_element_type=jnp.float32)
    for piece, part in zip(pieces[1:], parts[1:]):
        total = total + jnp.dot(piece, part, preferred_element_type=jnp.float32)
    return total


def project(pieces, positions, wq, wkv_head, heads_dev):
    row_count = pieces[0].shape[0]
    query_matrix = split_dot(pieces, wq).reshape(row_count, heads_dev, HEAD_SIZE)
    query_matrix = rotate(query_matrix, positions).astype(jnp.bfloat16)
    pairs = split_dot(pieces, wkv_head)
    key_matrix = rotate(pairs[:, None, :HEAD_SIZE], positions).astype(jnp.bfloat16)[:, 0]
    value_matrix = pairs[:, HEAD_SIZE:].astype(jnp.bfloat16)
    return jnp.concatenate(
        [query_matrix.reshape(row_count, heads_dev * HEAD_SIZE), key_matrix, value_matrix], axis=1
    )


def attend(soft_state, query_matrix, query_pos, key_matrix, value_matrix, key_pos, valid_keys):
    best_score, weight_sum, weighted = soft_state
    logit_scores = jnp.einsum(
        "rzsm,rvm->rzsv", query_matrix, key_matrix, preferred_element_type=jnp.float32
    ) * HEAD_SIZE ** (-0.5)
    allowed = (key_pos[None, :] <= query_pos[:, None])[None, None] & valid_keys[:, None, None, :]
    logit_scores = jnp.where(allowed, logit_scores, NEG)
    new_best = jnp.maximum(best_score, jnp.max(logit_scores, axis=-1))
    weights = jnp.where(allowed, jnp.exp(logit_scores - new_best[..., None]), 0.0)
    weight_sum = jnp.sum(weights, axis=-1)
    weighted = jnp.einsum(
        "awlp,ape->awle",
        weights.astype(jnp.bfloat16),
        value_matrix,
        preferred_element_type=jnp.float32,
    )
    return (new_best, weight_sum, weighted)


def per_device(states, short_lengths, attn_gain, wq, wkv, wo, mlp_gain, w_gate, w_up, w_down):
    n_ctx = lax.axis_size("ctx")
    n_tp = lax.axis_size("tp")
    ctx_rank = lax.axis_index("ctx")
    tp_index = lax.axis_index("tp")
    tok_rows = states.shape[0]
    rank_rows = tok_rows * n_tp
    n_blocks = 2 * n_ctx
    block_len = LLEN // n_blocks
    long_rows = LONG * 2 * block_len
    heads_dev = wq.shape[1] // HEAD_SIZE
    q_cols = heads_dev * HEAD_SIZE
    pair_width = 2 * HEAD_SIZE
    cache_cols = KVH * pair_width // n_tp
    kv_group = tp_index * KVH // n_tp
    wkv_head = lax.dynamic_slice_in_dim(wkv, kv_group * pair_width, pair_width, 1)
    first_col = tp_index * cache_cols - kv_group * pair_width
    positions = rank_positions(ctx_rank, rank_rows, block_len, long_rows, n_blocks)
    packed = project(
        [tp_all_gather(rms_scale(states, attn_gain))],
        positions,
        wq,
        wkv_head,
        heads_dev,
    )
    query_matrix = packed[:, :q_cols].reshape(rank_rows, heads_dev, HEAD_SIZE)
    key_matrix = packed[:, q_cols : q_cols + HEAD_SIZE]
    value_matrix = packed[:, q_cols + HEAD_SIZE :]
    long_q = (
        query_matrix[:long_rows]
        .reshape(LONG, 2 * block_len, heads_dev, HEAD_SIZE)
        .transpose(0, 2, 1, 3)
    )
    long_k = key_matrix[:long_rows].reshape(LONG, 2, 1, block_len, HEAD_SIZE)
    long_v = value_matrix[:long_rows].reshape(LONG, 2, 1, block_len, HEAD_SIZE)
    long_qpos = positions[: 2 * block_len]
    half_pick = jnp.arange(2, dtype=jnp.int32)[:, None, None]
    long_init = (
        jnp.full((LONG, heads_dev, 2 * block_len), NEG, jnp.float32),
        jnp.zeros((LONG, heads_dev, 2 * block_len), jnp.float32),
        jnp.zeros((LONG, heads_dev, 2 * block_len, HEAD_SIZE), jnp.float32),
        jnp.zeros((LONG, 2, block_len, cache_cols), jnp.float32),
    )
    parts = ctx_all_gather(jnp.concatenate([long_k[:, :, 0], long_v[:, :, 0]], axis=-1))
    piece_blocks = len(parts)
    block_ids = (ctx_rank + jnp.arange(piece_blocks, dtype=jnp.int32)) % n_ctx
    held_blocks = jnp.stack([block_ids, n_blocks - 1 - block_ids], axis=1)
    key_pos = (
        held_blocks[:, :, None] * block_len + jnp.arange(block_len, dtype=jnp.int32)
    ).reshape(-1)
    key_count = 2 * piece_blocks * block_len
    flat_kv = jnp.concatenate(
        [part.reshape(LONG, 2 * block_len, pair_width) for part in parts], axis=1
    )
    flat_k = flat_kv[..., :HEAD_SIZE]
    flat_v = flat_kv[..., HEAD_SIZE:]
    all_valid = jnp.ones((LONG, key_count), dtype=bool)
    soft_state = long_init[:3]
    soft_state = attend(soft_state, long_q, long_qpos, flat_k, flat_v, key_pos, all_valid)
    own_cols = lax.dynamic_slice_in_dim(flat_kv, first_col, cache_cols, 2).reshape(
        LONG, piece_blocks, 2, block_len, cache_cols
    )
    selector = ((held_blocks[None] // 2 == ctx_rank) & (held_blocks[None] % 2 == half_pick)).astype(
        jnp.bfloat16
    )
    cache_rows = jnp.einsum(
        "ejh,pjhbc->pebc", selector, own_cols, preferred_element_type=jnp.float32
    )
    folded = soft_state + (cache_rows,)
    long_out = (
        (folded[2] / folded[1][..., None])
        .astype(jnp.bfloat16)
        .transpose(0, 2, 1, 3)
        .reshape(long_rows, q_cols)
    )
    long_cache = folded[3].astype(jnp.bfloat16).reshape(LONG, 2 * block_len, cache_cols)
    short_count = short_lengths.shape[0]
    short_q = (
        query_matrix[long_rows:]
        .reshape(short_count, SLEN, heads_dev, HEAD_SIZE)
        .transpose(0, 2, 1, 3)
    )
    short_k = key_matrix[long_rows:].reshape(short_count, SLEN, HEAD_SIZE)
    short_v = value_matrix[long_rows:].reshape(short_count, SLEN, HEAD_SIZE)
    offsets = jnp.arange(SLEN, dtype=jnp.int32)
    short_valid = offsets[None, :] < short_lengths[:, None]
    short_init = (
        jnp.full((short_count, heads_dev, SLEN), NEG, jnp.float32),
        jnp.zeros((short_count, heads_dev, SLEN), jnp.float32),
        jnp.zeros((short_count, heads_dev, SLEN, HEAD_SIZE), jnp.float32),
    )
    short_state = attend(short_init, short_q, offsets, short_k, short_v, offsets, short_valid)
    short_out = (
        (short_state[2] / short_state[1][..., None])
        .astype(jnp.bfloat16)
        .transpose(0, 2, 1, 3)
        .reshape(short_count * SLEN, q_cols)
    )
    short_cache = lax.dynamic_slice_in_dim(
        jnp.concatenate([short_k, short_v], axis=-1), first_col, cache_cols, 2
    )
    attn = jnp.concatenate([long_out, short_out], axis=0)
    mixed = jnp.concatenate(
        [
            tp_reduce_scatter(jnp.dot(attn, part, preferred_element_type=jnp.float32).astype(jnp.bfloat16))
            for part in column_chunks(wo)
        ],
        axis=1,
    )
    residual = (states.astype(jnp.float32) + mixed).astype(jnp.bfloat16)
    pieces = [tp_all_gather(rms_scale(residual, mlp_gain), placed=False)]
    gate = split_dot(pieces, w_gate)
    up_part = split_dot(pieces, w_up)
    hidden = (jax.nn.silu(gate) * up_part).astype(jnp.bfloat16)
    down = jnp.concatenate(
        [
            tp_reduce_scatter_relative(
                jnp.dot(hidden, part, preferred_element_type=jnp.float32).astype(jnp.bfloat16)
            )
            for part in column_chunks(w_down)
        ],
        axis=1,
    )
    updated = (residual.astype(jnp.float32) + down).astype(jnp.bfloat16)
    return (updated, long_cache, short_cache)


def solution(mesh):
    in_specs = (
        P(("ctx", "tp"), None),
        P("ctx"),
        P(),
        P(None, "tp"),
        P(),
        P("tp", None),
        P(),
        P(None, "tp"),
        P(None, "tp"),
        P("tp", None),
    )
    out_specs = (P(("ctx", "tp"), None), P(None, "ctx", "tp"), P("ctx", None, "tp"))
    return jax.shard_map(
        per_device, mesh=mesh, in_specs=in_specs, out_specs=out_specs, check_vma=False
    )
```

```python
import jax
import jax.numpy as jnp
from jax import lax
from jax.sharding import PartitionSpec as P

KVH = 4
HEAD_SIZE = 64
LONG = 2
LLEN = 2048
SLEN = 64


EPS = 1e-05
THETA = 10000.0
NEG = -1e30


def rms_scale(matrix, gain):
    entries = matrix.astype(jnp.float32)
    power = jnp.mean(entries * entries, axis=-1, keepdims=True)
    return (entries * lax.rsqrt(power + EPS) * gain).astype(jnp.bfloat16)


def rotate(entries, positions):
    half_width = entries.shape[-1] // 2
    frequency = THETA ** (-jnp.arange(half_width, dtype=jnp.float32) * 2.0 / entries.shape[-1])
    angles = positions.astype(jnp.float32)[:, None] * frequency[None, :]
    cosine = jnp.cos(angles)[:, None, :]
    sine_wave = jnp.sin(angles)[:, None, :]
    first_half = entries[..., :half_width]
    second_half = entries[..., half_width:]
    return jnp.concatenate(
        [
            first_half * cosine - second_half * sine_wave,
            second_half * cosine + first_half * sine_wave,
        ],
        axis=-1,
    )


def rank_positions(ctx_rank, rank_rows, block_len, long_rows, n_blocks):
    index_row = jnp.arange(rank_rows, dtype=jnp.int32)
    half_index = index_row // block_len % 2
    offset_row = index_row % block_len
    which_block = jnp.where(half_index == 0, ctx_rank, n_blocks - 1 - ctx_rank)
    long_pos = which_block * block_len + offset_row
    short_pos = (index_row - long_rows) % SLEN
    return jnp.where(index_row < long_rows, long_pos, short_pos)


TP_DIMS = ((4, 8), (4, 2), (2, 1))


def shift_perm(n, stride, d, total):
    return [(t, t + (((t // stride) % n + d) % n - (t // stride) % n) * stride) for t in range(total)]


def scatter_stage(x, axis, n, stride, total):
    me = (lax.axis_index("tp") // stride) % n
    acc = lax.dynamic_index_in_dim(x, me, axis, keepdims=False).astype(jnp.float32)
    for d in range(1, n):
        part = lax.dynamic_index_in_dim(x, (me + d) % n, axis, keepdims=False)
        got = lax.ppermute(part.astype(jnp.bfloat16), "tp", shift_perm(n, stride, d, total))
        acc = acc + got.astype(jnp.float32)
    return acc


def tp_reduce_scatter(x):
    total = lax.axis_size("tp")
    rows, width = x.shape
    sizes = [n for n, _ in TP_DIMS]
    x = x.reshape(tuple(sizes) + (rows // total, width))
    for axis in reversed(range(len(TP_DIMS))):
        n, stride = TP_DIMS[axis]
        x = scatter_stage(x, axis, n, stride, total)
    return x


def gather_stage(x, axis, n, stride, total, placed):
    parts = [x] + [
        lax.ppermute(x, "tp", shift_perm(n, stride, (n - k) % n, total)) for k in range(1, n)
    ]
    if not placed:
        return jnp.stack(parts, axis=axis)
    me = (lax.axis_index("tp") // stride) % n
    out = jnp.zeros(x.shape[:axis] + (n,) + x.shape[axis:], x.dtype)
    for k, part in enumerate(parts):
        out = lax.dynamic_update_index_in_dim(out, part, (me + k) % n, axis)
    return out


def tp_all_gather(x, placed=True):
    total = lax.axis_size("tp")
    rows, width = x.shape
    for axis, (n, stride) in enumerate(TP_DIMS):
        x = gather_stage(x, axis, n, stride, total, placed)
    return x.reshape(rows * total, width)


def relative_scatter_stage(x, axis, n, stride, total):
    acc = lax.index_in_dim(x, 0, axis, keepdims=False).astype(jnp.float32)
    for d in range(1, n):
        part = lax.index_in_dim(x, d, axis, keepdims=False)
        got = lax.ppermute(part.astype(jnp.bfloat16), "tp", shift_perm(n, stride, d, total))
        acc = acc + got.astype(jnp.float32)
    return acc


def tp_reduce_scatter_relative(x):
    total = lax.axis_size("tp")
    rows, width = x.shape
    sizes = [n for n, _ in TP_DIMS]
    x = x.reshape(tuple(sizes) + (rows // total, width))
    for axis in reversed(range(len(TP_DIMS))):
        n, stride = TP_DIMS[axis]
        x = relative_scatter_stage(x, axis, n, stride, total)
    return x


def ctx_all_gather(x):
    n = lax.axis_size("ctx")
    rings = n // 2
    both = jnp.stack([x, lax.ppermute(x, "ctx", shift_perm(2, 1, 1, n))])
    parts = [both] + [
        lax.ppermute(both, "ctx", shift_perm(rings, 2, (rings - k) % rings, n)) for k in range(1, rings)
    ]
    return [part[m] for part in parts for m in range(2)]


def ctx_sources(ctx_rank, n):
    slot = jnp.arange(n, dtype=jnp.int32)
    rings = n // 2
    return ((ctx_rank // 2 + slot // 2) % rings) * 2 + (ctx_rank + slot) % 2


CHUNKS = 2


def column_chunks(matrix, axis=1, count=CHUNKS):
    width = matrix.shape[axis] // count
    return [lax.slice_in_dim(matrix, i * width, (i + 1) * width, axis=axis) for i in range(count)]


def split_dot(pieces, weight):
    parts = column_chunks(weight, axis=0, count=len(pieces))
    total = jnp.dot(pieces[0], parts[0], preferred_element_type=jnp.float32)
    for piece, part in zip(pieces[1:], parts[1:]):
        total = total + jnp.dot(piece, part, preferred_element_type=jnp.float32)
    return total


def project(pieces, positions, wq, wkv_head, heads_dev):
    row_count = pieces[0].shape[0]
    query_matrix = split_dot(pieces, wq).reshape(row_count, heads_dev, HEAD_SIZE)
    query_matrix = rotate(query_matrix, positions).astype(jnp.bfloat16)
    pairs = split_dot(pieces, wkv_head)
    key_matrix = rotate(pairs[:, None, :HEAD_SIZE], positions).astype(jnp.bfloat16)[:, 0]
    value_matrix = pairs[:, HEAD_SIZE:].astype(jnp.bfloat16)
    return jnp.concatenate(
        [query_matrix.reshape(row_count, heads_dev * HEAD_SIZE), key_matrix, value_matrix], axis=1
    )


def attend(soft_state, query_matrix, query_pos, key_matrix, value_matrix, key_pos, valid_keys):
    best_score, weight_sum, weighted = soft_state
    logit_scores = jnp.einsum(
        "rzsm,rvm->rzsv", query_matrix, key_matrix, preferred_element_type=jnp.float32
    ) * HEAD_SIZE ** (-0.5)
    allowed = (key_pos[None, :] <= query_pos[:, None])[None, None] & valid_keys[:, None, None, :]
    logit_scores = jnp.where(allowed, logit_scores, NEG)
    new_best = jnp.maximum(best_score, jnp.max(logit_scores, axis=-1))
    weights = jnp.where(allowed, jnp.exp(logit_scores - new_best[..., None]), 0.0)
    weight_sum = jnp.sum(weights, axis=-1)
    weighted = jnp.einsum(
        "awlp,ape->awle",
        weights.astype(jnp.bfloat16),
        value_matrix,
        preferred_element_type=jnp.float32,
    )
    return (new_best, weight_sum, weighted)


def per_device(states, short_lengths, attn_gain, wq, wkv, wo, mlp_gain, w_gate, w_up, w_down):
    n_ctx = lax.axis_size("ctx")
    n_tp = lax.axis_size("tp")
    ctx_rank = lax.axis_index("ctx")
    tp_index = lax.axis_index("tp")
    tok_rows = states.shape[0]
    rank_rows = tok_rows * n_tp
    n_blocks = 2 * n_ctx
    block_len = LLEN // n_blocks
    long_rows = LONG * 2 * block_len
    heads_dev = wq.shape[1] // HEAD_SIZE
    q_cols = heads_dev * HEAD_SIZE
    pair_width = 2 * HEAD_SIZE
    cache_cols = KVH * pair_width // n_tp
    kv_group = tp_index * KVH // n_tp
    wkv_head = lax.dynamic_slice_in_dim(wkv, kv_group * pair_width, pair_width, 1)
    first_col = tp_index * cache_cols - kv_group * pair_width
    positions = rank_positions(ctx_rank, rank_rows, block_len, long_rows, n_blocks)
    packed = project(
        [tp_all_gather(rms_scale(states, attn_gain))],
        positions,
        wq,
        wkv_head,
        heads_dev,
    )
    query_matrix = packed[:, :q_cols].reshape(rank_rows, heads_dev, HEAD_SIZE)
    key_matrix = packed[:, q_cols : q_cols + HEAD_SIZE]
    value_matrix = packed[:, q_cols + HEAD_SIZE :]
    long_q = (
        query_matrix[:long_rows]
        .reshape(LONG, 2 * block_len, heads_dev, HEAD_SIZE)
        .transpose(0, 2, 1, 3)
    )
    long_k = key_matrix[:long_rows].reshape(LONG, 2, 1, block_len, HEAD_SIZE)
    long_v = value_matrix[:long_rows].reshape(LONG, 2, 1, block_len, HEAD_SIZE)
    long_qpos = positions[: 2 * block_len]
    half_pick = jnp.arange(2, dtype=jnp.int32)[:, None, None]
    long_init = (
        jnp.full((LONG, heads_dev, 2 * block_len), NEG, jnp.float32),
        jnp.zeros((LONG, heads_dev, 2 * block_len), jnp.float32),
        jnp.zeros((LONG, heads_dev, 2 * block_len, HEAD_SIZE), jnp.float32),
        jnp.zeros((LONG, 2, block_len, cache_cols), jnp.float32),
    )
    parts = ctx_all_gather(jnp.concatenate([long_k[:, :, 0], long_v[:, :, 0]], axis=-1))
    piece_blocks = len(parts)
    block_ids = ctx_sources(ctx_rank, n_ctx)
    held_blocks = jnp.stack([block_ids, n_blocks - 1 - block_ids], axis=1)
    key_pos = (
        held_blocks[:, :, None] * block_len + jnp.arange(block_len, dtype=jnp.int32)
    ).reshape(-1)
    key_count = 2 * piece_blocks * block_len
    flat_kv = jnp.concatenate(
        [part.reshape(LONG, 2 * block_len, pair_width) for part in parts], axis=1
    )
    flat_k = flat_kv[..., :HEAD_SIZE]
    flat_v = flat_kv[..., HEAD_SIZE:]
    all_valid = jnp.ones((LONG, key_count), dtype=bool)
    soft_state = long_init[:3]
    soft_state = attend(soft_state, long_q, long_qpos, flat_k, flat_v, key_pos, all_valid)
    own_cols = lax.dynamic_slice_in_dim(flat_kv, first_col, cache_cols, 2).reshape(
        LONG, piece_blocks, 2, block_len, cache_cols
    )
    selector = ((held_blocks[None] // 2 == ctx_rank) & (held_blocks[None] % 2 == half_pick)).astype(
        jnp.bfloat16
    )
    cache_rows = jnp.einsum(
        "ejh,pjhbc->pebc", selector, own_cols, preferred_element_type=jnp.float32
    )
    folded = soft_state + (cache_rows,)
    long_out = (
        (folded[2] / folded[1][..., None])
        .astype(jnp.bfloat16)
        .transpose(0, 2, 1, 3)
        .reshape(long_rows, q_cols)
    )
    long_cache = folded[3].astype(jnp.bfloat16).reshape(LONG, 2 * block_len, cache_cols)
    short_count = short_lengths.shape[0]
    short_q = (
        query_matrix[long_rows:]
        .reshape(short_count, SLEN, heads_dev, HEAD_SIZE)
        .transpose(0, 2, 1, 3)
    )
    short_k = key_matrix[long_rows:].reshape(short_count, SLEN, HEAD_SIZE)
    short_v = value_matrix[long_rows:].reshape(short_count, SLEN, HEAD_SIZE)
    offsets = jnp.arange(SLEN, dtype=jnp.int32)
    short_valid = offsets[None, :] < short_lengths[:, None]
    short_init = (
        jnp.full((short_count, heads_dev, SLEN), NEG, jnp.float32),
        jnp.zeros((short_count, heads_dev, SLEN), jnp.float32),
        jnp.zeros((short_count, heads_dev, SLEN, HEAD_SIZE), jnp.float32),
    )
    short_state = attend(short_init, short_q, offsets, short_k, short_v, offsets, short_valid)
    short_out = (
        (short_state[2] / short_state[1][..., None])
        .astype(jnp.bfloat16)
        .transpose(0, 2, 1, 3)
        .reshape(short_count * SLEN, q_cols)
    )
    short_cache = lax.dynamic_slice_in_dim(
        jnp.concatenate([short_k, short_v], axis=-1), first_col, cache_cols, 2
    )
    attn = jnp.concatenate([long_out, short_out], axis=0)
    mixed = jnp.concatenate(
        [
            tp_reduce_scatter(jnp.dot(attn, part, preferred_element_type=jnp.float32).astype(jnp.bfloat16))
            for part in column_chunks(wo)
        ],
        axis=1,
    )
    residual = (states.astype(jnp.float32) + mixed).astype(jnp.bfloat16)
    pieces = [tp_all_gather(rms_scale(residual, mlp_gain), placed=False)]
    gate = split_dot(pieces, w_gate)
    up_part = split_dot(pieces, w_up)
    hidden = (jax.nn.silu(gate) * up_part).astype(jnp.bfloat16)
    down = jnp.concatenate(
        [
            tp_reduce_scatter_relative(
                jnp.dot(hidden, part, preferred_element_type=jnp.float32).astype(jnp.bfloat16)
            )
            for part in column_chunks(w_down)
        ],
        axis=1,
    )
    updated = (residual.astype(jnp.float32) + down).astype(jnp.bfloat16)
    return (updated, long_cache, short_cache)


def solution(mesh):
    in_specs = (
        P(("ctx", "tp"), None),
        P("ctx"),
        P(),
        P(None, "tp"),
        P(),
        P("tp", None),
        P(),
        P(None, "tp"),
        P(None, "tp"),
        P("tp", None),
    )
    out_specs = (P(("ctx", "tp"), None), P(None, "ctx", "tp"), P("ctx", None, "tp"))
    return jax.shard_map(
        per_device, mesh=mesh, in_specs=in_specs, out_specs=out_specs, check_vma=False
    )
```

```python
import jax
import jax.numpy as jnp
from jax import lax
from jax.sharding import PartitionSpec as P

KVH = 4
HEAD_SIZE = 64
LONG = 2
LLEN = 2048
SLEN = 64


EPS = 1e-05
THETA = 10000.0
NEG = -1e30


def rms_scale(matrix, gain):
    entries = matrix.astype(jnp.float32)
    power = jnp.mean(entries * entries, axis=-1, keepdims=True)
    return (entries * lax.rsqrt(power + EPS) * gain).astype(jnp.bfloat16)


def rotate(entries, positions):
    half_width = entries.shape[-1] // 2
    frequency = THETA ** (-jnp.arange(half_width, dtype=jnp.float32) * 2.0 / entries.shape[-1])
    angles = positions.astype(jnp.float32)[:, None] * frequency[None, :]
    cosine = jnp.cos(angles)[:, None, :]
    sine_wave = jnp.sin(angles)[:, None, :]
    first_half = entries[..., :half_width]
    second_half = entries[..., half_width:]
    return jnp.concatenate(
        [
            first_half * cosine - second_half * sine_wave,
            second_half * cosine + first_half * sine_wave,
        ],
        axis=-1,
    )


def rank_positions(ctx_rank, rank_rows, block_len, long_rows, n_blocks):
    index_row = jnp.arange(rank_rows, dtype=jnp.int32)
    half_index = index_row // block_len % 2
    offset_row = index_row % block_len
    which_block = jnp.where(half_index == 0, ctx_rank, n_blocks - 1 - ctx_rank)
    long_pos = which_block * block_len + offset_row
    short_pos = (index_row - long_rows) % SLEN
    return jnp.where(index_row < long_rows, long_pos, short_pos)


TP_DIMS = ((4, 8), (4, 2), (2, 1))


def shift_perm(n, stride, d, total):
    return [(t, t + (((t // stride) % n + d) % n - (t // stride) % n) * stride) for t in range(total)]


def scatter_stage(x, axis, n, stride, total):
    me = (lax.axis_index("tp") // stride) % n
    acc = lax.dynamic_index_in_dim(x, me, axis, keepdims=False).astype(jnp.float32)
    for d in range(1, n):
        part = lax.dynamic_index_in_dim(x, (me + d) % n, axis, keepdims=False)
        got = lax.ppermute(part.astype(jnp.bfloat16), "tp", shift_perm(n, stride, d, total))
        acc = acc + got.astype(jnp.float32)
    return acc


def tp_reduce_scatter(x):
    total = lax.axis_size("tp")
    rows, width = x.shape
    sizes = [n for n, _ in TP_DIMS]
    x = x.reshape(tuple(sizes) + (rows // total, width))
    for axis in reversed(range(len(TP_DIMS))):
        n, stride = TP_DIMS[axis]
        x = scatter_stage(x, axis, n, stride, total)
    return x


def gather_stage(x, axis, n, stride, total, placed):
    parts = [x] + [
        lax.ppermute(x, "tp", shift_perm(n, stride, (n - k) % n, total)) for k in range(1, n)
    ]
    if not placed:
        return jnp.stack(parts, axis=axis)
    me = (lax.axis_index("tp") // stride) % n
    out = jnp.zeros(x.shape[:axis] + (n,) + x.shape[axis:], x.dtype)
    for k, part in enumerate(parts):
        out = lax.dynamic_update_index_in_dim(out, part, (me + k) % n, axis)
    return out


def plane_gather(x, placed):
    total = lax.axis_size("tp")
    (nz, sz), (ny, sy) = TP_DIMS[:2]

    def fetch(value, n, stride, k):
        return lax.ppermute(value, "tp", shift_perm(n, stride, (n - k) % n, total))

    far = jnp.stack([fetch(x, nz, sz, k) for k in range(1, nz)])
    near = [fetch(x, ny, sy, k) for k in range(1, ny)]
    rest = [fetch(far, ny, sy, k) for k in range(1, ny)]
    columns = [jnp.concatenate([x[None], far])] + [
        jnp.concatenate([own[None], other]) for own, other in zip(near, rest)
    ]
    if not placed:
        return jnp.stack(columns, axis=1)
    tp_index = lax.axis_index("tp")
    me_z, me_y = (tp_index // sz) % nz, (tp_index // sy) % ny
    out = jnp.zeros((nz, ny) + x.shape, x.dtype)
    for k, column in enumerate(columns):
        slot = jnp.zeros((nz,) + x.shape, x.dtype)
        for j in range(nz):
            slot = lax.dynamic_update_index_in_dim(slot, column[j], (me_z + j) % nz, 0)
        out = lax.dynamic_update_index_in_dim(out, slot, (me_y + k) % ny, 1)
    return out


def tp_all_gather(x, placed=True):
    total = lax.axis_size("tp")
    rows, width = x.shape
    x = plane_gather(x, placed)
    for axis, (n, stride) in enumerate(TP_DIMS):
        if axis >= 2:
            x = gather_stage(x, axis, n, stride, total, placed)
    return x.reshape(rows * total, width)


def relative_scatter_stage(x, axis, n, stride, total):
    acc = lax.index_in_dim(x, 0, axis, keepdims=False).astype(jnp.float32)
    for d in range(1, n):
        part = lax.index_in_dim(x, d, axis, keepdims=False)
        got = lax.ppermute(part.astype(jnp.bfloat16), "tp", shift_perm(n, stride, d, total))
        acc = acc + got.astype(jnp.float32)
    return acc


def tp_reduce_scatter_relative(x):
    total = lax.axis_size("tp")
    rows, width = x.shape
    sizes = [n for n, _ in TP_DIMS]
    x = x.reshape(tuple(sizes) + (rows // total, width))
    for axis in reversed(range(len(TP_DIMS))):
        n, stride = TP_DIMS[axis]
        x = relative_scatter_stage(x, axis, n, stride, total)
    return x


def ctx_all_gather(x):
    n = lax.axis_size("ctx")
    parts = [x] + [
        lax.ppermute(x, "ctx", [(j, (j - k) % n) for j in range(n)]) for k in range(1, n)
    ]
    return parts


CHUNKS = 2


def column_chunks(matrix, axis=1, count=CHUNKS):
    width = matrix.shape[axis] // count
    return [lax.slice_in_dim(matrix, i * width, (i + 1) * width, axis=axis) for i in range(count)]


def split_dot(pieces, weight):
    parts = column_chunks(weight, axis=0, count=len(pieces))
    total = jnp.dot(pieces[0], parts[0], preferred_element_type=jnp.float32)
    for piece, part in zip(pieces[1:], parts[1:]):
        total = total + jnp.dot(piece, part, preferred_element_type=jnp.float32)
    return total


def project(pieces, positions, wq, wkv_head, heads_dev):
    row_count = pieces[0].shape[0]
    query_matrix = split_dot(pieces, wq).reshape(row_count, heads_dev, HEAD_SIZE)
    query_matrix = rotate(query_matrix, positions).astype(jnp.bfloat16)
    pairs = split_dot(pieces, wkv_head)
    key_matrix = rotate(pairs[:, None, :HEAD_SIZE], positions).astype(jnp.bfloat16)[:, 0]
    value_matrix = pairs[:, HEAD_SIZE:].astype(jnp.bfloat16)
    return jnp.concatenate(
        [query_matrix.reshape(row_count, heads_dev * HEAD_SIZE), key_matrix, value_matrix], axis=1
    )


def attend(soft_state, query_matrix, query_pos, key_matrix, value_matrix, key_pos, valid_keys):
    best_score, weight_sum, weighted = soft_state
    logit_scores = jnp.einsum(
        "rzsm,rvm->rzsv", query_matrix, key_matrix, preferred_element_type=jnp.float32
    ) * HEAD_SIZE ** (-0.5)
    allowed = (key_pos[None, :] <= query_pos[:, None])[None, None] & valid_keys[:, None, None, :]
    logit_scores = jnp.where(allowed, logit_scores, NEG)
    new_best = jnp.maximum(best_score, jnp.max(logit_scores, axis=-1))
    weights = jnp.where(allowed, jnp.exp(logit_scores - new_best[..., None]), 0.0)
    weight_sum = jnp.sum(weights, axis=-1)
    weighted = jnp.einsum(
        "awlp,ape->awle",
        weights.astype(jnp.bfloat16),
        value_matrix,
        preferred_element_type=jnp.float32,
    )
    return (new_best, weight_sum, weighted)


def per_device(states, short_lengths, attn_gain, wq, wkv, wo, mlp_gain, w_gate, w_up, w_down):
    n_ctx = lax.axis_size("ctx")
    n_tp = lax.axis_size("tp")
    ctx_rank = lax.axis_index("ctx")
    tp_index = lax.axis_index("tp")
    tok_rows = states.shape[0]
    rank_rows = tok_rows * n_tp
    n_blocks = 2 * n_ctx
    block_len = LLEN // n_blocks
    long_rows = LONG * 2 * block_len
    heads_dev = wq.shape[1] // HEAD_SIZE
    q_cols = heads_dev * HEAD_SIZE
    pair_width = 2 * HEAD_SIZE
    cache_cols = KVH * pair_width // n_tp
    kv_group = tp_index * KVH // n_tp
    wkv_head = lax.dynamic_slice_in_dim(wkv, kv_group * pair_width, pair_width, 1)
    first_col = tp_index * cache_cols - kv_group * pair_width
    positions = rank_positions(ctx_rank, rank_rows, block_len, long_rows, n_blocks)
    packed = project(
        [tp_all_gather(rms_scale(states, attn_gain))],
        positions,
        wq,
        wkv_head,
        heads_dev,
    )
    query_matrix = packed[:, :q_cols].reshape(rank_rows, heads_dev, HEAD_SIZE)
    key_matrix = packed[:, q_cols : q_cols + HEAD_SIZE]
    value_matrix = packed[:, q_cols + HEAD_SIZE :]
    long_q = (
        query_matrix[:long_rows]
        .reshape(LONG, 2 * block_len, heads_dev, HEAD_SIZE)
        .transpose(0, 2, 1, 3)
    )
    long_k = key_matrix[:long_rows].reshape(LONG, 2, 1, block_len, HEAD_SIZE)
    long_v = value_matrix[:long_rows].reshape(LONG, 2, 1, block_len, HEAD_SIZE)
    long_qpos = positions[: 2 * block_len]
    half_pick = jnp.arange(2, dtype=jnp.int32)[:, None, None]
    long_init = (
        jnp.full((LONG, heads_dev, 2 * block_len), NEG, jnp.float32),
        jnp.zeros((LONG, heads_dev, 2 * block_len), jnp.float32),
        jnp.zeros((LONG, heads_dev, 2 * block_len, HEAD_SIZE), jnp.float32),
        jnp.zeros((LONG, 2, block_len, cache_cols), jnp.float32),
    )
    parts = ctx_all_gather(jnp.concatenate([long_k[:, :, 0], long_v[:, :, 0]], axis=-1))
    piece_blocks = len(parts)
    block_ids = (ctx_rank + jnp.arange(piece_blocks, dtype=jnp.int32)) % n_ctx
    held_blocks = jnp.stack([block_ids, n_blocks - 1 - block_ids], axis=1)
    key_pos = (
        held_blocks[:, :, None] * block_len + jnp.arange(block_len, dtype=jnp.int32)
    ).reshape(-1)
    key_count = 2 * piece_blocks * block_len
    flat_kv = jnp.concatenate(
        [part.reshape(LONG, 2 * block_len, pair_width) for part in parts], axis=1
    )
    flat_k = flat_kv[..., :HEAD_SIZE]
    flat_v = flat_kv[..., HEAD_SIZE:]
    all_valid = jnp.ones((LONG, key_count), dtype=bool)
    soft_state = long_init[:3]
    soft_state = attend(soft_state, long_q, long_qpos, flat_k, flat_v, key_pos, all_valid)
    own_cols = lax.dynamic_slice_in_dim(flat_kv, first_col, cache_cols, 2).reshape(
        LONG, piece_blocks, 2, block_len, cache_cols
    )
    selector = ((held_blocks[None] // 2 == ctx_rank) & (held_blocks[None] % 2 == half_pick)).astype(
        jnp.bfloat16
    )
    cache_rows = jnp.einsum(
        "ejh,pjhbc->pebc", selector, own_cols, preferred_element_type=jnp.float32
    )
    folded = soft_state + (cache_rows,)
    long_out = (
        (folded[2] / folded[1][..., None])
        .astype(jnp.bfloat16)
        .transpose(0, 2, 1, 3)
        .reshape(long_rows, q_cols)
    )
    long_cache = folded[3].astype(jnp.bfloat16).reshape(LONG, 2 * block_len, cache_cols)
    short_count = short_lengths.shape[0]
    short_q = (
        query_matrix[long_rows:]
        .reshape(short_count, SLEN, heads_dev, HEAD_SIZE)
        .transpose(0, 2, 1, 3)
    )
    short_k = key_matrix[long_rows:].reshape(short_count, SLEN, HEAD_SIZE)
    short_v = value_matrix[long_rows:].reshape(short_count, SLEN, HEAD_SIZE)
    offsets = jnp.arange(SLEN, dtype=jnp.int32)
    short_valid = offsets[None, :] < short_lengths[:, None]
    short_init = (
        jnp.full((short_count, heads_dev, SLEN), NEG, jnp.float32),
        jnp.zeros((short_count, heads_dev, SLEN), jnp.float32),
        jnp.zeros((short_count, heads_dev, SLEN, HEAD_SIZE), jnp.float32),
    )
    short_state = attend(short_init, short_q, offsets, short_k, short_v, offsets, short_valid)
    short_out = (
        (short_state[2] / short_state[1][..., None])
        .astype(jnp.bfloat16)
        .transpose(0, 2, 1, 3)
        .reshape(short_count * SLEN, q_cols)
    )
    short_cache = lax.dynamic_slice_in_dim(
        jnp.concatenate([short_k, short_v], axis=-1), first_col, cache_cols, 2
    )
    attn = jnp.concatenate([long_out, short_out], axis=0)
    mixed = jnp.concatenate(
        [
            tp_reduce_scatter(jnp.dot(attn, part, preferred_element_type=jnp.float32).astype(jnp.bfloat16))
            for part in column_chunks(wo)
        ],
        axis=1,
    )
    residual = (states.astype(jnp.float32) + mixed).astype(jnp.bfloat16)
    pieces = [tp_all_gather(rms_scale(residual, mlp_gain), placed=False)]
    gate = split_dot(pieces, w_gate)
    up_part = split_dot(pieces, w_up)
    hidden = (jax.nn.silu(gate) * up_part).astype(jnp.bfloat16)
    down = jnp.concatenate(
        [
            tp_reduce_scatter_relative(
                jnp.dot(hidden, part, preferred_element_type=jnp.float32).astype(jnp.bfloat16)
            )
            for part in column_chunks(w_down)
        ],
        axis=1,
    )
    updated = (residual.astype(jnp.float32) + down).astype(jnp.bfloat16)
    return (updated, long_cache, short_cache)


def solution(mesh):
    in_specs = (
        P(("ctx", "tp"), None),
        P("ctx"),
        P(),
        P(None, "tp"),
        P(),
        P("tp", None),
        P(),
        P(None, "tp"),
        P(None, "tp"),
        P("tp", None),
    )
    out_specs = (P(("ctx", "tp"), None), P(None, "ctx", "tp"), P("ctx", None, "tp"))
    return jax.shard_map(
        per_device, mesh=mesh, in_specs=in_specs, out_specs=out_specs, check_vma=False
    )
```

```python
import jax
import jax.numpy as jnp
from jax import lax
from jax.sharding import PartitionSpec as P

KVH = 4
HEAD_SIZE = 64
LONG = 2
LLEN = 2048
SLEN = 64


EPS = 1e-05
THETA = 10000.0
NEG = -1e30


def rms_scale(matrix, gain):
    entries = matrix.astype(jnp.float32)
    power = jnp.mean(entries * entries, axis=-1, keepdims=True)
    return (entries * lax.rsqrt(power + EPS) * gain).astype(jnp.bfloat16)


def rotate(entries, positions):
    half_width = entries.shape[-1] // 2
    frequency = THETA ** (-jnp.arange(half_width, dtype=jnp.float32) * 2.0 / entries.shape[-1])
    angles = positions.astype(jnp.float32)[:, None] * frequency[None, :]
    cosine = jnp.cos(angles)[:, None, :]
    sine_wave = jnp.sin(angles)[:, None, :]
    first_half = entries[..., :half_width]
    second_half = entries[..., half_width:]
    return jnp.concatenate(
        [
            first_half * cosine - second_half * sine_wave,
            second_half * cosine + first_half * sine_wave,
        ],
        axis=-1,
    )


def rank_positions(ctx_rank, rank_rows, block_len, long_rows, n_blocks):
    index_row = jnp.arange(rank_rows, dtype=jnp.int32)
    half_index = index_row // block_len % 2
    offset_row = index_row % block_len
    which_block = jnp.where(half_index == 0, ctx_rank, n_blocks - 1 - ctx_rank)
    long_pos = which_block * block_len + offset_row
    short_pos = (index_row - long_rows) % SLEN
    return jnp.where(index_row < long_rows, long_pos, short_pos)


TP_DIMS = ((4, 8), (4, 2), (2, 1))


def shift_perm(n, stride, d, total):
    return [(t, t + (((t // stride) % n + d) % n - (t // stride) % n) * stride) for t in range(total)]


def scatter_stage(x, axis, n, stride, total):
    me = (lax.axis_index("tp") // stride) % n
    acc = lax.dynamic_index_in_dim(x, me, axis, keepdims=False).astype(jnp.float32)
    for d in range(1, n):
        part = lax.dynamic_index_in_dim(x, (me + d) % n, axis, keepdims=False)
        got = lax.ppermute(part.astype(jnp.bfloat16), "tp", shift_perm(n, stride, d, total))
        acc = acc + got.astype(jnp.float32)
    return acc


def tp_reduce_scatter(x):
    total = lax.axis_size("tp")
    rows, width = x.shape
    sizes = [n for n, _ in TP_DIMS]
    x = x.reshape(tuple(sizes) + (rows // total, width))
    for axis in reversed(range(len(TP_DIMS))):
        n, stride = TP_DIMS[axis]
        x = scatter_stage(x, axis, n, stride, total)
    return x


def gather_stage(x, axis, n, stride, total, placed):
    parts = [x] + [
        lax.ppermute(x, "tp", shift_perm(n, stride, (n - k) % n, total)) for k in range(1, n)
    ]
    if not placed:
        return jnp.stack(parts, axis=axis)
    me = (lax.axis_index("tp") // stride) % n
    out = jnp.zeros(x.shape[:axis] + (n,) + x.shape[axis:], x.dtype)
    for k, part in enumerate(parts):
        out = lax.dynamic_update_index_in_dim(out, part, (me + k) % n, axis)
    return out


def plane_gather(x, placed):
    total = lax.axis_size("tp")
    (nz, sz), (ny, sy) = TP_DIMS[:2]

    def fetch(value, n, stride, k):
        return lax.ppermute(value, "tp", shift_perm(n, stride, (n - k) % n, total))

    far = jnp.stack([fetch(x, nz, sz, k) for k in range(1, nz)])
    near = [fetch(x, ny, sy, k) for k in range(1, ny)]
    rest = [fetch(far, ny, sy, k) for k in range(1, ny)]
    columns = [jnp.concatenate([x[None], far])] + [
        jnp.concatenate([own[None], other]) for own, other in zip(near, rest)
    ]
    if not placed:
        return jnp.stack(columns, axis=1)
    tp_index = lax.axis_index("tp")
    me_z, me_y = (tp_index // sz) % nz, (tp_index // sy) % ny
    out = jnp.zeros((nz, ny) + x.shape, x.dtype)
    for k, column in enumerate(columns):
        slot = jnp.zeros((nz,) + x.shape, x.dtype)
        for j in range(nz):
            slot = lax.dynamic_update_index_in_dim(slot, column[j], (me_z + j) % nz, 0)
        out = lax.dynamic_update_index_in_dim(out, slot, (me_y + k) % ny, 1)
    return out


def tp_all_gather(x, placed=True, overlap=False):
    total = lax.axis_size("tp")
    rows, width = x.shape
    if overlap:
        x = plane_gather(x, placed)
    for axis, (n, stride) in enumerate(TP_DIMS):
        if axis >= 2 or not overlap:
            x = gather_stage(x, axis, n, stride, total, placed)
    return x.reshape(rows * total, width)


def relative_scatter_stage(x, axis, n, stride, total):
    acc = lax.index_in_dim(x, 0, axis, keepdims=False).astype(jnp.float32)
    for d in range(1, n):
        part = lax.index_in_dim(x, d, axis, keepdims=False)
        got = lax.ppermute(part.astype(jnp.bfloat16), "tp", shift_perm(n, stride, d, total))
        acc = acc + got.astype(jnp.float32)
    return acc


def tp_reduce_scatter_relative(x):
    total = lax.axis_size("tp")
    rows, width = x.shape
    sizes = [n for n, _ in TP_DIMS]
    x = x.reshape(tuple(sizes) + (rows // total, width))
    for axis in reversed(range(len(TP_DIMS))):
        n, stride = TP_DIMS[axis]
        x = relative_scatter_stage(x, axis, n, stride, total)
    return x


def ctx_all_gather(x):
    n = lax.axis_size("ctx")
    parts = [x] + [
        lax.ppermute(x, "ctx", [(j, (j - k) % n) for j in range(n)]) for k in range(1, n)
    ]
    return parts


CHUNKS = 2


def column_chunks(matrix, axis=1, count=CHUNKS):
    width = matrix.shape[axis] // count
    return [lax.slice_in_dim(matrix, i * width, (i + 1) * width, axis=axis) for i in range(count)]


def split_dot(pieces, weight):
    parts = column_chunks(weight, axis=0, count=len(pieces))
    total = jnp.dot(pieces[0], parts[0], preferred_element_type=jnp.float32)
    for piece, part in zip(pieces[1:], parts[1:]):
        total = total + jnp.dot(piece, part, preferred_element_type=jnp.float32)
    return total


def project(pieces, positions, wq, wkv_head, heads_dev):
    row_count = pieces[0].shape[0]
    query_matrix = split_dot(pieces, wq).reshape(row_count, heads_dev, HEAD_SIZE)
    query_matrix = rotate(query_matrix, positions).astype(jnp.bfloat16)
    pairs = split_dot(pieces, wkv_head)
    key_matrix = rotate(pairs[:, None, :HEAD_SIZE], positions).astype(jnp.bfloat16)[:, 0]
    value_matrix = pairs[:, HEAD_SIZE:].astype(jnp.bfloat16)
    return jnp.concatenate(
        [query_matrix.reshape(row_count, heads_dev * HEAD_SIZE), key_matrix, value_matrix], axis=1
    )


def attend(soft_state, query_matrix, query_pos, key_matrix, value_matrix, key_pos, valid_keys):
    best_score, weight_sum, weighted = soft_state
    logit_scores = jnp.einsum(
        "rzsm,rvm->rzsv", query_matrix, key_matrix, preferred_element_type=jnp.float32
    ) * HEAD_SIZE ** (-0.5)
    allowed = (key_pos[None, :] <= query_pos[:, None])[None, None] & valid_keys[:, None, None, :]
    logit_scores = jnp.where(allowed, logit_scores, NEG)
    new_best = jnp.maximum(best_score, jnp.max(logit_scores, axis=-1))
    weights = jnp.where(allowed, jnp.exp(logit_scores - new_best[..., None]), 0.0)
    weight_sum = jnp.sum(weights, axis=-1)
    weighted = jnp.einsum(
        "awlp,ape->awle",
        weights.astype(jnp.bfloat16),
        value_matrix,
        preferred_element_type=jnp.float32,
    )
    return (new_best, weight_sum, weighted)


def per_device(states, short_lengths, attn_gain, wq, wkv, wo, mlp_gain, w_gate, w_up, w_down):
    n_ctx = lax.axis_size("ctx")
    n_tp = lax.axis_size("tp")
    ctx_rank = lax.axis_index("ctx")
    tp_index = lax.axis_index("tp")
    tok_rows = states.shape[0]
    rank_rows = tok_rows * n_tp
    n_blocks = 2 * n_ctx
    block_len = LLEN // n_blocks
    long_rows = LONG * 2 * block_len
    heads_dev = wq.shape[1] // HEAD_SIZE
    q_cols = heads_dev * HEAD_SIZE
    pair_width = 2 * HEAD_SIZE
    cache_cols = KVH * pair_width // n_tp
    kv_group = tp_index * KVH // n_tp
    wkv_head = lax.dynamic_slice_in_dim(wkv, kv_group * pair_width, pair_width, 1)
    first_col = tp_index * cache_cols - kv_group * pair_width
    positions = rank_positions(ctx_rank, rank_rows, block_len, long_rows, n_blocks)
    packed = project(
        [tp_all_gather(rms_scale(states, attn_gain), overlap=True)],
        positions,
        wq,
        wkv_head,
        heads_dev,
    )
    query_matrix = packed[:, :q_cols].reshape(rank_rows, heads_dev, HEAD_SIZE)
    key_matrix = packed[:, q_cols : q_cols + HEAD_SIZE]
    value_matrix = packed[:, q_cols + HEAD_SIZE :]
    long_q = (
        query_matrix[:long_rows]
        .reshape(LONG, 2 * block_len, heads_dev, HEAD_SIZE)
        .transpose(0, 2, 1, 3)
    )
    long_k = key_matrix[:long_rows].reshape(LONG, 2, 1, block_len, HEAD_SIZE)
    long_v = value_matrix[:long_rows].reshape(LONG, 2, 1, block_len, HEAD_SIZE)
    long_qpos = positions[: 2 * block_len]
    half_pick = jnp.arange(2, dtype=jnp.int32)[:, None, None]
    long_init = (
        jnp.full((LONG, heads_dev, 2 * block_len), NEG, jnp.float32),
        jnp.zeros((LONG, heads_dev, 2 * block_len), jnp.float32),
        jnp.zeros((LONG, heads_dev, 2 * block_len, HEAD_SIZE), jnp.float32),
        jnp.zeros((LONG, 2, block_len, cache_cols), jnp.float32),
    )
    parts = ctx_all_gather(jnp.concatenate([long_k[:, :, 0], long_v[:, :, 0]], axis=-1))
    piece_blocks = len(parts)
    block_ids = (ctx_rank + jnp.arange(piece_blocks, dtype=jnp.int32)) % n_ctx
    held_blocks = jnp.stack([block_ids, n_blocks - 1 - block_ids], axis=1)
    key_pos = (
        held_blocks[:, :, None] * block_len + jnp.arange(block_len, dtype=jnp.int32)
    ).reshape(-1)
    key_count = 2 * piece_blocks * block_len
    flat_kv = jnp.concatenate(
        [part.reshape(LONG, 2 * block_len, pair_width) for part in parts], axis=1
    )
    flat_k = flat_kv[..., :HEAD_SIZE]
    flat_v = flat_kv[..., HEAD_SIZE:]
    all_valid = jnp.ones((LONG, key_count), dtype=bool)
    soft_state = long_init[:3]
    soft_state = attend(soft_state, long_q, long_qpos, flat_k, flat_v, key_pos, all_valid)
    own_cols = lax.dynamic_slice_in_dim(flat_kv, first_col, cache_cols, 2).reshape(
        LONG, piece_blocks, 2, block_len, cache_cols
    )
    selector = ((held_blocks[None] // 2 == ctx_rank) & (held_blocks[None] % 2 == half_pick)).astype(
        jnp.bfloat16
    )
    cache_rows = jnp.einsum(
        "ejh,pjhbc->pebc", selector, own_cols, preferred_element_type=jnp.float32
    )
    folded = soft_state + (cache_rows,)
    long_out = (
        (folded[2] / folded[1][..., None])
        .astype(jnp.bfloat16)
        .transpose(0, 2, 1, 3)
        .reshape(long_rows, q_cols)
    )
    long_cache = folded[3].astype(jnp.bfloat16).reshape(LONG, 2 * block_len, cache_cols)
    short_count = short_lengths.shape[0]
    short_q = (
        query_matrix[long_rows:]
        .reshape(short_count, SLEN, heads_dev, HEAD_SIZE)
        .transpose(0, 2, 1, 3)
    )
    short_k = key_matrix[long_rows:].reshape(short_count, SLEN, HEAD_SIZE)
    short_v = value_matrix[long_rows:].reshape(short_count, SLEN, HEAD_SIZE)
    offsets = jnp.arange(SLEN, dtype=jnp.int32)
    short_valid = offsets[None, :] < short_lengths[:, None]
    short_init = (
        jnp.full((short_count, heads_dev, SLEN), NEG, jnp.float32),
        jnp.zeros((short_count, heads_dev, SLEN), jnp.float32),
        jnp.zeros((short_count, heads_dev, SLEN, HEAD_SIZE), jnp.float32),
    )
    short_state = attend(short_init, short_q, offsets, short_k, short_v, offsets, short_valid)
    short_out = (
        (short_state[2] / short_state[1][..., None])
        .astype(jnp.bfloat16)
        .transpose(0, 2, 1, 3)
        .reshape(short_count * SLEN, q_cols)
    )
    short_cache = lax.dynamic_slice_in_dim(
        jnp.concatenate([short_k, short_v], axis=-1), first_col, cache_cols, 2
    )
    attn = jnp.concatenate([long_out, short_out], axis=0)
    mixed = jnp.concatenate(
        [
            tp_reduce_scatter(jnp.dot(attn, part, preferred_element_type=jnp.float32).astype(jnp.bfloat16))
            for part in column_chunks(wo)
        ],
        axis=1,
    )
    residual = (states.astype(jnp.float32) + mixed).astype(jnp.bfloat16)
    pieces = [tp_all_gather(rms_scale(residual, mlp_gain), placed=False)]
    gate = split_dot(pieces, w_gate)
    up_part = split_dot(pieces, w_up)
    hidden = (jax.nn.silu(gate) * up_part).astype(jnp.bfloat16)
    down = jnp.concatenate(
        [
            tp_reduce_scatter_relative(
                jnp.dot(hidden, part, preferred_element_type=jnp.float32).astype(jnp.bfloat16)
            )
            for part in column_chunks(w_down)
        ],
        axis=1,
    )
    updated = (residual.astype(jnp.float32) + down).astype(jnp.bfloat16)
    return (updated, long_cache, short_cache)


def solution(mesh):
    in_specs = (
        P(("ctx", "tp"), None),
        P("ctx"),
        P(),
        P(None, "tp"),
        P(),
        P("tp", None),
        P(),
        P(None, "tp"),
        P(None, "tp"),
        P("tp", None),
    )
    out_specs = (P(("ctx", "tp"), None), P(None, "ctx", "tp"), P("ctx", None, "tp"))
    return jax.shard_map(
        per_device, mesh=mesh, in_specs=in_specs, out_specs=out_specs, check_vma=False
    )
```

```python
import jax
import jax.numpy as jnp
from jax import lax
from jax.sharding import PartitionSpec as P

KVH = 4
HEAD_SIZE = 64
LONG = 2
LLEN = 2048
SLEN = 64


EPS = 1e-05
THETA = 10000.0
NEG = -1e30


def rms_scale(matrix, gain):
    entries = matrix.astype(jnp.float32)
    power = jnp.mean(entries * entries, axis=-1, keepdims=True)
    return (entries * lax.rsqrt(power + EPS) * gain).astype(jnp.bfloat16)


def rotate(entries, positions):
    half_width = entries.shape[-1] // 2
    frequency = THETA ** (-jnp.arange(half_width, dtype=jnp.float32) * 2.0 / entries.shape[-1])
    angles = positions.astype(jnp.float32)[:, None] * frequency[None, :]
    cosine = jnp.cos(angles)[:, None, :]
    sine_wave = jnp.sin(angles)[:, None, :]
    first_half = entries[..., :half_width]
    second_half = entries[..., half_width:]
    return jnp.concatenate(
        [
            first_half * cosine - second_half * sine_wave,
            second_half * cosine + first_half * sine_wave,
        ],
        axis=-1,
    )


def rank_positions(ctx_rank, rank_rows, block_len, long_rows, n_blocks):
    index_row = jnp.arange(rank_rows, dtype=jnp.int32)
    half_index = index_row // block_len % 2
    offset_row = index_row % block_len
    which_block = jnp.where(half_index == 0, ctx_rank, n_blocks - 1 - ctx_rank)
    long_pos = which_block * block_len + offset_row
    short_pos = (index_row - long_rows) % SLEN
    return jnp.where(index_row < long_rows, long_pos, short_pos)


TP_DIMS = ((4, 8), (4, 2), (2, 1))


def shift_perm(n, stride, d, total):
    return [(t, t + (((t // stride) % n + d) % n - (t // stride) % n) * stride) for t in range(total)]


def scatter_stage(x, axis, n, stride, total):
    me = (lax.axis_index("tp") // stride) % n
    acc = lax.dynamic_index_in_dim(x, me, axis, keepdims=False).astype(jnp.float32)
    for d in range(1, n):
        part = lax.dynamic_index_in_dim(x, (me + d) % n, axis, keepdims=False)
        got = lax.ppermute(part.astype(jnp.bfloat16), "tp", shift_perm(n, stride, d, total))
        acc = acc + got.astype(jnp.float32)
    return acc


def tp_reduce_scatter(x):
    total = lax.axis_size("tp")
    rows, width = x.shape
    sizes = [n for n, _ in TP_DIMS]
    x = x.reshape(tuple(sizes) + (rows // total, width))
    for axis in reversed(range(len(TP_DIMS))):
        n, stride = TP_DIMS[axis]
        x = scatter_stage(x, axis, n, stride, total)
    return x


def gather_stage(x, axis, n, stride, total, placed):
    parts = [x] + [
        lax.ppermute(x, "tp", shift_perm(n, stride, (n - k) % n, total)) for k in range(1, n)
    ]
    if not placed:
        return jnp.stack(parts, axis=axis)
    me = (lax.axis_index("tp") // stride) % n
    out = jnp.zeros(x.shape[:axis] + (n,) + x.shape[axis:], x.dtype)
    for k, part in enumerate(parts):
        out = lax.dynamic_update_index_in_dim(out, part, (me + k) % n, axis)
    return out


def plane_gather(x, placed):
    total = lax.axis_size("tp")
    (nz, sz), (ny, sy) = TP_DIMS[:2]

    def fetch(value, n, stride, k):
        return lax.ppermute(value, "tp", shift_perm(n, stride, (n - k) % n, total))

    far = jnp.stack([fetch(x, nz, sz, k) for k in range(1, nz)])
    near = [fetch(x, ny, sy, k) for k in range(1, ny)]
    rest = [fetch(far, ny, sy, k) for k in range(1, ny)]
    columns = [jnp.concatenate([x[None], far])] + [
        jnp.concatenate([own[None], other]) for own, other in zip(near, rest)
    ]
    if not placed:
        return jnp.stack(columns, axis=1)
    tp_index = lax.axis_index("tp")
    me_z, me_y = (tp_index // sz) % nz, (tp_index // sy) % ny
    out = jnp.zeros((nz, ny) + x.shape, x.dtype)
    for k, column in enumerate(columns):
        slot = jnp.zeros((nz,) + x.shape, x.dtype)
        for j in range(nz):
            slot = lax.dynamic_update_index_in_dim(slot, column[j], (me_z + j) % nz, 0)
        out = lax.dynamic_update_index_in_dim(out, slot, (me_y + k) % ny, 1)
    return out


def tp_all_gather(x, placed=True, overlap=False):
    total = lax.axis_size("tp")
    rows, width = x.shape
    if overlap:
        x = plane_gather(x, placed)
    for axis, (n, stride) in enumerate(TP_DIMS):
        if axis >= 2 or not overlap:
            x = gather_stage(x, axis, n, stride, total, placed)
    return x.reshape(rows * total, width)


def relative_scatter_stage(x, axis, n, stride, total):
    acc = lax.index_in_dim(x, 0, axis, keepdims=False).astype(jnp.float32)
    for d in range(1, n):
        part = lax.index_in_dim(x, d, axis, keepdims=False)
        got = lax.ppermute(part.astype(jnp.bfloat16), "tp", shift_perm(n, stride, d, total))
        acc = acc + got.astype(jnp.float32)
    return acc


def tp_reduce_scatter_relative(x):
    total = lax.axis_size("tp")
    rows, width = x.shape
    sizes = [n for n, _ in TP_DIMS]
    x = x.reshape(tuple(sizes) + (rows // total, width))
    for axis in reversed(range(len(TP_DIMS))):
        n, stride = TP_DIMS[axis]
        x = relative_scatter_stage(x, axis, n, stride, total)
    return x


def ctx_all_gather(x):
    n = lax.axis_size("ctx")
    parts = [x] + [
        lax.ppermute(x, "ctx", [(j, (j - k) % n) for j in range(n)]) for k in range(1, n)
    ]
    return parts


CHUNKS = 2


def column_chunks(matrix, axis=1, count=CHUNKS):
    width = matrix.shape[axis] // count
    return [lax.slice_in_dim(matrix, i * width, (i + 1) * width, axis=axis) for i in range(count)]


def split_dot(pieces, weight):
    parts = column_chunks(weight, axis=0, count=len(pieces))
    total = jnp.dot(pieces[0], parts[0], preferred_element_type=jnp.float32)
    for piece, part in zip(pieces[1:], parts[1:]):
        total = total + jnp.dot(piece, part, preferred_element_type=jnp.float32)
    return total


def project(pieces, positions, wq, wkv_head, heads_dev):
    row_count = pieces[0].shape[0]
    query_matrix = split_dot(pieces, wq).reshape(row_count, heads_dev, HEAD_SIZE)
    query_matrix = rotate(query_matrix, positions).astype(jnp.bfloat16)
    pairs = split_dot(pieces, wkv_head)
    key_matrix = rotate(pairs[:, None, :HEAD_SIZE], positions).astype(jnp.bfloat16)[:, 0]
    value_matrix = pairs[:, HEAD_SIZE:].astype(jnp.bfloat16)
    return query_matrix, key_matrix, value_matrix


def attend(soft_state, query_matrix, query_pos, key_matrix, value_matrix, key_pos, valid_keys):
    best_score, weight_sum, weighted = soft_state
    logit_scores = jnp.einsum(
        "rzsm,rvm->rzsv", query_matrix, key_matrix, preferred_element_type=jnp.float32
    ) * HEAD_SIZE ** (-0.5)
    allowed = (key_pos[None, :] <= query_pos[:, None])[None, None] & valid_keys[:, None, None, :]
    logit_scores = jnp.where(allowed, logit_scores, NEG)
    new_best = jnp.maximum(best_score, jnp.max(logit_scores, axis=-1))
    weights = jnp.where(allowed, jnp.exp(logit_scores - new_best[..., None]), 0.0)
    weight_sum = jnp.sum(weights, axis=-1)
    weighted = jnp.einsum(
        "awlp,ape->awle",
        weights.astype(jnp.bfloat16),
        value_matrix,
        preferred_element_type=jnp.float32,
    )
    return (new_best, weight_sum, weighted)


def per_device(states, short_lengths, attn_gain, wq, wkv, wo, mlp_gain, w_gate, w_up, w_down):
    n_ctx = lax.axis_size("ctx")
    n_tp = lax.axis_size("tp")
    ctx_rank = lax.axis_index("ctx")
    tp_index = lax.axis_index("tp")
    tok_rows = states.shape[0]
    rank_rows = tok_rows * n_tp
    n_blocks = 2 * n_ctx
    block_len = LLEN // n_blocks
    long_rows = LONG * 2 * block_len
    heads_dev = wq.shape[1] // HEAD_SIZE
    q_cols = heads_dev * HEAD_SIZE
    pair_width = 2 * HEAD_SIZE
    cache_cols = KVH * pair_width // n_tp
    kv_group = tp_index * KVH // n_tp
    wkv_head = lax.dynamic_slice_in_dim(wkv, kv_group * pair_width, pair_width, 1)
    first_col = tp_index * cache_cols - kv_group * pair_width
    positions = rank_positions(ctx_rank, rank_rows, block_len, long_rows, n_blocks)
    query_matrix, key_matrix, value_matrix = project(
        [tp_all_gather(rms_scale(states, attn_gain), overlap=True)],
        positions,
        wq,
        wkv_head,
        heads_dev,
    )
    long_q = (
        query_matrix[:long_rows]
        .reshape(LONG, 2 * block_len, heads_dev, HEAD_SIZE)
        .transpose(0, 2, 1, 3)
    )
    long_k = key_matrix[:long_rows].reshape(LONG, 2, 1, block_len, HEAD_SIZE)
    long_v = value_matrix[:long_rows].reshape(LONG, 2, 1, block_len, HEAD_SIZE)
    long_qpos = positions[: 2 * block_len]
    half_pick = jnp.arange(2, dtype=jnp.int32)[:, None, None]
    long_init = (
        jnp.full((LONG, heads_dev, 2 * block_len), NEG, jnp.float32),
        jnp.zeros((LONG, heads_dev, 2 * block_len), jnp.float32),
        jnp.zeros((LONG, heads_dev, 2 * block_len, HEAD_SIZE), jnp.float32),
        jnp.zeros((LONG, 2, block_len, cache_cols), jnp.float32),
    )
    short_count = short_lengths.shape[0]
    short_q = (
        query_matrix[long_rows:]
        .reshape(short_count, SLEN, heads_dev, HEAD_SIZE)
        .transpose(0, 2, 1, 3)
    )
    short_k = key_matrix[long_rows:].reshape(short_count, SLEN, HEAD_SIZE)
    short_v = value_matrix[long_rows:].reshape(short_count, SLEN, HEAD_SIZE)
    offsets = jnp.arange(SLEN, dtype=jnp.int32)
    short_valid = offsets[None, :] < short_lengths[:, None]
    short_init = (
        jnp.full((short_count, heads_dev, SLEN), NEG, jnp.float32),
        jnp.zeros((short_count, heads_dev, SLEN), jnp.float32),
        jnp.zeros((short_count, heads_dev, SLEN, HEAD_SIZE), jnp.float32),
    )
    short_state = attend(short_init, short_q, offsets, short_k, short_v, offsets, short_valid)
    short_out = (
        (short_state[2] / short_state[1][..., None])
        .astype(jnp.bfloat16)
        .transpose(0, 2, 1, 3)
        .reshape(short_count * SLEN, q_cols)
    )
    short_cache = lax.dynamic_slice_in_dim(
        jnp.concatenate([short_k, short_v], axis=-1), first_col, cache_cols, 2
    )
    parts = ctx_all_gather(jnp.concatenate([long_k[:, :, 0], long_v[:, :, 0]], axis=-1))
    parts, short_out = lax.optimization_barrier((parts, short_out))
    piece_blocks = len(parts)
    block_ids = (ctx_rank + jnp.arange(piece_blocks, dtype=jnp.int32)) % n_ctx
    held_blocks = jnp.stack([block_ids, n_blocks - 1 - block_ids], axis=1)
    key_pos = (
        held_blocks[:, :, None] * block_len + jnp.arange(block_len, dtype=jnp.int32)
    ).reshape(-1)
    key_count = 2 * piece_blocks * block_len
    flat_kv = jnp.concatenate(
        [part.reshape(LONG, 2 * block_len, pair_width) for part in parts], axis=1
    )
    flat_k = flat_kv[..., :HEAD_SIZE]
    flat_v = flat_kv[..., HEAD_SIZE:]
    all_valid = jnp.ones((LONG, key_count), dtype=bool)
    soft_state = long_init[:3]
    soft_state = attend(soft_state, long_q, long_qpos, flat_k, flat_v, key_pos, all_valid)
    own_cols = lax.dynamic_slice_in_dim(flat_kv, first_col, cache_cols, 2).reshape(
        LONG, piece_blocks, 2, block_len, cache_cols
    )
    selector = ((held_blocks[None] // 2 == ctx_rank) & (held_blocks[None] % 2 == half_pick)).astype(
        jnp.bfloat16
    )
    cache_rows = jnp.einsum(
        "ejh,pjhbc->pebc", selector, own_cols, preferred_element_type=jnp.float32
    )
    folded = soft_state + (cache_rows,)
    long_out = (
        (folded[2] / folded[1][..., None])
        .astype(jnp.bfloat16)
        .transpose(0, 2, 1, 3)
        .reshape(long_rows, q_cols)
    )
    long_cache = folded[3].astype(jnp.bfloat16).reshape(LONG, 2 * block_len, cache_cols)
    attn = jnp.concatenate([long_out, short_out], axis=0)
    mixed = jnp.concatenate(
        [
            tp_reduce_scatter(jnp.dot(attn, part, preferred_element_type=jnp.float32).astype(jnp.bfloat16))
            for part in column_chunks(wo)
        ],
        axis=1,
    )
    residual = (states.astype(jnp.float32) + mixed).astype(jnp.bfloat16)
    pieces = [tp_all_gather(rms_scale(residual, mlp_gain), placed=False)]
    gate = split_dot(pieces, w_gate)
    up_part = split_dot(pieces, w_up)
    hidden = (jax.nn.silu(gate) * up_part).astype(jnp.bfloat16)
    down = jnp.concatenate(
        [
            tp_reduce_scatter_relative(
                jnp.dot(hidden, part, preferred_element_type=jnp.float32).astype(jnp.bfloat16)
            )
            for part in column_chunks(w_down)
        ],
        axis=1,
    )
    updated = (residual.astype(jnp.float32) + down).astype(jnp.bfloat16)
    return (updated, long_cache, short_cache)


def solution(mesh):
    in_specs = (
        P(("ctx", "tp"), None),
        P("ctx"),
        P(),
        P(None, "tp"),
        P(),
        P("tp", None),
        P(),
        P(None, "tp"),
        P(None, "tp"),
        P("tp", None),
    )
    out_specs = (P(("ctx", "tp"), None), P(None, "ctx", "tp"), P("ctx", None, "tp"))
    return jax.shard_map(
        per_device, mesh=mesh, in_specs=in_specs, out_specs=out_specs, check_vma=False
    )
```

```python
import jax
import jax.numpy as jnp
from jax import lax
from jax.sharding import PartitionSpec as P

KVH = 4
HEAD_SIZE = 64
LONG = 2
LLEN = 2048
SLEN = 64


EPS = 1e-05
THETA = 10000.0
NEG = -1e30


def rms_scale(matrix, gain):
    entries = matrix.astype(jnp.float32)
    power = jnp.mean(entries * entries, axis=-1, keepdims=True)
    return (entries * lax.rsqrt(power + EPS) * gain).astype(jnp.bfloat16)


def rotate(entries, positions):
    half_width = entries.shape[-1] // 2
    frequency = THETA ** (-jnp.arange(half_width, dtype=jnp.float32) * 2.0 / entries.shape[-1])
    angles = positions.astype(jnp.float32)[:, None] * frequency[None, :]
    cosine = jnp.cos(angles)[:, None, :]
    sine_wave = jnp.sin(angles)[:, None, :]
    first_half = entries[..., :half_width]
    second_half = entries[..., half_width:]
    return jnp.concatenate(
        [
            first_half * cosine - second_half * sine_wave,
            second_half * cosine + first_half * sine_wave,
        ],
        axis=-1,
    )


def rank_positions(ctx_rank, rank_rows, block_len, long_rows, n_blocks):
    index_row = jnp.arange(rank_rows, dtype=jnp.int32)
    half_index = index_row // block_len % 2
    offset_row = index_row % block_len
    which_block = jnp.where(half_index == 0, ctx_rank, n_blocks - 1 - ctx_rank)
    long_pos = which_block * block_len + offset_row
    short_pos = (index_row - long_rows) % SLEN
    return jnp.where(index_row < long_rows, long_pos, short_pos)


TP_DIMS = ((4, 8), (4, 2), (2, 1))


def shift_perm(n, stride, d, total):
    return [(t, t + (((t // stride) % n + d) % n - (t // stride) % n) * stride) for t in range(total)]


def scatter_stage(x, axis, n, stride, total):
    me = (lax.axis_index("tp") // stride) % n
    acc = lax.dynamic_index_in_dim(x, me, axis, keepdims=False).astype(jnp.float32)
    for d in range(1, n):
        part = lax.dynamic_index_in_dim(x, (me + d) % n, axis, keepdims=False)
        got = lax.ppermute(part.astype(jnp.bfloat16), "tp", shift_perm(n, stride, d, total))
        acc = acc + got.astype(jnp.float32)
    return acc


def tp_reduce_scatter(x):
    total = lax.axis_size("tp")
    rows, width = x.shape
    sizes = [n for n, _ in TP_DIMS]
    x = x.reshape(tuple(sizes) + (rows // total, width))
    for axis in reversed(range(len(TP_DIMS))):
        n, stride = TP_DIMS[axis]
        x = scatter_stage(x, axis, n, stride, total)
    return x


def gather_stage(x, axis, n, stride, total, placed):
    parts = [x] + [
        lax.ppermute(x, "tp", shift_perm(n, stride, (n - k) % n, total)) for k in range(1, n)
    ]
    if not placed:
        return jnp.stack(parts, axis=axis)
    me = (lax.axis_index("tp") // stride) % n
    out = jnp.zeros(x.shape[:axis] + (n,) + x.shape[axis:], x.dtype)
    for k, part in enumerate(parts):
        out = lax.dynamic_update_index_in_dim(out, part, (me + k) % n, axis)
    return out


def plane_gather(x, placed):
    total = lax.axis_size("tp")
    (nz, sz), (ny, sy) = TP_DIMS[:2]

    def fetch(value, n, stride, k):
        return lax.ppermute(value, "tp", shift_perm(n, stride, (n - k) % n, total))

    far = jnp.stack([fetch(x, nz, sz, k) for k in range(1, nz)])
    near = [fetch(x, ny, sy, k) for k in range(1, ny)]
    far, near = lax.optimization_barrier((far, near))
    rest = [fetch(far, ny, sy, k) for k in range(1, ny)]
    columns = [jnp.concatenate([x[None], far])] + [
        jnp.concatenate([own[None], other]) for own, other in zip(near, rest)
    ]
    if not placed:
        return jnp.stack(columns, axis=1)
    tp_index = lax.axis_index("tp")
    me_z, me_y = (tp_index // sz) % nz, (tp_index // sy) % ny
    out = jnp.zeros((nz, ny) + x.shape, x.dtype)
    for k, column in enumerate(columns):
        slot = jnp.zeros((nz,) + x.shape, x.dtype)
        for j in range(nz):
            slot = lax.dynamic_update_index_in_dim(slot, column[j], (me_z + j) % nz, 0)
        out = lax.dynamic_update_index_in_dim(out, slot, (me_y + k) % ny, 1)
    return out


def tp_all_gather(x, placed=True, overlap=False):
    total = lax.axis_size("tp")
    rows, width = x.shape
    if overlap:
        x = plane_gather(x, placed)
    for axis, (n, stride) in enumerate(TP_DIMS):
        if axis >= 2 or not overlap:
            x = gather_stage(x, axis, n, stride, total, placed)
    return x.reshape(rows * total, width)


def relative_scatter_stage(x, axis, n, stride, total):
    acc = lax.index_in_dim(x, 0, axis, keepdims=False).astype(jnp.float32)
    for d in range(1, n):
        part = lax.index_in_dim(x, d, axis, keepdims=False)
        got = lax.ppermute(part.astype(jnp.bfloat16), "tp", shift_perm(n, stride, d, total))
        acc = acc + got.astype(jnp.float32)
    return acc


def tp_reduce_scatter_relative(x):
    total = lax.axis_size("tp")
    rows, width = x.shape
    sizes = [n for n, _ in TP_DIMS]
    x = x.reshape(tuple(sizes) + (rows // total, width))
    for axis in reversed(range(len(TP_DIMS))):
        n, stride = TP_DIMS[axis]
        x = relative_scatter_stage(x, axis, n, stride, total)
    return x


def ctx_all_gather(x):
    n = lax.axis_size("ctx")
    parts = [x] + [
        lax.ppermute(x, "ctx", [(j, (j - k) % n) for j in range(n)]) for k in range(1, n)
    ]
    return parts


CHUNKS = 2


def column_chunks(matrix, axis=1, count=CHUNKS):
    width = matrix.shape[axis] // count
    return [lax.slice_in_dim(matrix, i * width, (i + 1) * width, axis=axis) for i in range(count)]


def split_dot(pieces, weight):
    parts = column_chunks(weight, axis=0, count=len(pieces))
    total = jnp.dot(pieces[0], parts[0], preferred_element_type=jnp.float32)
    for piece, part in zip(pieces[1:], parts[1:]):
        total = total + jnp.dot(piece, part, preferred_element_type=jnp.float32)
    return total


def project(pieces, positions, wq, wkv_head, heads_dev):
    row_count = pieces[0].shape[0]
    query_matrix = split_dot(pieces, wq).reshape(row_count, heads_dev, HEAD_SIZE)
    query_matrix = rotate(query_matrix, positions).astype(jnp.bfloat16)
    pairs = split_dot(pieces, wkv_head)
    key_matrix = rotate(pairs[:, None, :HEAD_SIZE], positions).astype(jnp.bfloat16)[:, 0]
    value_matrix = pairs[:, HEAD_SIZE:].astype(jnp.bfloat16)
    return jnp.concatenate(
        [query_matrix.reshape(row_count, heads_dev * HEAD_SIZE), key_matrix, value_matrix], axis=1
    )


def attend(soft_state, query_matrix, query_pos, key_matrix, value_matrix, key_pos, valid_keys):
    best_score, weight_sum, weighted = soft_state
    logit_scores = jnp.einsum(
        "rzsm,rvm->rzsv", query_matrix, key_matrix, preferred_element_type=jnp.float32
    ) * HEAD_SIZE ** (-0.5)
    allowed = (key_pos[None, :] <= query_pos[:, None])[None, None] & valid_keys[:, None, None, :]
    logit_scores = jnp.where(allowed, logit_scores, NEG)
    new_best = jnp.maximum(best_score, jnp.max(logit_scores, axis=-1))
    weights = jnp.where(allowed, jnp.exp(logit_scores - new_best[..., None]), 0.0)
    weight_sum = jnp.sum(weights, axis=-1)
    weighted = jnp.einsum(
        "awlp,ape->awle",
        weights.astype(jnp.bfloat16),
        value_matrix,
        preferred_element_type=jnp.float32,
    )
    return (new_best, weight_sum, weighted)


def per_device(states, short_lengths, attn_gain, wq, wkv, wo, mlp_gain, w_gate, w_up, w_down):
    n_ctx = lax.axis_size("ctx")
    n_tp = lax.axis_size("tp")
    ctx_rank = lax.axis_index("ctx")
    tp_index = lax.axis_index("tp")
    tok_rows = states.shape[0]
    rank_rows = tok_rows * n_tp
    n_blocks = 2 * n_ctx
    block_len = LLEN // n_blocks
    long_rows = LONG * 2 * block_len
    heads_dev = wq.shape[1] // HEAD_SIZE
    q_cols = heads_dev * HEAD_SIZE
    pair_width = 2 * HEAD_SIZE
    cache_cols = KVH * pair_width // n_tp
    kv_group = tp_index * KVH // n_tp
    wkv_head = lax.dynamic_slice_in_dim(wkv, kv_group * pair_width, pair_width, 1)
    first_col = tp_index * cache_cols - kv_group * pair_width
    positions = rank_positions(ctx_rank, rank_rows, block_len, long_rows, n_blocks)
    packed = project(
        [tp_all_gather(rms_scale(states, attn_gain), overlap=True)],
        positions,
        wq,
        wkv_head,
        heads_dev,
    )
    query_matrix = packed[:, :q_cols].reshape(rank_rows, heads_dev, HEAD_SIZE)
    key_matrix = packed[:, q_cols : q_cols + HEAD_SIZE]
    value_matrix = packed[:, q_cols + HEAD_SIZE :]
    long_q = (
        query_matrix[:long_rows]
        .reshape(LONG, 2 * block_len, heads_dev, HEAD_SIZE)
        .transpose(0, 2, 1, 3)
    )
    long_k = key_matrix[:long_rows].reshape(LONG, 2, 1, block_len, HEAD_SIZE)
    long_v = value_matrix[:long_rows].reshape(LONG, 2, 1, block_len, HEAD_SIZE)
    long_qpos = positions[: 2 * block_len]
    half_pick = jnp.arange(2, dtype=jnp.int32)[:, None, None]
    long_init = (
        jnp.full((LONG, heads_dev, 2 * block_len), NEG, jnp.float32),
        jnp.zeros((LONG, heads_dev, 2 * block_len), jnp.float32),
        jnp.zeros((LONG, heads_dev, 2 * block_len, HEAD_SIZE), jnp.float32),
        jnp.zeros((LONG, 2, block_len, cache_cols), jnp.float32),
    )
    parts = ctx_all_gather(jnp.concatenate([long_k[:, :, 0], long_v[:, :, 0]], axis=-1))
    piece_blocks = len(parts)
    block_ids = (ctx_rank + jnp.arange(piece_blocks, dtype=jnp.int32)) % n_ctx
    held_blocks = jnp.stack([block_ids, n_blocks - 1 - block_ids], axis=1)
    key_pos = (
        held_blocks[:, :, None] * block_len + jnp.arange(block_len, dtype=jnp.int32)
    ).reshape(-1)
    key_count = 2 * piece_blocks * block_len
    flat_kv = jnp.concatenate(
        [part.reshape(LONG, 2 * block_len, pair_width) for part in parts], axis=1
    )
    flat_k = flat_kv[..., :HEAD_SIZE]
    flat_v = flat_kv[..., HEAD_SIZE:]
    all_valid = jnp.ones((LONG, key_count), dtype=bool)
    soft_state = long_init[:3]
    soft_state = attend(soft_state, long_q, long_qpos, flat_k, flat_v, key_pos, all_valid)
    own_cols = lax.dynamic_slice_in_dim(flat_kv, first_col, cache_cols, 2).reshape(
        LONG, piece_blocks, 2, block_len, cache_cols
    )
    selector = ((held_blocks[None] // 2 == ctx_rank) & (held_blocks[None] % 2 == half_pick)).astype(
        jnp.bfloat16
    )
    cache_rows = jnp.einsum(
        "ejh,pjhbc->pebc", selector, own_cols, preferred_element_type=jnp.float32
    )
    folded = soft_state + (cache_rows,)
    long_out = (
        (folded[2] / folded[1][..., None])
        .astype(jnp.bfloat16)
        .transpose(0, 2, 1, 3)
        .reshape(long_rows, q_cols)
    )
    long_cache = folded[3].astype(jnp.bfloat16).reshape(LONG, 2 * block_len, cache_cols)
    short_count = short_lengths.shape[0]
    short_q = (
        query_matrix[long_rows:]
        .reshape(short_count, SLEN, heads_dev, HEAD_SIZE)
        .transpose(0, 2, 1, 3)
    )
    short_k = key_matrix[long_rows:].reshape(short_count, SLEN, HEAD_SIZE)
    short_v = value_matrix[long_rows:].reshape(short_count, SLEN, HEAD_SIZE)
    offsets = jnp.arange(SLEN, dtype=jnp.int32)
    short_valid = offsets[None, :] < short_lengths[:, None]
    short_init = (
        jnp.full((short_count, heads_dev, SLEN), NEG, jnp.float32),
        jnp.zeros((short_count, heads_dev, SLEN), jnp.float32),
        jnp.zeros((short_count, heads_dev, SLEN, HEAD_SIZE), jnp.float32),
    )
    short_state = attend(short_init, short_q, offsets, short_k, short_v, offsets, short_valid)
    short_out = (
        (short_state[2] / short_state[1][..., None])
        .astype(jnp.bfloat16)
        .transpose(0, 2, 1, 3)
        .reshape(short_count * SLEN, q_cols)
    )
    short_cache = lax.dynamic_slice_in_dim(
        jnp.concatenate([short_k, short_v], axis=-1), first_col, cache_cols, 2
    )
    attn = jnp.concatenate([long_out, short_out], axis=0)
    mixed = jnp.concatenate(
        [
            tp_reduce_scatter(jnp.dot(attn, part, preferred_element_type=jnp.float32).astype(jnp.bfloat16))
            for part in column_chunks(wo)
        ],
        axis=1,
    )
    residual = (states.astype(jnp.float32) + mixed).astype(jnp.bfloat16)
    pieces = [tp_all_gather(rms_scale(residual, mlp_gain), placed=False, overlap=True)]
    gate = split_dot(pieces, w_gate)
    up_part = split_dot(pieces, w_up)
    hidden = (jax.nn.silu(gate) * up_part).astype(jnp.bfloat16)
    down = jnp.concatenate(
        [
            tp_reduce_scatter_relative(
                jnp.dot(hidden, part, preferred_element_type=jnp.float32).astype(jnp.bfloat16)
            )
            for part in column_chunks(w_down)
        ],
        axis=1,
    )
    updated = (residual.astype(jnp.float32) + down).astype(jnp.bfloat16)
    return (updated, long_cache, short_cache)


def solution(mesh):
    in_specs = (
        P(("ctx", "tp"), None),
        P("ctx"),
        P(),
        P(None, "tp"),
        P(),
        P("tp", None),
        P(),
        P(None, "tp"),
        P(None, "tp"),
        P("tp", None),
    )
    out_specs = (P(("ctx", "tp"), None), P(None, "ctx", "tp"), P("ctx", None, "tp"))
    return jax.shard_map(
        per_device, mesh=mesh, in_specs=in_specs, out_specs=out_specs, check_vma=False
    )
```

```python
import jax
import jax.numpy as jnp
from jax import lax
from jax.sharding import PartitionSpec as P

KVH = 4
HEAD_SIZE = 64
LONG = 2
LLEN = 2048
SLEN = 64


EPS = 1e-05
THETA = 10000.0
NEG = -1e30


def rms_scale(matrix, gain):
    entries = matrix.astype(jnp.float32)
    power = jnp.mean(entries * entries, axis=-1, keepdims=True)
    return (entries * lax.rsqrt(power + EPS) * gain).astype(jnp.bfloat16)


def rotate(entries, positions):
    half_width = entries.shape[-1] // 2
    frequency = THETA ** (-jnp.arange(half_width, dtype=jnp.float32) * 2.0 / entries.shape[-1])
    angles = positions.astype(jnp.float32)[:, None] * frequency[None, :]
    cosine = jnp.cos(angles)[:, None, :]
    sine_wave = jnp.sin(angles)[:, None, :]
    first_half = entries[..., :half_width]
    second_half = entries[..., half_width:]
    return jnp.concatenate(
        [
            first_half * cosine - second_half * sine_wave,
            second_half * cosine + first_half * sine_wave,
        ],
        axis=-1,
    )


def rank_positions(ctx_rank, rank_rows, block_len, long_rows, n_blocks):
    index_row = jnp.arange(rank_rows, dtype=jnp.int32)
    half_index = index_row // block_len % 2
    offset_row = index_row % block_len
    which_block = jnp.where(half_index == 0, ctx_rank, n_blocks - 1 - ctx_rank)
    long_pos = which_block * block_len + offset_row
    short_pos = (index_row - long_rows) % SLEN
    return jnp.where(index_row < long_rows, long_pos, short_pos)


TP_DIMS = ((4, 8), (4, 2), (2, 1))


def shift_perm(n, stride, d, total):
    return [(t, t + (((t // stride) % n + d) % n - (t // stride) % n) * stride) for t in range(total)]


def scatter_stage(x, axis, n, stride, total):
    me = (lax.axis_index("tp") // stride) % n
    acc = lax.dynamic_index_in_dim(x, me, axis, keepdims=False).astype(jnp.float32)
    for d in range(1, n):
        part = lax.dynamic_index_in_dim(x, (me + d) % n, axis, keepdims=False)
        got = lax.ppermute(part.astype(jnp.bfloat16), "tp", shift_perm(n, stride, d, total))
        acc = acc + got.astype(jnp.float32)
    return acc


def tp_reduce_scatter(x):
    total = lax.axis_size("tp")
    rows, width = x.shape
    sizes = [n for n, _ in TP_DIMS]
    x = x.reshape(tuple(sizes) + (rows // total, width))
    for axis in reversed(range(len(TP_DIMS))):
        n, stride = TP_DIMS[axis]
        x = scatter_stage(x, axis, n, stride, total)
    return x


def gather_stage(x, axis, n, stride, total, placed):
    parts = [x] + [
        lax.ppermute(x, "tp", shift_perm(n, stride, (n - k) % n, total)) for k in range(1, n)
    ]
    if not placed:
        return jnp.stack(parts, axis=axis)
    me = (lax.axis_index("tp") // stride) % n
    out = jnp.zeros(x.shape[:axis] + (n,) + x.shape[axis:], x.dtype)
    for k, part in enumerate(parts):
        out = lax.dynamic_update_index_in_dim(out, part, (me + k) % n, axis)
    return out


def plane_gather(x, placed, forced):
    total = lax.axis_size("tp")
    (nz, sz), (ny, sy) = TP_DIMS[:2]

    def fetch(value, n, stride, k):
        return lax.ppermute(value, "tp", shift_perm(n, stride, (n - k) % n, total))

    far = jnp.stack([fetch(x, nz, sz, k) for k in range(1, nz)])
    near = [fetch(x, ny, sy, k) for k in range(1, ny)]
    if forced:
        far, near = lax.optimization_barrier((far, near))
    rest = [fetch(far, ny, sy, k) for k in range(1, ny)]
    columns = [jnp.concatenate([x[None], far])] + [
        jnp.concatenate([own[None], other]) for own, other in zip(near, rest)
    ]
    if not placed:
        return jnp.stack(columns, axis=1)
    tp_index = lax.axis_index("tp")
    me_z, me_y = (tp_index // sz) % nz, (tp_index // sy) % ny
    out = jnp.zeros((nz, ny) + x.shape, x.dtype)
    for k, column in enumerate(columns):
        slot = jnp.zeros((nz,) + x.shape, x.dtype)
        for j in range(nz):
            slot = lax.dynamic_update_index_in_dim(slot, column[j], (me_z + j) % nz, 0)
        out = lax.dynamic_update_index_in_dim(out, slot, (me_y + k) % ny, 1)
    return out


def tp_all_gather(x, placed=True, overlap=False, forced=False):
    total = lax.axis_size("tp")
    rows, width = x.shape
    if overlap:
        x = plane_gather(x, placed, forced)
    for axis, (n, stride) in enumerate(TP_DIMS):
        if axis >= 2 or not overlap:
            x = gather_stage(x, axis, n, stride, total, placed)
    return x.reshape(rows * total, width)


def relative_scatter_stage(x, axis, n, stride, total):
    acc = lax.index_in_dim(x, 0, axis, keepdims=False).astype(jnp.float32)
    for d in range(1, n):
        part = lax.index_in_dim(x, d, axis, keepdims=False)
        got = lax.ppermute(part.astype(jnp.bfloat16), "tp", shift_perm(n, stride, d, total))
        acc = acc + got.astype(jnp.float32)
    return acc


def tp_reduce_scatter_relative(x):
    total = lax.axis_size("tp")
    rows, width = x.shape
    sizes = [n for n, _ in TP_DIMS]
    x = x.reshape(tuple(sizes) + (rows // total, width))
    for axis in reversed(range(len(TP_DIMS))):
        n, stride = TP_DIMS[axis]
        x = relative_scatter_stage(x, axis, n, stride, total)
    return x


def ctx_all_gather(x):
    n = lax.axis_size("ctx")
    parts = [x] + [
        lax.ppermute(x, "ctx", [(j, (j - k) % n) for j in range(n)]) for k in range(1, n)
    ]
    return parts


CHUNKS = 2


def column_chunks(matrix, axis=1, count=CHUNKS):
    width = matrix.shape[axis] // count
    return [lax.slice_in_dim(matrix, i * width, (i + 1) * width, axis=axis) for i in range(count)]


def split_dot(pieces, weight):
    parts = column_chunks(weight, axis=0, count=len(pieces))
    total = jnp.dot(pieces[0], parts[0], preferred_element_type=jnp.float32)
    for piece, part in zip(pieces[1:], parts[1:]):
        total = total + jnp.dot(piece, part, preferred_element_type=jnp.float32)
    return total


def project(pieces, positions, wq, wkv_head, heads_dev):
    row_count = pieces[0].shape[0]
    query_matrix = split_dot(pieces, wq).reshape(row_count, heads_dev, HEAD_SIZE)
    query_matrix = rotate(query_matrix, positions).astype(jnp.bfloat16)
    pairs = split_dot(pieces, wkv_head)
    key_matrix = rotate(pairs[:, None, :HEAD_SIZE], positions).astype(jnp.bfloat16)[:, 0]
    value_matrix = pairs[:, HEAD_SIZE:].astype(jnp.bfloat16)
    return jnp.concatenate(
        [query_matrix.reshape(row_count, heads_dev * HEAD_SIZE), key_matrix, value_matrix], axis=1
    )


def attend(soft_state, query_matrix, query_pos, key_matrix, value_matrix, key_pos, valid_keys):
    best_score, weight_sum, weighted = soft_state
    logit_scores = jnp.einsum(
        "rzsm,rvm->rzsv", query_matrix, key_matrix, preferred_element_type=jnp.float32
    ) * HEAD_SIZE ** (-0.5)
    allowed = (key_pos[None, :] <= query_pos[:, None])[None, None] & valid_keys[:, None, None, :]
    logit_scores = jnp.where(allowed, logit_scores, NEG)
    new_best = jnp.maximum(best_score, jnp.max(logit_scores, axis=-1))
    weights = jnp.where(allowed, jnp.exp(logit_scores - new_best[..., None]), 0.0)
    weight_sum = jnp.sum(weights, axis=-1)
    weighted = jnp.einsum(
        "awlp,ape->awle",
        weights.astype(jnp.bfloat16),
        value_matrix,
        preferred_element_type=jnp.float32,
    )
    return (new_best, weight_sum, weighted)


def per_device(states, short_lengths, attn_gain, wq, wkv, wo, mlp_gain, w_gate, w_up, w_down):
    n_ctx = lax.axis_size("ctx")
    n_tp = lax.axis_size("tp")
    ctx_rank = lax.axis_index("ctx")
    tp_index = lax.axis_index("tp")
    tok_rows = states.shape[0]
    rank_rows = tok_rows * n_tp
    n_blocks = 2 * n_ctx
    block_len = LLEN // n_blocks
    long_rows = LONG * 2 * block_len
    heads_dev = wq.shape[1] // HEAD_SIZE
    q_cols = heads_dev * HEAD_SIZE
    pair_width = 2 * HEAD_SIZE
    cache_cols = KVH * pair_width // n_tp
    kv_group = tp_index * KVH // n_tp
    wkv_head = lax.dynamic_slice_in_dim(wkv, kv_group * pair_width, pair_width, 1)
    first_col = tp_index * cache_cols - kv_group * pair_width
    positions = rank_positions(ctx_rank, rank_rows, block_len, long_rows, n_blocks)
    packed = project(
        [tp_all_gather(rms_scale(states, attn_gain), overlap=True)],
        positions,
        wq,
        wkv_head,
        heads_dev,
    )
    query_matrix = packed[:, :q_cols].reshape(rank_rows, heads_dev, HEAD_SIZE)
    key_matrix = packed[:, q_cols : q_cols + HEAD_SIZE]
    value_matrix = packed[:, q_cols + HEAD_SIZE :]
    long_q = (
        query_matrix[:long_rows]
        .reshape(LONG, 2 * block_len, heads_dev, HEAD_SIZE)
        .transpose(0, 2, 1, 3)
    )
    long_k = key_matrix[:long_rows].reshape(LONG, 2, 1, block_len, HEAD_SIZE)
    long_v = value_matrix[:long_rows].reshape(LONG, 2, 1, block_len, HEAD_SIZE)
    long_qpos = positions[: 2 * block_len]
    half_pick = jnp.arange(2, dtype=jnp.int32)[:, None, None]
    long_init = (
        jnp.full((LONG, heads_dev, 2 * block_len), NEG, jnp.float32),
        jnp.zeros((LONG, heads_dev, 2 * block_len), jnp.float32),
        jnp.zeros((LONG, heads_dev, 2 * block_len, HEAD_SIZE), jnp.float32),
        jnp.zeros((LONG, 2, block_len, cache_cols), jnp.float32),
    )
    parts = ctx_all_gather(jnp.concatenate([long_k[:, :, 0], long_v[:, :, 0]], axis=-1))
    piece_blocks = len(parts)
    block_ids = (ctx_rank + jnp.arange(piece_blocks, dtype=jnp.int32)) % n_ctx
    held_blocks = jnp.stack([block_ids, n_blocks - 1 - block_ids], axis=1)
    key_pos = (
        held_blocks[:, :, None] * block_len + jnp.arange(block_len, dtype=jnp.int32)
    ).reshape(-1)
    key_count = 2 * piece_blocks * block_len
    flat_kv = jnp.concatenate(
        [part.reshape(LONG, 2 * block_len, pair_width) for part in parts], axis=1
    )
    flat_k = flat_kv[..., :HEAD_SIZE]
    flat_v = flat_kv[..., HEAD_SIZE:]
    all_valid = jnp.ones((LONG, key_count), dtype=bool)
    soft_state = long_init[:3]
    soft_state = attend(soft_state, long_q, long_qpos, flat_k, flat_v, key_pos, all_valid)
    own_cols = lax.dynamic_slice_in_dim(flat_kv, first_col, cache_cols, 2).reshape(
        LONG, piece_blocks, 2, block_len, cache_cols
    )
    selector = ((held_blocks[None] // 2 == ctx_rank) & (held_blocks[None] % 2 == half_pick)).astype(
        jnp.bfloat16
    )
    cache_rows = jnp.einsum(
        "ejh,pjhbc->pebc", selector, own_cols, preferred_element_type=jnp.float32
    )
    folded = soft_state + (cache_rows,)
    long_out = (
        (folded[2] / folded[1][..., None])
        .astype(jnp.bfloat16)
        .transpose(0, 2, 1, 3)
        .reshape(long_rows, q_cols)
    )
    long_cache = folded[3].astype(jnp.bfloat16).reshape(LONG, 2 * block_len, cache_cols)
    short_count = short_lengths.shape[0]
    short_q = (
        query_matrix[long_rows:]
        .reshape(short_count, SLEN, heads_dev, HEAD_SIZE)
        .transpose(0, 2, 1, 3)
    )
    short_k = key_matrix[long_rows:].reshape(short_count, SLEN, HEAD_SIZE)
    short_v = value_matrix[long_rows:].reshape(short_count, SLEN, HEAD_SIZE)
    offsets = jnp.arange(SLEN, dtype=jnp.int32)
    short_valid = offsets[None, :] < short_lengths[:, None]
    short_init = (
        jnp.full((short_count, heads_dev, SLEN), NEG, jnp.float32),
        jnp.zeros((short_count, heads_dev, SLEN), jnp.float32),
        jnp.zeros((short_count, heads_dev, SLEN, HEAD_SIZE), jnp.float32),
    )
    short_state = attend(short_init, short_q, offsets, short_k, short_v, offsets, short_valid)
    short_out = (
        (short_state[2] / short_state[1][..., None])
        .astype(jnp.bfloat16)
        .transpose(0, 2, 1, 3)
        .reshape(short_count * SLEN, q_cols)
    )
    short_cache = lax.dynamic_slice_in_dim(
        jnp.concatenate([short_k, short_v], axis=-1), first_col, cache_cols, 2
    )
    attn = jnp.concatenate([long_out, short_out], axis=0)
    mixed = jnp.concatenate(
        [
            tp_reduce_scatter(jnp.dot(attn, part, preferred_element_type=jnp.float32).astype(jnp.bfloat16))
            for part in column_chunks(wo)
        ],
        axis=1,
    )
    residual = (states.astype(jnp.float32) + mixed).astype(jnp.bfloat16)
    pieces = [tp_all_gather(rms_scale(residual, mlp_gain), placed=False, overlap=True, forced=True)]
    gate = split_dot(pieces, w_gate)
    up_part = split_dot(pieces, w_up)
    hidden = (jax.nn.silu(gate) * up_part).astype(jnp.bfloat16)
    down = jnp.concatenate(
        [
            tp_reduce_scatter_relative(
                jnp.dot(hidden, part, preferred_element_type=jnp.float32).astype(jnp.bfloat16)
            )
            for part in column_chunks(w_down)
        ],
        axis=1,
    )
    updated = (residual.astype(jnp.float32) + down).astype(jnp.bfloat16)
    return (updated, long_cache, short_cache)


def solution(mesh):
    in_specs = (
        P(("ctx", "tp"), None),
        P("ctx"),
        P(),
        P(None, "tp"),
        P(),
        P("tp", None),
        P(),
        P(None, "tp"),
        P(None, "tp"),
        P("tp", None),
    )
    out_specs = (P(("ctx", "tp"), None), P(None, "ctx", "tp"), P("ctx", None, "tp"))
    return jax.shard_map(
        per_device, mesh=mesh, in_specs=in_specs, out_specs=out_specs, check_vma=False
    )
```

```python
import jax
import jax.numpy as jnp
from jax import lax
from jax.sharding import PartitionSpec as P

KVH = 4
HEAD_SIZE = 64
LONG = 2
LLEN = 2048
SLEN = 64


EPS = 1e-05
THETA = 10000.0
NEG = -1e30


def rms_scale(matrix, gain):
    entries = matrix.astype(jnp.float32)
    power = jnp.mean(entries * entries, axis=-1, keepdims=True)
    return (entries * lax.rsqrt(power + EPS) * gain).astype(jnp.bfloat16)


def rotate(entries, positions):
    half_width = entries.shape[-1] // 2
    frequency = THETA ** (-jnp.arange(half_width, dtype=jnp.float32) * 2.0 / entries.shape[-1])
    angles = positions.astype(jnp.float32)[:, None] * frequency[None, :]
    cosine = jnp.cos(angles)[:, None, :]
    sine_wave = jnp.sin(angles)[:, None, :]
    first_half = entries[..., :half_width]
    second_half = entries[..., half_width:]
    return jnp.concatenate(
        [
            first_half * cosine - second_half * sine_wave,
            second_half * cosine + first_half * sine_wave,
        ],
        axis=-1,
    )


def rank_positions(ctx_rank, rank_rows, block_len, long_rows, n_blocks):
    index_row = jnp.arange(rank_rows, dtype=jnp.int32)
    half_index = index_row // block_len % 2
    offset_row = index_row % block_len
    which_block = jnp.where(half_index == 0, ctx_rank, n_blocks - 1 - ctx_rank)
    long_pos = which_block * block_len + offset_row
    short_pos = (index_row - long_rows) % SLEN
    return jnp.where(index_row < long_rows, long_pos, short_pos)


TP_DIMS = ((4, 8), (4, 2), (2, 1))


def shift_perm(n, stride, d, total):
    return [(t, t + (((t // stride) % n + d) % n - (t // stride) % n) * stride) for t in range(total)]


def scatter_stage(x, axis, n, stride, total):
    me = (lax.axis_index("tp") // stride) % n
    acc = lax.dynamic_index_in_dim(x, me, axis, keepdims=False).astype(jnp.float32)
    for d in range(1, n):
        part = lax.dynamic_index_in_dim(x, (me + d) % n, axis, keepdims=False)
        got = lax.ppermute(part.astype(jnp.bfloat16), "tp", shift_perm(n, stride, d, total))
        acc = acc + got.astype(jnp.float32)
    return acc


def tp_reduce_scatter(x):
    total = lax.axis_size("tp")
    rows, width = x.shape
    sizes = [n for n, _ in TP_DIMS]
    x = x.reshape(tuple(sizes) + (rows // total, width))
    for axis in reversed(range(len(TP_DIMS))):
        n, stride = TP_DIMS[axis]
        x = scatter_stage(x, axis, n, stride, total)
    return x


def gather_stage(x, axis, n, stride, total, placed):
    parts = [x] + [
        lax.ppermute(x, "tp", shift_perm(n, stride, (n - k) % n, total)) for k in range(1, n)
    ]
    if not placed:
        return jnp.stack(parts, axis=axis)
    me = (lax.axis_index("tp") // stride) % n
    out = jnp.zeros(x.shape[:axis] + (n,) + x.shape[axis:], x.dtype)
    for k, part in enumerate(parts):
        out = lax.dynamic_update_index_in_dim(out, part, (me + k) % n, axis)
    return out


def plane_gather(x, placed, forced):
    total = lax.axis_size("tp")
    (nz, sz), (ny, sy) = TP_DIMS[:2]

    def fetch(value, n, stride, k):
        return lax.ppermute(value, "tp", shift_perm(n, stride, (n - k) % n, total))

    far = jnp.stack([fetch(x, nz, sz, k) for k in range(1, nz)])
    near = [fetch(x, ny, sy, k) for k in range(1, ny)]
    if forced:
        far, near = lax.optimization_barrier((far, near))
    rest = [fetch(far, ny, sy, k) for k in range(1, ny)]
    columns = [jnp.concatenate([x[None], far])] + [
        jnp.concatenate([own[None], other]) for own, other in zip(near, rest)
    ]
    if not placed:
        return jnp.stack(columns, axis=1)
    tp_index = lax.axis_index("tp")
    me_z, me_y = (tp_index // sz) % nz, (tp_index // sy) % ny
    out = jnp.zeros((nz, ny) + x.shape, x.dtype)
    for k, column in enumerate(columns):
        slot = jnp.zeros((nz,) + x.shape, x.dtype)
        for j in range(nz):
            slot = lax.dynamic_update_index_in_dim(slot, column[j], (me_z + j) % nz, 0)
        out = lax.dynamic_update_index_in_dim(out, slot, (me_y + k) % ny, 1)
    return out


def tp_all_gather(x, placed=True, overlap=False, forced=False):
    total = lax.axis_size("tp")
    rows, width = x.shape
    if overlap:
        x = plane_gather(x, placed, forced)
    for axis, (n, stride) in enumerate(TP_DIMS):
        if axis >= 2 or not overlap:
            x = gather_stage(x, axis, n, stride, total, placed)
    return x.reshape(rows * total, width)


def relative_scatter_stage(x, axis, n, stride, total):
    acc = lax.index_in_dim(x, 0, axis, keepdims=False).astype(jnp.float32)
    for d in range(1, n):
        part = lax.index_in_dim(x, d, axis, keepdims=False)
        got = lax.ppermute(part.astype(jnp.bfloat16), "tp", shift_perm(n, stride, d, total))
        acc = acc + got.astype(jnp.float32)
    return acc


def tp_reduce_scatter_relative(x):
    total = lax.axis_size("tp")
    rows, width = x.shape
    sizes = [n for n, _ in TP_DIMS]
    (nz, sz), (ny, sy), (nc, sc) = TP_DIMS
    x = x.reshape(tuple(sizes) + (rows // total, width))
    x = relative_scatter_stage(x, 2, nc, sc, total)

    def send(value, n, stride, d):
        got = lax.ppermute(value.astype(jnp.bfloat16), "tp", shift_perm(n, stride, d, total))
        return got.astype(jnp.float32)

    rest = x[1:, 0]
    for d in range(1, ny):
        rest = rest + send(x[1:, d], ny, sy, d)
    own = x[0, 0]
    for d in range(1, ny):
        own = own + send(x[0, d], ny, sy, d)
    for d in range(1, nz):
        own = own + send(rest[d - 1], nz, sz, d)
    return own


def ctx_all_gather(x):
    n = lax.axis_size("ctx")
    parts = [x] + [
        lax.ppermute(x, "ctx", [(j, (j - k) % n) for j in range(n)]) for k in range(1, n)
    ]
    return parts


CHUNKS = 2


def column_chunks(matrix, axis=1, count=CHUNKS):
    width = matrix.shape[axis] // count
    return [lax.slice_in_dim(matrix, i * width, (i + 1) * width, axis=axis) for i in range(count)]


def split_dot(pieces, weight):
    parts = column_chunks(weight, axis=0, count=len(pieces))
    total = jnp.dot(pieces[0], parts[0], preferred_element_type=jnp.float32)
    for piece, part in zip(pieces[1:], parts[1:]):
        total = total + jnp.dot(piece, part, preferred_element_type=jnp.float32)
    return total


def project(pieces, positions, wq, wkv_head, heads_dev):
    row_count = pieces[0].shape[0]
    query_matrix = split_dot(pieces, wq).reshape(row_count, heads_dev, HEAD_SIZE)
    query_matrix = rotate(query_matrix, positions).astype(jnp.bfloat16)
    pairs = split_dot(pieces, wkv_head)
    key_matrix = rotate(pairs[:, None, :HEAD_SIZE], positions).astype(jnp.bfloat16)[:, 0]
    value_matrix = pairs[:, HEAD_SIZE:].astype(jnp.bfloat16)
    return jnp.concatenate(
        [query_matrix.reshape(row_count, heads_dev * HEAD_SIZE), key_matrix, value_matrix], axis=1
    )


def attend(soft_state, query_matrix, query_pos, key_matrix, value_matrix, key_pos, valid_keys):
    best_score, weight_sum, weighted = soft_state
    logit_scores = jnp.einsum(
        "rzsm,rvm->rzsv", query_matrix, key_matrix, preferred_element_type=jnp.float32
    ) * HEAD_SIZE ** (-0.5)
    allowed = (key_pos[None, :] <= query_pos[:, None])[None, None] & valid_keys[:, None, None, :]
    logit_scores = jnp.where(allowed, logit_scores, NEG)
    new_best = jnp.maximum(best_score, jnp.max(logit_scores, axis=-1))
    weights = jnp.where(allowed, jnp.exp(logit_scores - new_best[..., None]), 0.0)
    weight_sum = jnp.sum(weights, axis=-1)
    weighted = jnp.einsum(
        "awlp,ape->awle",
        weights.astype(jnp.bfloat16),
        value_matrix,
        preferred_element_type=jnp.float32,
    )
    return (new_best, weight_sum, weighted)


def per_device(states, short_lengths, attn_gain, wq, wkv, wo, mlp_gain, w_gate, w_up, w_down):
    n_ctx = lax.axis_size("ctx")
    n_tp = lax.axis_size("tp")
    ctx_rank = lax.axis_index("ctx")
    tp_index = lax.axis_index("tp")
    tok_rows = states.shape[0]
    rank_rows = tok_rows * n_tp
    n_blocks = 2 * n_ctx
    block_len = LLEN // n_blocks
    long_rows = LONG * 2 * block_len
    heads_dev = wq.shape[1] // HEAD_SIZE
    q_cols = heads_dev * HEAD_SIZE
    pair_width = 2 * HEAD_SIZE
    cache_cols = KVH * pair_width // n_tp
    kv_group = tp_index * KVH // n_tp
    wkv_head = lax.dynamic_slice_in_dim(wkv, kv_group * pair_width, pair_width, 1)
    first_col = tp_index * cache_cols - kv_group * pair_width
    positions = rank_positions(ctx_rank, rank_rows, block_len, long_rows, n_blocks)
    packed = project(
        [tp_all_gather(rms_scale(states, attn_gain), overlap=True)],
        positions,
        wq,
        wkv_head,
        heads_dev,
    )
    query_matrix = packed[:, :q_cols].reshape(rank_rows, heads_dev, HEAD_SIZE)
    key_matrix = packed[:, q_cols : q_cols + HEAD_SIZE]
    value_matrix = packed[:, q_cols + HEAD_SIZE :]
    long_q = (
        query_matrix[:long_rows]
        .reshape(LONG, 2 * block_len, heads_dev, HEAD_SIZE)
        .transpose(0, 2, 1, 3)
    )
    long_k = key_matrix[:long_rows].reshape(LONG, 2, 1, block_len, HEAD_SIZE)
    long_v = value_matrix[:long_rows].reshape(LONG, 2, 1, block_len, HEAD_SIZE)
    long_qpos = positions[: 2 * block_len]
    half_pick = jnp.arange(2, dtype=jnp.int32)[:, None, None]
    long_init = (
        jnp.full((LONG, heads_dev, 2 * block_len), NEG, jnp.float32),
        jnp.zeros((LONG, heads_dev, 2 * block_len), jnp.float32),
        jnp.zeros((LONG, heads_dev, 2 * block_len, HEAD_SIZE), jnp.float32),
        jnp.zeros((LONG, 2, block_len, cache_cols), jnp.float32),
    )
    parts = ctx_all_gather(jnp.concatenate([long_k[:, :, 0], long_v[:, :, 0]], axis=-1))
    piece_blocks = len(parts)
    block_ids = (ctx_rank + jnp.arange(piece_blocks, dtype=jnp.int32)) % n_ctx
    held_blocks = jnp.stack([block_ids, n_blocks - 1 - block_ids], axis=1)
    key_pos = (
        held_blocks[:, :, None] * block_len + jnp.arange(block_len, dtype=jnp.int32)
    ).reshape(-1)
    key_count = 2 * piece_blocks * block_len
    flat_kv = jnp.concatenate(
        [part.reshape(LONG, 2 * block_len, pair_width) for part in parts], axis=1
    )
    flat_k = flat_kv[..., :HEAD_SIZE]
    flat_v = flat_kv[..., HEAD_SIZE:]
    all_valid = jnp.ones((LONG, key_count), dtype=bool)
    soft_state = long_init[:3]
    soft_state = attend(soft_state, long_q, long_qpos, flat_k, flat_v, key_pos, all_valid)
    own_cols = lax.dynamic_slice_in_dim(flat_kv, first_col, cache_cols, 2).reshape(
        LONG, piece_blocks, 2, block_len, cache_cols
    )
    selector = ((held_blocks[None] // 2 == ctx_rank) & (held_blocks[None] % 2 == half_pick)).astype(
        jnp.bfloat16
    )
    cache_rows = jnp.einsum(
        "ejh,pjhbc->pebc", selector, own_cols, preferred_element_type=jnp.float32
    )
    folded = soft_state + (cache_rows,)
    long_out = (
        (folded[2] / folded[1][..., None])
        .astype(jnp.bfloat16)
        .transpose(0, 2, 1, 3)
        .reshape(long_rows, q_cols)
    )
    long_cache = folded[3].astype(jnp.bfloat16).reshape(LONG, 2 * block_len, cache_cols)
    short_count = short_lengths.shape[0]
    short_q = (
        query_matrix[long_rows:]
        .reshape(short_count, SLEN, heads_dev, HEAD_SIZE)
        .transpose(0, 2, 1, 3)
    )
    short_k = key_matrix[long_rows:].reshape(short_count, SLEN, HEAD_SIZE)
    short_v = value_matrix[long_rows:].reshape(short_count, SLEN, HEAD_SIZE)
    offsets = jnp.arange(SLEN, dtype=jnp.int32)
    short_valid = offsets[None, :] < short_lengths[:, None]
    short_init = (
        jnp.full((short_count, heads_dev, SLEN), NEG, jnp.float32),
        jnp.zeros((short_count, heads_dev, SLEN), jnp.float32),
        jnp.zeros((short_count, heads_dev, SLEN, HEAD_SIZE), jnp.float32),
    )
    short_state = attend(short_init, short_q, offsets, short_k, short_v, offsets, short_valid)
    short_out = (
        (short_state[2] / short_state[1][..., None])
        .astype(jnp.bfloat16)
        .transpose(0, 2, 1, 3)
        .reshape(short_count * SLEN, q_cols)
    )
    short_cache = lax.dynamic_slice_in_dim(
        jnp.concatenate([short_k, short_v], axis=-1), first_col, cache_cols, 2
    )
    attn = jnp.concatenate([long_out, short_out], axis=0)
    mixed = jnp.concatenate(
        [
            tp_reduce_scatter(jnp.dot(attn, part, preferred_element_type=jnp.float32).astype(jnp.bfloat16))
            for part in column_chunks(wo)
        ],
        axis=1,
    )
    residual = (states.astype(jnp.float32) + mixed).astype(jnp.bfloat16)
    pieces = [tp_all_gather(rms_scale(residual, mlp_gain), placed=False, overlap=True, forced=True)]
    gate = split_dot(pieces, w_gate)
    up_part = split_dot(pieces, w_up)
    hidden = (jax.nn.silu(gate) * up_part).astype(jnp.bfloat16)
    down = jnp.concatenate(
        [
            tp_reduce_scatter_relative(
                jnp.dot(hidden, part, preferred_element_type=jnp.float32).astype(jnp.bfloat16)
            )
            for part in column_chunks(w_down)
        ],
        axis=1,
    )
    updated = (residual.astype(jnp.float32) + down).astype(jnp.bfloat16)
    return (updated, long_cache, short_cache)


def solution(mesh):
    in_specs = (
        P(("ctx", "tp"), None),
        P("ctx"),
        P(),
        P(None, "tp"),
        P(),
        P("tp", None),
        P(),
        P(None, "tp"),
        P(None, "tp"),
        P("tp", None),
    )
    out_specs = (P(("ctx", "tp"), None), P(None, "ctx", "tp"), P("ctx", None, "tp"))
    return jax.shard_map(
        per_device, mesh=mesh, in_specs=in_specs, out_specs=out_specs, check_vma=False
    )
```

```python
import jax
import jax.numpy as jnp
from jax import lax
from jax.sharding import PartitionSpec as P

KVH = 4
HEAD_SIZE = 64
LONG = 2
LLEN = 2048
SLEN = 64


EPS = 1e-05
THETA = 10000.0
NEG = -1e30


def rms_scale(matrix, gain):
    entries = matrix.astype(jnp.float32)
    power = jnp.mean(entries * entries, axis=-1, keepdims=True)
    return (entries * lax.rsqrt(power + EPS) * gain).astype(jnp.bfloat16)


def rotate(entries, positions):
    half_width = entries.shape[-1] // 2
    frequency = THETA ** (-jnp.arange(half_width, dtype=jnp.float32) * 2.0 / entries.shape[-1])
    angles = positions.astype(jnp.float32)[:, None] * frequency[None, :]
    cosine = jnp.cos(angles)[:, None, :]
    sine_wave = jnp.sin(angles)[:, None, :]
    first_half = entries[..., :half_width]
    second_half = entries[..., half_width:]
    return jnp.concatenate(
        [
            first_half * cosine - second_half * sine_wave,
            second_half * cosine + first_half * sine_wave,
        ],
        axis=-1,
    )


def rank_positions(ctx_rank, rank_rows, block_len, long_rows, n_blocks):
    index_row = jnp.arange(rank_rows, dtype=jnp.int32)
    half_index = index_row // block_len % 2
    offset_row = index_row % block_len
    which_block = jnp.where(half_index == 0, ctx_rank, n_blocks - 1 - ctx_rank)
    long_pos = which_block * block_len + offset_row
    short_pos = (index_row - long_rows) % SLEN
    return jnp.where(index_row < long_rows, long_pos, short_pos)


TP_DIMS = ((4, 8), (4, 2), (2, 1))


def shift_perm(n, stride, d, total):
    return [(t, t + (((t // stride) % n + d) % n - (t // stride) % n) * stride) for t in range(total)]


def scatter_stage(x, axis, n, stride, total):
    me = (lax.axis_index("tp") // stride) % n
    acc = lax.dynamic_index_in_dim(x, me, axis, keepdims=False).astype(jnp.float32)
    for d in range(1, n):
        part = lax.dynamic_index_in_dim(x, (me + d) % n, axis, keepdims=False)
        got = lax.ppermute(part.astype(jnp.bfloat16), "tp", shift_perm(n, stride, d, total))
        acc = acc + got.astype(jnp.float32)
    return acc


def tp_reduce_scatter(x):
    total = lax.axis_size("tp")
    rows, width = x.shape
    sizes = [n for n, _ in TP_DIMS]
    x = x.reshape(tuple(sizes) + (rows // total, width))
    for axis in reversed(range(len(TP_DIMS))):
        n, stride = TP_DIMS[axis]
        x = scatter_stage(x, axis, n, stride, total)
    return x


def gather_stage(x, axis, n, stride, total, placed):
    parts = [x] + [
        lax.ppermute(x, "tp", shift_perm(n, stride, (n - k) % n, total)) for k in range(1, n)
    ]
    if not placed:
        return jnp.stack(parts, axis=axis)
    me = (lax.axis_index("tp") // stride) % n
    out = jnp.zeros(x.shape[:axis] + (n,) + x.shape[axis:], x.dtype)
    for k, part in enumerate(parts):
        out = lax.dynamic_update_index_in_dim(out, part, (me + k) % n, axis)
    return out


def plane_gather(x, placed, forced):
    total = lax.axis_size("tp")
    (nz, sz), (ny, sy) = TP_DIMS[:2]

    def fetch(value, n, stride, k):
        return lax.ppermute(value, "tp", shift_perm(n, stride, (n - k) % n, total))

    far = jnp.stack([fetch(x, nz, sz, k) for k in range(1, nz)])
    near = [fetch(x, ny, sy, k) for k in range(1, ny)]
    if forced:
        far, near = lax.optimization_barrier((far, near))
    rest = [fetch(far, ny, sy, k) for k in range(1, ny)]
    columns = [jnp.concatenate([x[None], far])] + [
        jnp.concatenate([own[None], other]) for own, other in zip(near, rest)
    ]
    if not placed:
        return jnp.stack(columns, axis=1)
    tp_index = lax.axis_index("tp")
    me_z, me_y = (tp_index // sz) % nz, (tp_index // sy) % ny
    out = jnp.zeros((nz, ny) + x.shape, x.dtype)
    for k, column in enumerate(columns):
        slot = jnp.zeros((nz,) + x.shape, x.dtype)
        for j in range(nz):
            slot = lax.dynamic_update_index_in_dim(slot, column[j], (me_z + j) % nz, 0)
        out = lax.dynamic_update_index_in_dim(out, slot, (me_y + k) % ny, 1)
    return out


def tp_all_gather(x, placed=True, overlap=False, forced=False):
    total = lax.axis_size("tp")
    rows, width = x.shape
    if overlap:
        x = plane_gather(x, placed, forced)
    for axis, (n, stride) in enumerate(TP_DIMS):
        if axis >= 2 or not overlap:
            x = gather_stage(x, axis, n, stride, total, placed)
    return x.reshape(rows * total, width)


def relative_scatter_stage(x, axis, n, stride, total):
    acc = lax.index_in_dim(x, 0, axis, keepdims=False).astype(jnp.float32)
    for d in range(1, n):
        part = lax.index_in_dim(x, d, axis, keepdims=False)
        got = lax.ppermute(part.astype(jnp.bfloat16), "tp", shift_perm(n, stride, d, total))
        acc = acc + got.astype(jnp.float32)
    return acc


def tp_reduce_scatter_relative(x):
    total = lax.axis_size("tp")
    rows, width = x.shape
    sizes = [n for n, _ in TP_DIMS]
    x = x.reshape(tuple(sizes) + (rows // total, width))
    for axis in reversed(range(len(TP_DIMS))):
        n, stride = TP_DIMS[axis]
        x = relative_scatter_stage(x, axis, n, stride, total)
    return x


def ctx_all_gather(x):
    n = lax.axis_size("ctx")
    parts = [x] + [
        lax.ppermute(x, "ctx", [(j, (j - k) % n) for j in range(n)]) for k in range(1, n)
    ]
    return parts


CHUNKS = 2


def column_chunks(matrix, axis=1, count=CHUNKS):
    width = matrix.shape[axis] // count
    return [lax.slice_in_dim(matrix, i * width, (i + 1) * width, axis=axis) for i in range(count)]


def split_dot(pieces, weight):
    parts = column_chunks(weight, axis=0, count=len(pieces))
    total = jnp.dot(pieces[0], parts[0], preferred_element_type=jnp.float32)
    for piece, part in zip(pieces[1:], parts[1:]):
        total = total + jnp.dot(piece, part, preferred_element_type=jnp.float32)
    return total


def project(pieces, positions, wq, wkv_head, heads_dev):
    row_count = pieces[0].shape[0]
    query_matrix = split_dot(pieces, wq).reshape(row_count, heads_dev, HEAD_SIZE)
    query_matrix = rotate(query_matrix, positions).astype(jnp.bfloat16)
    pairs = split_dot(pieces, wkv_head)
    key_matrix = rotate(pairs[:, None, :HEAD_SIZE], positions).astype(jnp.bfloat16)[:, 0]
    value_matrix = pairs[:, HEAD_SIZE:].astype(jnp.bfloat16)
    return jnp.concatenate(
        [query_matrix.reshape(row_count, heads_dev * HEAD_SIZE), key_matrix, value_matrix], axis=1
    )


def attend(soft_state, query_matrix, query_pos, key_matrix, value_matrix, key_pos, valid_keys):
    best_score, weight_sum, weighted = soft_state
    logit_scores = jnp.einsum(
        "rzsm,rvm->rzsv", query_matrix, key_matrix, preferred_element_type=jnp.float32
    ) * HEAD_SIZE ** (-0.5)
    allowed = (key_pos[None, :] <= query_pos[:, None])[None, None] & valid_keys[:, None, None, :]
    logit_scores = jnp.where(allowed, logit_scores, NEG)
    new_best = jnp.maximum(best_score, jnp.max(logit_scores, axis=-1))
    weights = jnp.where(allowed, jnp.exp(logit_scores - new_best[..., None]), 0.0)
    weight_sum = jnp.sum(weights, axis=-1)
    weighted = jnp.einsum(
        "awlp,ape->awle",
        weights.astype(jnp.bfloat16),
        value_matrix,
        preferred_element_type=jnp.float32,
    )
    return (new_best, weight_sum, weighted)


def per_device(states, short_lengths, attn_gain, wq, wkv, wo, mlp_gain, w_gate, w_up, w_down):
    n_ctx = lax.axis_size("ctx")
    n_tp = lax.axis_size("tp")
    ctx_rank = lax.axis_index("ctx")
    tp_index = lax.axis_index("tp")
    tok_rows = states.shape[0]
    rank_rows = tok_rows * n_tp
    n_blocks = 2 * n_ctx
    block_len = LLEN // n_blocks
    long_rows = LONG * 2 * block_len
    heads_dev = wq.shape[1] // HEAD_SIZE
    q_cols = heads_dev * HEAD_SIZE
    pair_width = 2 * HEAD_SIZE
    cache_cols = KVH * pair_width // n_tp
    kv_group = tp_index * KVH // n_tp
    wkv_head = lax.dynamic_slice_in_dim(wkv, kv_group * pair_width, pair_width, 1)
    first_col = tp_index * cache_cols - kv_group * pair_width
    positions = rank_positions(ctx_rank, rank_rows, block_len, long_rows, n_blocks)
    packed = project(
        [tp_all_gather(rms_scale(states, attn_gain), overlap=True)],
        positions,
        wq,
        wkv_head,
        heads_dev,
    )
    query_matrix = packed[:, :q_cols].reshape(rank_rows, heads_dev, HEAD_SIZE)
    key_matrix = packed[:, q_cols : q_cols + HEAD_SIZE]
    value_matrix = packed[:, q_cols + HEAD_SIZE :]
    long_q = (
        query_matrix[:long_rows]
        .reshape(LONG, 2 * block_len, heads_dev, HEAD_SIZE)
        .transpose(0, 2, 1, 3)
    )
    long_k = key_matrix[:long_rows].reshape(LONG, 2, 1, block_len, HEAD_SIZE)
    long_v = value_matrix[:long_rows].reshape(LONG, 2, 1, block_len, HEAD_SIZE)
    long_qpos = positions[: 2 * block_len]
    half_pick = jnp.arange(2, dtype=jnp.int32)[:, None, None]
    long_init = (
        jnp.full((LONG, heads_dev, 2 * block_len), NEG, jnp.float32),
        jnp.zeros((LONG, heads_dev, 2 * block_len), jnp.float32),
        jnp.zeros((LONG, heads_dev, 2 * block_len, HEAD_SIZE), jnp.float32),
        jnp.zeros((LONG, 2, block_len, cache_cols), jnp.float32),
    )
    parts = ctx_all_gather(jnp.concatenate([long_k[:, :, 0], long_v[:, :, 0]], axis=-1))
    piece_blocks = len(parts)
    block_ids = (ctx_rank + jnp.arange(piece_blocks, dtype=jnp.int32)) % n_ctx
    held_blocks = jnp.stack([block_ids, n_blocks - 1 - block_ids], axis=1)
    key_pos = (
        held_blocks[:, :, None] * block_len + jnp.arange(block_len, dtype=jnp.int32)
    ).reshape(-1)
    key_count = 2 * piece_blocks * block_len
    flat_kv = jnp.concatenate(
        [part.reshape(LONG, 2 * block_len, pair_width) for part in parts], axis=1
    )
    flat_k = flat_kv[..., :HEAD_SIZE]
    flat_v = flat_kv[..., HEAD_SIZE:]
    all_valid = jnp.ones((LONG, key_count), dtype=bool)
    soft_state = long_init[:3]
    soft_state = attend(soft_state, long_q, long_qpos, flat_k, flat_v, key_pos, all_valid)
    own_cols = lax.dynamic_slice_in_dim(flat_kv, first_col, cache_cols, 2).reshape(
        LONG, piece_blocks, 2, block_len, cache_cols
    )
    selector = ((held_blocks[None] // 2 == ctx_rank) & (held_blocks[None] % 2 == half_pick)).astype(
        jnp.bfloat16
    )
    cache_rows = jnp.einsum(
        "ejh,pjhbc->pebc", selector, own_cols, preferred_element_type=jnp.float32
    )
    folded = soft_state + (cache_rows,)
    long_out = (
        (folded[2] / folded[1][..., None])
        .astype(jnp.bfloat16)
        .transpose(0, 2, 1, 3)
        .reshape(long_rows, q_cols)
    )
    long_cache = folded[3].astype(jnp.bfloat16).reshape(LONG, 2 * block_len, cache_cols)
    short_count = short_lengths.shape[0]
    short_q = (
        query_matrix[long_rows:]
        .reshape(short_count, SLEN, heads_dev, HEAD_SIZE)
        .transpose(0, 2, 1, 3)
    )
    short_k = key_matrix[long_rows:].reshape(short_count, SLEN, HEAD_SIZE)
    short_v = value_matrix[long_rows:].reshape(short_count, SLEN, HEAD_SIZE)
    offsets = jnp.arange(SLEN, dtype=jnp.int32)
    short_valid = offsets[None, :] < short_lengths[:, None]
    short_init = (
        jnp.full((short_count, heads_dev, SLEN), NEG, jnp.float32),
        jnp.zeros((short_count, heads_dev, SLEN), jnp.float32),
        jnp.zeros((short_count, heads_dev, SLEN, HEAD_SIZE), jnp.float32),
    )
    short_state = attend(short_init, short_q, offsets, short_k, short_v, offsets, short_valid)
    short_out = (
        (short_state[2] / short_state[1][..., None])
        .astype(jnp.bfloat16)
        .transpose(0, 2, 1, 3)
        .reshape(short_count * SLEN, q_cols)
    )
    short_cache = lax.dynamic_slice_in_dim(
        jnp.concatenate([short_k, short_v], axis=-1), first_col, cache_cols, 2
    )
    attn = jnp.concatenate([long_out, short_out], axis=0)
    mixed = jnp.concatenate(
        [
            tp_reduce_scatter(jnp.dot(attn, part, preferred_element_type=jnp.float32).astype(jnp.bfloat16))
            for part in column_chunks(wo)
        ],
        axis=1,
    )
    residual = (states.astype(jnp.float32) + mixed).astype(jnp.bfloat16)
    total = lax.axis_size("tp")
    width = residual.shape[1]
    mine = plane_gather(rms_scale(residual, mlp_gain), False, True)
    partner = lax.ppermute(mine, "tp", shift_perm(2, 1, 1, total))

    def feed_forward(rows):
        rows = rows.reshape(-1, width)
        gate = jnp.dot(rows, w_gate, preferred_element_type=jnp.float32)
        up_part = jnp.dot(rows, w_up, preferred_element_type=jnp.float32)
        hidden = (jax.nn.silu(gate) * up_part).astype(jnp.bfloat16)
        return [
            jnp.dot(hidden, part, preferred_element_type=jnp.float32).astype(jnp.bfloat16)
            for part in column_chunks(w_down)
        ]

    def scatter_tail(kept, sent):
        acc = kept.astype(jnp.float32) + lax.ppermute(sent, "tp", shift_perm(2, 1, 1, total)).astype(
            jnp.float32
        )
        acc = acc.reshape(mine.shape[:3] + (kept.shape[1],))
        for axis in (1, 0):
            n, stride = TP_DIMS[axis]
            acc = relative_scatter_stage(acc, axis, n, stride, total)
        return acc

    down = jnp.concatenate(
        [scatter_tail(a, b) for a, b in zip(feed_forward(mine), feed_forward(partner))], axis=1
    )
    updated = (residual.astype(jnp.float32) + down).astype(jnp.bfloat16)
    return (updated, long_cache, short_cache)


def solution(mesh):
    in_specs = (
        P(("ctx", "tp"), None),
        P("ctx"),
        P(),
        P(None, "tp"),
        P(),
        P("tp", None),
        P(),
        P(None, "tp"),
        P(None, "tp"),
        P("tp", None),
    )
    out_specs = (P(("ctx", "tp"), None), P(None, "ctx", "tp"), P("ctx", None, "tp"))
    return jax.shard_map(
        per_device, mesh=mesh, in_specs=in_specs, out_specs=out_specs, check_vma=False
    )
```
